32 devices in a mesh: dp: 8 (over y, x, core), fsdp: 4 (over z).
Axes of the slice: x: 2, y: 2, z: 4, core: 2. Of those that a mesh axis runs over, the one named last changes fastest.
Arguments:
- tokens: bfloat16 [18432, 768], P(('dp', 'fsdp')), may hold values from -6 to 6
- image_lengths: int32 [32, 9], P(('dp', 'fsdp')), may hold values from 0 to 576, as said below
- w_qkv: bfloat16 [768, 2304], P('fsdp'), may hold values from -0.21875 to 0.21875
- w_out: bfloat16 [768, 768], P('fsdp'), may hold values from -0.875 to 0.875
- w_up: bfloat16 [768, 3072], P('fsdp'), may hold values from -0.21875 to 0.21875
- w_down: bfloat16 [3072, 768], P('fsdp'), may hold values from -0.109375 to 0.109375
- ln_gain: bfloat16 [2, 768], P(None, 'fsdp'), may hold values from 0.25 to 1.75
- ln_bias: bfloat16 [2, 768], P(None, 'fsdp'), may hold values from -3 to 3
- qk_gain: bfloat16 [2, 768], P(None, 'fsdp'), may hold values from 0.25 to 1.75
- cotangent: bfloat16 [18432, 768], P(('dp', 'fsdp')), may hold values from -6 to 6
Outputs:
- layer_out: bfloat16 [18432, 768], P(('dp', 'fsdp'))
- grad_tokens: bfloat16 [18432, 768], P(('dp', 'fsdp'))
- grad_w_qkv: float32 [768, 2304], P('fsdp')
- grad_w_out: float32 [768, 768], P('fsdp')
- grad_w_up: float32 [768, 3072], P('fsdp')
- grad_w_down: float32 [3072, 768], P('fsdp')
- grad_ln_gain: float32 [2, 768], P(None, 'fsdp')
- grad_ln_bias: float32 [2, 768], P(None, 'fsdp')
- grad_qk_gain: float32 [2, 768], P(None, 'fsdp')
The draws below stay inside these ranges and needn't reach their ends.
Inputs may be any that keep to these rules, and one draw needn't show every extreme that they name: Each row of image_lengths is either 1 large images of 576 patches, or between 1 and 9 small images of 64 patches; used slots come first, zeros after. Exactly half of the rows hold large images. No image crosses a multiple of 576 rows, and padding lies after the last image.
All inputs are finite; a program needn't handle non-finite values.
Results may differ from the reference program's by a relative error of at most 0.02.
Values may be sent and summed in bfloat16 or wider, within the bound.
No kernel may reach another device: no remote copies, remote signals or barrier semaphores. Data moves between devices by JAX's collectives and lax.ppermute only.
A program may use at most 192 MiB of HBM per device.

```python
import jax
import jax.numpy as jnp
from jax import lax

D = 768
HEADS = 12
HEAD_DIM = 64
FF = 3072
PATCH_BIG = 576
PATCH_SMALL = 64
BLOCKS_DEV = 1
ROWS = 576
SLOTS = 9
HOLDERS = 32
TOKENS = 18432


def draw_image_lengths(key, part):
    kind_key = jax.random.fold_in(key, 11)
    count_key = jax.random.fold_in(key, 23)
    order = jax.random.permutation(kind_key, HOLDERS)
    large = order < HOLDERS // 2
    slot = jnp.arange(SLOTS, dtype=jnp.int32)
    count = jax.random.randint(count_key, (HOLDERS,), SLOTS - PATCH_BIG // PATCH_SMALL + 1, SLOTS + 1)
    small_row = jnp.where(slot[None, :] < count[:, None], PATCH_SMALL, 0)
    large_row = jnp.where(slot[None, :] < BLOCKS_DEV, PATCH_BIG, 0)
    large_full = jnp.broadcast_to(large_row, (HOLDERS, SLOTS))
    return jnp.where(large[:, None], large_full, small_row).astype(jnp.int32)


def block_levels(rng, extent, cuts, least, top_value):
    level, own = 1.0, jax.random.fold_in(rng, 6)
    for dim, shards_of in cuts:
        heights = jnp.exp(jax.random.uniform(jax.random.fold_in(own, dim), (shards_of,), jnp.float32, least / len(cuts), top_value / len(cuts)))
        level = level * jnp.repeat(heights, extent[dim] // shards_of).reshape([-1 if axis == dim else 1 for axis in range(len(extent))])
    return level


def bell_draw(key, extent, deviation, reach, cuts=(), held_as=jnp.bfloat16):
    result = deviation * jax.random.normal(key, extent, jnp.float32)
    if cuts:
        result = result * block_levels(key, extent, cuts, -0.22, 0.18)
    return jnp.clip(result, -reach, reach).astype(held_as)


def setup_inputs(seed: int = 0) -> dict:
    splits = jax.random.split(jax.random.key(seed), 11)
    return {
        "tokens": bell_draw(splits[0], (TOKENS, D), 1.0, 6.0, ((0, 32),)),
        "image_lengths": draw_image_lengths(jax.random.fold_in(splits[10], 71), 0),
        "w_qkv": bell_draw(splits[2], (D, 3 * D), D ** -0.5, 0.21875, ((0, 4),)),
        "w_out": bell_draw(splits[3], (D, D), (D // 16) ** -0.5, 0.875, ((0, 4),)),
        "w_up": bell_draw(splits[4], (D, FF), D ** -0.5, 0.21875, ((0, 4),)),
        "w_down": bell_draw(splits[5], (FF, D), FF ** -0.5, 0.109375, ((0, 4),)),
        "ln_gain": jnp.clip(1.0 + 0.15 * jax.random.normal(splits[6], (2, D), jnp.float32), 0.25, 1.75).astype(jnp.bfloat16),
        "ln_bias": bell_draw(splits[7], (2, D), 0.5, 3.0, ((1, 4),)),
        "qk_gain": jnp.clip(1.0 + 0.15 * jax.random.normal(splits[8], (2, D), jnp.float32), 0.25, 1.75).astype(jnp.bfloat16),
        "cotangent": bell_draw(splits[9], (TOKENS, D), 1.0, 6.0, ((0, 32),)),
    }


epsilon = 1e-06

@jax.custom_vjp
def low(v):
    return lax.optimization_barrier(v.astype(jnp.bfloat16)).astype(jnp.float32)

@jax.custom_vjp
def low_back(v):
    return v

def low_keep(v):
    return (low(v), None)

def low_pass(kept, grad):
    return (grad,)

def back_keep(v):
    return (v, None)

def back_low(kept, grad):
    return (low(grad),)
low.defvjp(low_keep, low_pass)
low_back.defvjp(back_keep, back_low)

def layer_norm(v, gain_row, bias_row):
    centre = v - lax.optimization_barrier(jnp.mean(v, axis=-1, keepdims=True))
    spread = lax.optimization_barrier(jnp.mean(centre * centre, axis=-1, keepdims=True))
    return centre * lax.rsqrt(spread + epsilon) * gain_row + bias_row

def head_norm(v, gain_row):
    centre = v - lax.optimization_barrier(jnp.mean(v, axis=-1, keepdims=True))
    spread = lax.optimization_barrier(jnp.mean(centre * centre, axis=-1, keepdims=True))
    return centre * lax.rsqrt(spread + epsilon) * gain_row

def forward_rows(x, w_qkv, w_out, w_up, w_down, ln_gain, ln_bias, qk_gain, segment, valid_rows):
    highest = lax.Precision.HIGHEST
    length = x.shape[0]
    scaling = HEAD_DIM ** (-0.5)
    normed = low(layer_norm(x, ln_gain[0], ln_bias[0]))
    project = low_back(jnp.dot(normed, w_qkv, precision=highest))
    queries = project[:, :D].reshape(length, HEADS, HEAD_DIM)
    keys_raw = project[:, D:2 * D].reshape(length, HEADS, HEAD_DIM)
    values_raw = project[:, 2 * D:].reshape(length, HEADS, HEAD_DIM)
    q_hat = low(head_norm(queries, qk_gain[0].reshape(HEADS, HEAD_DIM)))
    k_hat = low(head_norm(keys_raw, qk_gain[1].reshape(HEADS, HEAD_DIM)))
    v_hat = low(values_raw)
    q_blocks = q_hat.reshape(length // PATCH_BIG, PATCH_BIG, HEADS, HEAD_DIM)
    s_blocks = segment.reshape(length // PATCH_BIG, PATCH_BIG)

    def attend(members):
        q_block, s_block = members
        scores = low_back(jnp.einsum('qhd,khd->hqk', q_block, k_hat, precision=highest) * scaling)
        scores = jnp.where((s_block[:, None] == segment[None, :])[None], scores, -1e+30)
        probability = low_back(low(jax.nn.softmax(scores, axis=-1)))
        return jnp.einsum('hqk,khd->qhd', probability, v_hat, precision=highest)
    mixed_heads = lax.map(jax.checkpoint(attend), (q_blocks, s_blocks))
    mixed_heads = low_back(low(mixed_heads.reshape(length, D)))
    branch = low_back(jnp.dot(mixed_heads, w_out, precision=highest))
    residual = x + branch
    second = low(layer_norm(residual, ln_gain[1], ln_bias[1]))
    up_pre = low_back(jnp.dot(second, w_up, precision=highest))
    active = low(jax.nn.gelu(up_pre, approximate=False))
    down_out = low_back(jnp.dot(active, w_down, precision=highest))
    return valid_rows * (residual + down_out)

def reference(tokens, image_lengths, w_qkv, w_out, w_up, w_down, ln_gain, ln_bias, qk_gain, cotangent):
    weights_all = (w_qkv.astype(jnp.float32), w_out.astype(jnp.float32), w_up.astype(jnp.float32), w_down.astype(jnp.float32), ln_gain.astype(jnp.float32), ln_bias.astype(jnp.float32), qk_gain.astype(jnp.float32))
    inputs_all = tokens.astype(jnp.float32).reshape(HOLDERS, ROWS, D)
    cot_all = cotangent.astype(jnp.float32).reshape(HOLDERS, ROWS, D)
    position = jnp.arange(ROWS, dtype=jnp.int32)

    def layer_step(totals, members):
        x, cot_rows, lengths = members
        limits = jnp.cumsum(lengths).astype(jnp.int32)
        segment = lax.optimization_barrier(jnp.sum((position[:, None] >= limits[None, :]).astype(jnp.int32), axis=1))
        valid_rows = (position < limits[-1]).astype(jnp.float32)[:, None]

        def closed(x_in, wq, wo, wu, wd, lg, lb, qg):
            return forward_rows(x_in, wq, wo, wu, wd, lg, lb, qg, segment, valid_rows)
        y, pullback = jax.vjp(closed, x, weights_all[0], weights_all[1], weights_all[2], weights_all[3], weights_all[4], weights_all[5], weights_all[6])
        gradients = pullback(cot_rows)
        totals = tuple((t + g for t, g in zip(totals, gradients[1:])))
        return (totals, (y.astype(jnp.bfloat16), gradients[0].astype(jnp.bfloat16)))
    zeros_init = tuple((jnp.zeros(w.shape, jnp.float32) for w in weights_all))
    totals, outputs_all = lax.scan(layer_step, zeros_init, (inputs_all, cot_all, image_lengths))
    layer_out = outputs_all[0].reshape(TOKENS, D)
    grad_tokens = outputs_all[1].reshape(TOKENS, D)
    return (layer_out, grad_tokens, totals[0], totals[1], totals[2], totals[3], totals[4], totals[5], totals[6])
```

```python
from functools import partial

import jax
import jax.numpy as jnp
from jax import lax
from jax.sharding import PartitionSpec as P

HEADS = 12
HEAD_DIM = 64
PATCH_BIG = 576


epsilon = 1e-06


def layer_norm(v, gain_row, bias_row):
    centre = v - jnp.mean(v, axis=-1, keepdims=True)
    spread = jnp.mean(centre * centre, axis=-1, keepdims=True)
    return centre * lax.rsqrt(spread + epsilon) * gain_row + bias_row


def head_norm(v, gain_row):
    centre = v - jnp.mean(v, axis=-1, keepdims=True)
    spread = jnp.mean(centre * centre, axis=-1, keepdims=True)
    return centre * lax.rsqrt(spread + epsilon) * gain_row


def both_norms(q_in, k_in, q_gain, k_gain):
    return (head_norm(q_in, q_gain), head_norm(k_in, k_gain))


NF_FAST = 4
NDP_FAST = 8


def _flat_pieces(mats, gains, d, ndp):
    parts = []
    for x in mats:
        r = x.shape[0] // ndp
        parts.append(lax.dynamic_slice_in_dim(x, d * r, r, 0).reshape(-1))
    for g in gains:
        r = g.shape[1] // ndp
        parts.append(lax.dynamic_slice_in_dim(g, d * r, r, 1).reshape(-1))
    return jnp.concatenate(parts)


def _plane_gather(z):
    d = lax.axis_index("dp")
    c = d % 2
    a = lax.ppermute(z, "dp", [(i, i ^ 2) for i in range(NDP_FAST)])
    b = lax.ppermute(z, "dp", [(i, i ^ 4) for i in range(NDP_FAST)])
    send = jnp.where(c == 0, b, a)
    diag = lax.ppermute(
        send, "dp", [(i, i ^ 2) if i % 2 == 0 else (i, i ^ 4) for i in range(NDP_FAST)]
    )
    mine = jnp.stack([z, a, b, diag])
    sib = lax.ppermute(mine, "dp", [(i, i ^ 1) for i in range(NDP_FAST)])
    return jnp.stack([mine[0], sib[0], mine[1], sib[1], mine[2], sib[2], mine[3], sib[3]])


def fast_gather(mats, gains):
    d = lax.axis_index("dp")
    f = lax.axis_index("fsdp")
    own = _flat_pieces(mats, gains, d, NDP_FAST)
    slots = [own] + [
        lax.ppermute(own, "fsdp", [(i, (i + k) % NF_FAST) for i in range(NF_FAST)])
        for k in range(1, NF_FAST)
    ]
    z = jnp.stack(slots)
    x = _plane_gather(z)
    e_idx = jnp.arange(NDP_FAST, dtype=jnp.int32) ^ d
    f_idx = (f - jnp.arange(NF_FAST, dtype=jnp.int32)) % NF_FAST
    x = jnp.take(jnp.take(x, e_idx, axis=0), f_idx, axis=1)
    out = []
    offset = 0
    for m in mats:
        r, cols = m.shape[0] // NDP_FAST, m.shape[1]
        seg = x[:, :, offset : offset + r * cols].reshape(NDP_FAST, NF_FAST, r, cols)
        out.append(seg.transpose(1, 0, 2, 3).reshape(NF_FAST * m.shape[0], cols))
        offset += r * cols
    for g in gains:
        rows, r = g.shape[0], g.shape[1] // NDP_FAST
        seg = x[:, :, offset : offset + rows * r].reshape(NDP_FAST, NF_FAST, rows, r)
        out.append(seg.transpose(2, 1, 0, 3).reshape(rows, NF_FAST * g.shape[1]))
        offset += rows * r
    return out


def fast_reduce(mats, gains):
    d = lax.axis_index("dp")
    f = lax.axis_index("fsdp")
    c = d % 2
    parts = []
    for m in mats:
        rows, cols = m.shape
        parts.append(m.astype(jnp.bfloat16).reshape(NF_FAST, NDP_FAST, -1))
    for g in gains:
        rows, cols = g.shape
        r = cols // (NF_FAST * NDP_FAST)
        seg = g.astype(jnp.bfloat16).reshape(rows, NF_FAST, NDP_FAST, r).transpose(1, 2, 0, 3)
        parts.append(seg.reshape(NF_FAST, NDP_FAST, -1))
    flat = jnp.concatenate(parts, axis=2)
    e_idx = jnp.arange(NDP_FAST, dtype=jnp.int32) ^ d
    bx = jnp.take(flat, e_idx, axis=1)
    got = lax.ppermute(bx[:, 1::2], "dp", [(i, i ^ 1) for i in range(NDP_FAST)])
    chip = bx[:, 0::2].astype(jnp.float32) + got.astype(jnp.float32)
    moved = lax.ppermute(
        chip[:, 3].astype(jnp.bfloat16),
        "dp",
        [(i, i ^ 2) if i % 2 == 0 else (i, i ^ 4) for i in range(NDP_FAST)],
    ).astype(jnp.float32)
    to_x = chip[:, 1] + jnp.where(c == 1, moved, 0.0)
    to_y = chip[:, 2] + jnp.where(c == 0, moved, 0.0)
    from_x = lax.ppermute(to_x.astype(jnp.bfloat16), "dp", [(i, i ^ 2) for i in range(NDP_FAST)])
    from_y = lax.ppermute(to_y.astype(jnp.bfloat16), "dp", [(i, i ^ 4) for i in range(NDP_FAST)])
    plane = chip[:, 0] + from_x.astype(jnp.float32) + from_y.astype(jnp.float32)
    total = lax.dynamic_index_in_dim(plane, f, 0, keepdims=False)
    for k in range(1, NF_FAST):
        part = lax.dynamic_index_in_dim(plane, (f + k) % NF_FAST, 0, keepdims=False)
        total = total + lax.ppermute(
            part.astype(jnp.bfloat16), "fsdp", [(i, (i + k) % NF_FAST) for i in range(NF_FAST)]
        ).astype(jnp.float32)
    x = _plane_gather(total)
    x = jnp.take(x, e_idx, axis=0)
    out = []
    offset = 0
    for m in mats:
        rows, cols = m.shape
        r = rows // (NF_FAST * NDP_FAST)
        out.append(x[:, offset : offset + r * cols].reshape(NDP_FAST * r, cols))
        offset += r * cols
    for g in gains:
        rows, cols = g.shape
        r = cols // (NF_FAST * NDP_FAST)
        seg = x[:, offset : offset + rows * r].reshape(NDP_FAST, rows, r)
        out.append(seg.transpose(1, 0, 2).reshape(rows, NDP_FAST * r))
        offset += rows * r
    return out


def on_device(
    fast, tokens, image_lengths, w_qkv, w_out, w_up, w_down, ln_gain, ln_bias, qk_gain, cotangent
):
    if fast:
        full_qkv, full_out, full_up, full_down, gain_all, bias_all, qk_all = fast_gather(
            (w_qkv, w_out, w_up, w_down), (ln_gain, ln_bias, qk_gain)
        )
    else:
        full_qkv, full_out, full_up, full_down, gain_all, bias_all, qk_all = (
            lax.all_gather(w_qkv, "fsdp", axis=0, tiled=True),
            lax.all_gather(w_out, "fsdp", axis=0, tiled=True),
            lax.all_gather(w_up, "fsdp", axis=0, tiled=True),
            lax.all_gather(w_down, "fsdp", axis=0, tiled=True),
            lax.all_gather(ln_gain, "fsdp", axis=1, tiled=True),
            lax.all_gather(ln_bias, "fsdp", axis=1, tiled=True),
            lax.all_gather(qk_gain, "fsdp", axis=1, tiled=True),
        )
    length = tokens.shape[0]
    model_width = tokens.shape[1]
    blocks = length // PATCH_BIG
    scaling = HEAD_DIM ** (-0.5)
    position = jnp.arange(length, dtype=jnp.int32)
    limits = jnp.cumsum(image_lengths[0])
    segment = jnp.sum((position[:, None] >= limits[None, :]).astype(jnp.int32), axis=1)
    valid_rows = (position < limits[-1]).astype(jnp.float32)[:, None]
    norm_gains = gain_all.astype(jnp.float32)
    biases = bias_all.astype(jnp.float32)
    qk_gains = qk_all.astype(jnp.float32).reshape(2, HEADS, HEAD_DIM)
    inputs = tokens.astype(jnp.float32)
    normed, first_back = jax.vjp(layer_norm, inputs, norm_gains[0], biases[0])
    normed_low = normed.astype(jnp.bfloat16)
    project = jnp.dot(normed_low, full_qkv, preferred_element_type=jnp.float32)
    queries = project[:, :model_width].reshape(length, HEADS, HEAD_DIM)
    keys_raw = project[:, model_width : 2 * model_width].reshape(length, HEADS, HEAD_DIM)
    values_raw = project[:, 2 * model_width :]
    (q_norm, k_norm), norms_back = jax.vjp(both_norms, queries, keys_raw, qk_gains[0], qk_gains[1])
    q_low = q_norm.astype(jnp.bfloat16).reshape(blocks, PATCH_BIG, HEADS, HEAD_DIM)
    k_low = k_norm.astype(jnp.bfloat16).reshape(blocks, PATCH_BIG, HEADS, HEAD_DIM)
    v_low = values_raw.astype(jnp.bfloat16).reshape(blocks, PATCH_BIG, HEADS, HEAD_DIM)
    s_blocks = segment.reshape(blocks, PATCH_BIG)

    def block_scores(q_block, k_block, s_block):
        scores = (
            jnp.einsum("qhd,khd->hqk", q_block, k_block, preferred_element_type=jnp.float32)
            * scaling
        )
        return jnp.where((s_block[:, None] == s_block[None, :])[None], scores, -1e30)

    def attend(members):
        q_block, k_block, v_block, s_block = members
        scores = block_scores(q_block, k_block, s_block)
        row_top = jnp.max(scores, axis=-1, keepdims=True)
        exp_scores = jnp.exp(scores - row_top)
        row_total = jnp.sum(exp_scores, axis=-1, keepdims=True)
        probability = (exp_scores / row_total).astype(jnp.bfloat16)
        mixed_block = jnp.einsum(
            "hqk,khd->qhd", probability, v_block, preferred_element_type=jnp.float32
        )
        return (mixed_block, row_top + jnp.log(row_total))

    mixed_heads, log_total = lax.map(attend, (q_low, k_low, v_low, s_blocks))
    mixed_low = mixed_heads.reshape(length, model_width).astype(jnp.bfloat16)
    residual = inputs + jnp.dot(mixed_low, full_out, preferred_element_type=jnp.float32)
    second, second_back = jax.vjp(layer_norm, residual, norm_gains[1], biases[1])
    second_low = second.astype(jnp.bfloat16)
    up_pre = jnp.dot(second_low, full_up, preferred_element_type=jnp.float32)
    active, gelu_back = jax.vjp(partial(jax.nn.gelu, approximate=False), up_pre)
    active_low = active.astype(jnp.bfloat16)
    output = residual + jnp.dot(active_low, full_down, preferred_element_type=jnp.float32)
    layer_out = (valid_rows * output).astype(jnp.bfloat16)
    back_qkv, back_out, back_up, back_down = full_qkv, full_out, full_up, full_down
    upstream = cotangent.astype(jnp.float32) * valid_rows
    up_low = upstream.astype(jnp.bfloat16)
    grad_down = jnp.dot(active_low.T, up_low, preferred_element_type=jnp.float32)
    grad_active = jnp.dot(up_low, back_down.T, preferred_element_type=jnp.float32)
    (grad_pre,) = gelu_back(grad_active)
    pre_low = grad_pre.astype(jnp.bfloat16)
    grad_up = jnp.dot(second_low.T, pre_low, preferred_element_type=jnp.float32)
    grad_second = jnp.dot(pre_low, back_up.T, preferred_element_type=jnp.float32)
    grad_resid, gain_two, bias_two = second_back(grad_second)
    grad_resid = grad_resid + upstream
    resid_low = grad_resid.astype(jnp.bfloat16)
    grad_outw = jnp.dot(mixed_low.T, resid_low, preferred_element_type=jnp.float32)
    grad_mixed = jnp.dot(resid_low, back_out.T, preferred_element_type=jnp.float32)
    grad_mixed = grad_mixed.astype(jnp.bfloat16).reshape(blocks, PATCH_BIG, HEADS, HEAD_DIM)

    def attend_back(members):
        q_block, k_block, v_block, s_block, l_block, d_block = members
        scores = block_scores(q_block, k_block, s_block)
        probability = jnp.exp(scores - l_block)
        prob_low = probability.astype(jnp.bfloat16)
        grad_v = jnp.einsum("hqk,qhd->khd", prob_low, d_block, preferred_element_type=jnp.float32)
        grad_p = jnp.einsum("qhd,khd->hqk", d_block, v_block, preferred_element_type=jnp.float32)
        grad_p = lax.optimization_barrier(grad_p.astype(jnp.bfloat16)).astype(jnp.float32)
        grad_s = probability * (grad_p - jnp.sum(probability * grad_p, axis=-1, keepdims=True))
        s_low = grad_s.astype(jnp.bfloat16)
        grad_q = (
            jnp.einsum("hqk,khd->qhd", s_low, k_block, preferred_element_type=jnp.float32) * scaling
        )
        grad_k = (
            jnp.einsum("hqk,qhd->khd", s_low, q_block, preferred_element_type=jnp.float32) * scaling
        )
        return (grad_q, grad_k, grad_v)

    grad_qn, grad_kn, grad_vn = lax.map(
        attend_back, (q_low, k_low, v_low, s_blocks, log_total, grad_mixed)
    )
    grad_q, grad_k, gain_q, gain_k = norms_back(
        (grad_qn.reshape(length, HEADS, HEAD_DIM), grad_kn.reshape(length, HEADS, HEAD_DIM))
    )
    grad_project = jnp.concatenate(
        [
            grad_q.reshape(length, model_width),
            grad_k.reshape(length, model_width),
            grad_vn.reshape(length, model_width),
        ],
        axis=1,
    ).astype(jnp.bfloat16)
    grad_qkv = jnp.dot(normed_low.T, grad_project, preferred_element_type=jnp.float32)
    grad_normed = jnp.dot(grad_project, back_qkv.T, preferred_element_type=jnp.float32)
    grad_input, gain_one, bias_one = first_back(grad_normed)
    grad_tokens = (grad_input + grad_resid).astype(jnp.bfloat16)
    grad_gain = jnp.stack([gain_one, gain_two])
    grad_bias = jnp.stack([bias_one, bias_two])
    grad_qk = jnp.stack([gain_q.reshape(model_width), gain_k.reshape(model_width)])
    summands = (grad_qkv, grad_outw, grad_up, grad_down, grad_gain, grad_bias, grad_qk)
    if fast:
        shares = fast_reduce(summands[:4], summands[4:])
    else:
        pieces = [
            lax.psum_scatter(
                s.astype(jnp.bfloat16), "fsdp", scatter_dimension=0 if k < 4 else 1, tiled=True
            ).astype(jnp.float32)
            for k, s in enumerate(summands)
        ]
        shares = [lax.psum(p.astype(jnp.bfloat16), "dp").astype(jnp.float32) for p in pieces]
    return (
        layer_out,
        grad_tokens,
        shares[0],
        shares[1],
        shares[2],
        shares[3],
        shares[4],
        shares[5],
        shares[6],
    )


def solution(mesh):
    in_specs = (
        P(("dp", "fsdp"), None),
        P(("dp", "fsdp"), None),
        P("fsdp", None),
        P("fsdp", None),
        P("fsdp", None),
        P("fsdp", None),
        P(None, "fsdp"),
        P(None, "fsdp"),
        P(None, "fsdp"),
        P(("dp", "fsdp"), None),
    )
    out_specs = (
        P(("dp", "fsdp"), None),
        P(("dp", "fsdp"), None),
        P("fsdp", None),
        P("fsdp", None),
        P("fsdp", None),
        P("fsdp", None),
        P(None, "fsdp"),
        P(None, "fsdp"),
        P(None, "fsdp"),
    )
    fast = dict(mesh.shape) == {"dp": NDP_FAST, "fsdp": NF_FAST}
    return jax.shard_map(
        partial(on_device, fast), mesh=mesh, in_specs=in_specs, out_specs=out_specs, check_vma=False
    )
```

```python
from functools import partial

import jax
import jax.numpy as jnp
from jax import lax
from jax.sharding import PartitionSpec as P

HEADS = 12
HEAD_DIM = 64
PATCH_BIG = 576


epsilon = 1e-06


def layer_norm(v, gain_row, bias_row):
    centre = v - jnp.mean(v, axis=-1, keepdims=True)
    spread = jnp.mean(centre * centre, axis=-1, keepdims=True)
    return centre * lax.rsqrt(spread + epsilon) * gain_row + bias_row


def head_norm(v, gain_row):
    centre = v - jnp.mean(v, axis=-1, keepdims=True)
    spread = jnp.mean(centre * centre, axis=-1, keepdims=True)
    return centre * lax.rsqrt(spread + epsilon) * gain_row


def both_norms(q_in, k_in, q_gain, k_gain):
    return (head_norm(q_in, q_gain), head_norm(k_in, k_gain))


NF_FAST = 4
NDP_FAST = 8


LANES = 128


def _to_rows(v):
    return v.reshape(-1, LANES)


def _gain_rows(gains, pick):
    flat = jnp.concatenate([pick(g).reshape(-1) for g in gains])
    pad = (-flat.shape[0]) % LANES
    return jnp.pad(flat, (0, pad)).reshape(-1, LANES)


def _plane_gather(z):
    d = lax.axis_index("dp")
    c = d % 2
    a = lax.ppermute(z, "dp", [(i, i ^ 2) for i in range(NDP_FAST)])
    b = lax.ppermute(z, "dp", [(i, i ^ 4) for i in range(NDP_FAST)])
    send = jnp.where(c == 0, b, a)
    diag = lax.ppermute(
        send, "dp", [(i, i ^ 2) if i % 2 == 0 else (i, i ^ 4) for i in range(NDP_FAST)]
    )
    mine = jnp.stack([z, a, b, diag])
    sib = lax.ppermute(mine, "dp", [(i, i ^ 1) for i in range(NDP_FAST)])
    return jnp.stack([mine[0], sib[0], mine[1], sib[1], mine[2], sib[2], mine[3], sib[3]])


def _take(x, idx, axis):
    return jnp.take(x, idx, axis=axis, mode="wrap")


def fast_gather(mats, gains):
    d = lax.axis_index("dp")
    f = lax.axis_index("fsdp")
    parts = []
    for m in mats:
        r = m.shape[0] // NDP_FAST
        parts.append(_to_rows(lax.dynamic_slice_in_dim(m, d * r, r, 0)))
    gr = gains[0].shape[1] // NDP_FAST
    parts.append(_gain_rows(gains, lambda g: lax.dynamic_slice_in_dim(g, d * gr, gr, 1)))
    own = jnp.concatenate(parts)
    slots = [own] + [
        lax.ppermute(own, "fsdp", [(i, (i + k) % NF_FAST) for i in range(NF_FAST)])
        for k in range(1, NF_FAST)
    ]
    x = _plane_gather(jnp.stack(slots))
    e_idx = jnp.arange(NDP_FAST, dtype=jnp.int32) ^ d
    f_idx = (f - jnp.arange(NF_FAST, dtype=jnp.int32)) % NF_FAST
    x = _take(_take(x, e_idx, 0), f_idx, 1)
    out = []
    row = 0
    for m in mats:
        r, cols = m.shape[0] // NDP_FAST, m.shape[1]
        n_rows = r * cols // LANES
        seg = x[:, :, row : row + n_rows].reshape(NDP_FAST, NF_FAST, r, cols)
        out.append(seg.transpose(1, 0, 2, 3).reshape(NF_FAST * m.shape[0], cols))
        row += n_rows
    flat = x[:, :, row:].reshape(NDP_FAST, NF_FAST, -1)
    offset = 0
    for g in gains:
        rows = g.shape[0]
        seg = flat[:, :, offset : offset + rows * gr].reshape(NDP_FAST, NF_FAST, rows, gr)
        out.append(seg.transpose(2, 1, 0, 3).reshape(rows, NF_FAST * g.shape[1]))
        offset += rows * gr
    return out


def fast_reduce(mats, gains):
    d = lax.axis_index("dp")
    f = lax.axis_index("fsdp")
    c = d % 2
    n_shards = NF_FAST * NDP_FAST
    parts = []
    for m in mats:
        parts.append(m.astype(jnp.bfloat16).reshape(NF_FAST, NDP_FAST, -1, LANES))
    gr = gains[0].shape[1] // n_shards
    flat_g = jnp.concatenate(
        [
            g.astype(jnp.bfloat16).reshape(g.shape[0], NF_FAST, NDP_FAST, gr).transpose(1, 2, 0, 3)
            .reshape(NF_FAST, NDP_FAST, -1)
            for g in gains
        ],
        axis=2,
    )
    pad = (-flat_g.shape[2]) % LANES
    parts.append(jnp.pad(flat_g, ((0, 0), (0, 0), (0, pad))).reshape(NF_FAST, NDP_FAST, -1, LANES))
    flat = jnp.concatenate(parts, axis=2)
    home = _take(flat, jnp.array([0, 2, 4, 6], dtype=jnp.int32) ^ d, 1)
    away = _take(flat, jnp.array([1, 3, 5, 7], dtype=jnp.int32) ^ d, 1)
    got = lax.ppermute(away, "dp", [(i, i ^ 1) for i in range(NDP_FAST)])
    chip = home.astype(jnp.float32) + got.astype(jnp.float32)
    moved = lax.ppermute(
        chip[:, 3].astype(jnp.bfloat16),
        "dp",
        [(i, i ^ 2) if i % 2 == 0 else (i, i ^ 4) for i in range(NDP_FAST)],
    ).astype(jnp.float32)
    to_x = chip[:, 1] + jnp.where(c == 1, moved, 0.0)
    to_y = chip[:, 2] + jnp.where(c == 0, moved, 0.0)
    from_x = lax.ppermute(to_x.astype(jnp.bfloat16), "dp", [(i, i ^ 2) for i in range(NDP_FAST)])
    from_y = lax.ppermute(to_y.astype(jnp.bfloat16), "dp", [(i, i ^ 4) for i in range(NDP_FAST)])
    plane = chip[:, 0] + from_x.astype(jnp.float32) + from_y.astype(jnp.float32)
    total = lax.dynamic_index_in_dim(plane, f, 0, keepdims=False)
    for k in range(1, NF_FAST):
        part = lax.dynamic_index_in_dim(plane, (f + k) % NF_FAST, 0, keepdims=False)
        total = total + lax.ppermute(
            part.astype(jnp.bfloat16), "fsdp", [(i, (i + k) % NF_FAST) for i in range(NF_FAST)]
        ).astype(jnp.float32)
    x = _take(_plane_gather(total), jnp.arange(NDP_FAST, dtype=jnp.int32) ^ d, 0)
    out = []
    row = 0
    for m in mats:
        rows, cols = m.shape
        r = rows // n_shards
        n_rows = r * cols // LANES
        out.append(x[:, row : row + n_rows].reshape(NDP_FAST * r, cols))
        row += n_rows
    flat_out = x[:, row:].reshape(NDP_FAST, -1)
    offset = 0
    for g in gains:
        rows = g.shape[0]
        seg = flat_out[:, offset : offset + rows * gr].reshape(NDP_FAST, rows, gr)
        out.append(seg.transpose(1, 0, 2).reshape(rows, NDP_FAST * gr))
        offset += rows * gr
    return out


def on_device(
    fast, tokens, image_lengths, w_qkv, w_out, w_up, w_down, ln_gain, ln_bias, qk_gain, cotangent
):
    if fast:
        full_qkv, full_out, full_up, full_down, gain_all, bias_all, qk_all = fast_gather(
            (w_qkv, w_out, w_up, w_down), (ln_gain, ln_bias, qk_gain)
        )
    else:
        full_qkv, full_out, full_up, full_down, gain_all, bias_all, qk_all = (
            lax.all_gather(w_qkv, "fsdp", axis=0, tiled=True),
            lax.all_gather(w_out, "fsdp", axis=0, tiled=True),
            lax.all_gather(w_up, "fsdp", axis=0, tiled=True),
            lax.all_gather(w_down, "fsdp", axis=0, tiled=True),
            lax.all_gather(ln_gain, "fsdp", axis=1, tiled=True),
            lax.all_gather(ln_bias, "fsdp", axis=1, tiled=True),
            lax.all_gather(qk_gain, "fsdp", axis=1, tiled=True),
        )
    length = tokens.shape[0]
    model_width = tokens.shape[1]
    blocks = length // PATCH_BIG
    scaling = HEAD_DIM ** (-0.5)
    position = jnp.arange(length, dtype=jnp.int32)
    limits = jnp.cumsum(image_lengths[0])
    segment = jnp.sum((position[:, None] >= limits[None, :]).astype(jnp.int32), axis=1)
    valid_rows = (position < limits[-1]).astype(jnp.float32)[:, None]
    norm_gains = gain_all.astype(jnp.float32)
    biases = bias_all.astype(jnp.float32)
    qk_gains = qk_all.astype(jnp.float32).reshape(2, HEADS, HEAD_DIM)
    inputs = tokens.astype(jnp.float32)
    normed, first_back = jax.vjp(layer_norm, inputs, norm_gains[0], biases[0])
    normed_low = normed.astype(jnp.bfloat16)
    project = jnp.dot(normed_low, full_qkv, preferred_element_type=jnp.float32)
    queries = project[:, :model_width].reshape(length, HEADS, HEAD_DIM)
    keys_raw = project[:, model_width : 2 * model_width].reshape(length, HEADS, HEAD_DIM)
    values_raw = project[:, 2 * model_width :]
    (q_norm, k_norm), norms_back = jax.vjp(both_norms, queries, keys_raw, qk_gains[0], qk_gains[1])
    q_low = q_norm.astype(jnp.bfloat16).reshape(blocks, PATCH_BIG, HEADS, HEAD_DIM)
    k_low = k_norm.astype(jnp.bfloat16).reshape(blocks, PATCH_BIG, HEADS, HEAD_DIM)
    v_low = values_raw.astype(jnp.bfloat16).reshape(blocks, PATCH_BIG, HEADS, HEAD_DIM)
    s_blocks = segment.reshape(blocks, PATCH_BIG)

    def block_scores(q_block, k_block, s_block):
        scores = (
            jnp.einsum("qhd,khd->hqk", q_block, k_block, preferred_element_type=jnp.float32)
            * scaling
        )
        return jnp.where((s_block[:, None] == s_block[None, :])[None], scores, -1e30)

    def attend(members):
        q_block, k_block, v_block, s_block = members
        scores = block_scores(q_block, k_block, s_block)
        row_top = jnp.max(scores, axis=-1, keepdims=True)
        exp_scores = jnp.exp(scores - row_top)
        row_total = jnp.sum(exp_scores, axis=-1, keepdims=True)
        probability = (exp_scores / row_total).astype(jnp.bfloat16)
        mixed_block = jnp.einsum(
            "hqk,khd->qhd", probability, v_block, preferred_element_type=jnp.float32
        )
        return (mixed_block, row_top + jnp.log(row_total))

    mixed_heads, log_total = lax.map(attend, (q_low, k_low, v_low, s_blocks))
    mixed_low = mixed_heads.reshape(length, model_width).astype(jnp.bfloat16)
    residual = inputs + jnp.dot(mixed_low, full_out, preferred_element_type=jnp.float32)
    second, second_back = jax.vjp(layer_norm, residual, norm_gains[1], biases[1])
    second_low = second.astype(jnp.bfloat16)
    up_pre = jnp.dot(second_low, full_up, preferred_element_type=jnp.float32)
    active, gelu_back = jax.vjp(partial(jax.nn.gelu, approximate=False), up_pre)
    active_low = active.astype(jnp.bfloat16)
    output = residual + jnp.dot(active_low, full_down, preferred_element_type=jnp.float32)
    layer_out = (valid_rows * output).astype(jnp.bfloat16)
    back_qkv, back_out, back_up, back_down = full_qkv, full_out, full_up, full_down
    upstream = cotangent.astype(jnp.float32) * valid_rows
    up_low = upstream.astype(jnp.bfloat16)
    grad_down = jnp.dot(active_low.T, up_low, preferred_element_type=jnp.float32)
    grad_active = jnp.dot(up_low, back_down.T, preferred_element_type=jnp.float32)
    (grad_pre,) = gelu_back(grad_active)
    pre_low = grad_pre.astype(jnp.bfloat16)
    grad_up = jnp.dot(second_low.T, pre_low, preferred_element_type=jnp.float32)
    grad_second = jnp.dot(pre_low, back_up.T, preferred_element_type=jnp.float32)
    grad_resid, gain_two, bias_two = second_back(grad_second)
    grad_resid = grad_resid + upstream
    resid_low = grad_resid.astype(jnp.bfloat16)
    grad_outw = jnp.dot(mixed_low.T, resid_low, preferred_element_type=jnp.float32)
    grad_mixed = jnp.dot(resid_low, back_out.T, preferred_element_type=jnp.float32)
    grad_mixed = grad_mixed.astype(jnp.bfloat16).reshape(blocks, PATCH_BIG, HEADS, HEAD_DIM)

    def attend_back(members):
        q_block, k_block, v_block, s_block, l_block, d_block = members
        scores = block_scores(q_block, k_block, s_block)
        probability = jnp.exp(scores - l_block)
        prob_low = probability.astype(jnp.bfloat16)
        grad_v = jnp.einsum("hqk,qhd->khd", prob_low, d_block, preferred_element_type=jnp.float32)
        grad_p = jnp.einsum("qhd,khd->hqk", d_block, v_block, preferred_element_type=jnp.float32)
        grad_p = lax.optimization_barrier(grad_p.astype(jnp.bfloat16)).astype(jnp.float32)
        grad_s = probability * (grad_p - jnp.sum(probability * grad_p, axis=-1, keepdims=True))
        s_low = grad_s.astype(jnp.bfloat16)
        grad_q = (
            jnp.einsum("hqk,khd->qhd", s_low, k_block, preferred_element_type=jnp.float32) * scaling
        )
        grad_k = (
            jnp.einsum("hqk,qhd->khd", s_low, q_block, preferred_element_type=jnp.float32) * scaling
        )
        return (grad_q, grad_k, grad_v)

    grad_qn, grad_kn, grad_vn = lax.map(
        attend_back, (q_low, k_low, v_low, s_blocks, log_total, grad_mixed)
    )
    grad_q, grad_k, gain_q, gain_k = norms_back(
        (grad_qn.reshape(length, HEADS, HEAD_DIM), grad_kn.reshape(length, HEADS, HEAD_DIM))
    )
    grad_project = jnp.concatenate(
        [
            grad_q.reshape(length, model_width),
            grad_k.reshape(length, model_width),
            grad_vn.reshape(length, model_width),
        ],
        axis=1,
    ).astype(jnp.bfloat16)
    grad_qkv = jnp.dot(normed_low.T, grad_project, preferred_element_type=jnp.float32)
    grad_normed = jnp.dot(grad_project, back_qkv.T, preferred_element_type=jnp.float32)
    grad_input, gain_one, bias_one = first_back(grad_normed)
    grad_tokens = (grad_input + grad_resid).astype(jnp.bfloat16)
    grad_gain = jnp.stack([gain_one, gain_two])
    grad_bias = jnp.stack([bias_one, bias_two])
    grad_qk = jnp.stack([gain_q.reshape(model_width), gain_k.reshape(model_width)])
    summands = (grad_qkv, grad_outw, grad_up, grad_down, grad_gain, grad_bias, grad_qk)
    if fast:
        shares = fast_reduce(summands[:4], summands[4:])
    else:
        pieces = [
            lax.psum_scatter(
                s.astype(jnp.bfloat16), "fsdp", scatter_dimension=0 if k < 4 else 1, tiled=True
            ).astype(jnp.float32)
            for k, s in enumerate(summands)
        ]
        shares = [lax.psum(p.astype(jnp.bfloat16), "dp").astype(jnp.float32) for p in pieces]
    return (
        layer_out,
        grad_tokens,
        shares[0],
        shares[1],
        shares[2],
        shares[3],
        shares[4],
        shares[5],
        shares[6],
    )


def solution(mesh):
    in_specs = (
        P(("dp", "fsdp"), None),
        P(("dp", "fsdp"), None),
        P("fsdp", None),
        P("fsdp", None),
        P("fsdp", None),
        P("fsdp", None),
        P(None, "fsdp"),
        P(None, "fsdp"),
        P(None, "fsdp"),
        P(("dp", "fsdp"), None),
    )
    out_specs = (
        P(("dp", "fsdp"), None),
        P(("dp", "fsdp"), None),
        P("fsdp", None),
        P("fsdp", None),
        P("fsdp", None),
        P("fsdp", None),
        P(None, "fsdp"),
        P(None, "fsdp"),
        P(None, "fsdp"),
    )
    fast = dict(mesh.shape) == {"dp": NDP_FAST, "fsdp": NF_FAST}
    return jax.shard_map(
        partial(on_device, fast), mesh=mesh, in_specs=in_specs, out_specs=out_specs, check_vma=False
    )
```

```python
from functools import partial

import jax
import jax.numpy as jnp
from jax import lax
from jax.sharding import PartitionSpec as P

HEADS = 12
HEAD_DIM = 64
PATCH_BIG = 576


epsilon = 1e-06


def layer_norm(v, gain_row, bias_row):
    centre = v - jnp.mean(v, axis=-1, keepdims=True)
    spread = jnp.mean(centre * centre, axis=-1, keepdims=True)
    return centre * lax.rsqrt(spread + epsilon) * gain_row + bias_row


def head_norm(v, gain_row):
    centre = v - jnp.mean(v, axis=-1, keepdims=True)
    spread = jnp.mean(centre * centre, axis=-1, keepdims=True)
    return centre * lax.rsqrt(spread + epsilon) * gain_row


def both_norms(q_in, k_in, q_gain, k_gain):
    return (head_norm(q_in, q_gain), head_norm(k_in, k_gain))


NF_FAST = 4
NDP_FAST = 8


LANES = 128


def _to_rows(v):
    return v.reshape(-1, LANES)


def _gain_rows(gains, pick):
    flat = jnp.concatenate([pick(g).reshape(-1) for g in gains])
    pad = (-flat.shape[0]) % LANES
    return jnp.pad(flat, (0, pad)).reshape(-1, LANES)


def _plane_gather(z):
    d = lax.axis_index("dp")
    c = d % 2
    a = lax.ppermute(z, "dp", [(i, i ^ 2) for i in range(NDP_FAST)])
    b = lax.ppermute(z, "dp", [(i, i ^ 4) for i in range(NDP_FAST)])
    send = jnp.where(c == 0, b, a)
    diag = lax.ppermute(
        send, "dp", [(i, i ^ 2) if i % 2 == 0 else (i, i ^ 4) for i in range(NDP_FAST)]
    )
    mine = jnp.stack([z, a, b, diag])
    sib = lax.ppermute(mine, "dp", [(i, i ^ 1) for i in range(NDP_FAST)])
    return jnp.stack([mine[0], sib[0], mine[1], sib[1], mine[2], sib[2], mine[3], sib[3]])


def _take(x, idx, axis):
    return jnp.take(x, idx, axis=axis, mode="wrap")


def _z_gather(piece):
    f = lax.axis_index("fsdp")
    slots = [piece] + [
        lax.ppermute(piece, "fsdp", [(i, (i + k) % NF_FAST) for i in range(NF_FAST)])
        for k in range(1, NF_FAST)
    ]
    return _take(jnp.stack(slots), (f - jnp.arange(NF_FAST, dtype=jnp.int32)) % NF_FAST, 0)


def _gather_matrix(m):
    d = lax.axis_index("dp")
    j, c = d // 2, d % 2
    rows, cols = m.shape[0] // (NDP_FAST // 2), m.shape[1] // 2
    piece = lax.dynamic_slice(m, (j * rows, c * cols), (rows, cols))
    z = _z_gather(piece)
    x = lax.all_gather(z, "dp", axis=1, tiled=False)
    x = x.reshape(NF_FAST, NDP_FAST // 2, 2, rows, cols).transpose(0, 1, 3, 2, 4)
    return x.reshape(NF_FAST * m.shape[0], m.shape[1])


def fast_gather(mats, gains):
    out = [_gather_matrix(m) for m in mats]
    stacked = jnp.concatenate(gains, axis=0)
    z = _z_gather(stacked)
    full = z.transpose(1, 0, 2).reshape(stacked.shape[0], NF_FAST * stacked.shape[1])
    rows = 0
    for g in gains:
        out.append(full[rows : rows + g.shape[0]])
        rows += g.shape[0]
    return out


def fast_reduce(mats, gains):
    d = lax.axis_index("dp")
    f = lax.axis_index("fsdp")
    c = d % 2
    n_shards = NF_FAST * NDP_FAST
    parts = []
    for m in mats:
        parts.append(m.astype(jnp.bfloat16).reshape(NF_FAST, NDP_FAST, -1, LANES))
    gr = gains[0].shape[1] // n_shards
    flat_g = jnp.concatenate(
        [
            g.astype(jnp.bfloat16).reshape(g.shape[0], NF_FAST, NDP_FAST, gr).transpose(1, 2, 0, 3)
            .reshape(NF_FAST, NDP_FAST, -1)
            for g in gains
        ],
        axis=2,
    )
    pad = (-flat_g.shape[2]) % LANES
    parts.append(jnp.pad(flat_g, ((0, 0), (0, 0), (0, pad))).reshape(NF_FAST, NDP_FAST, -1, LANES))
    flat = jnp.concatenate(parts, axis=2)
    home = _take(flat, jnp.array([0, 2, 4, 6], dtype=jnp.int32) ^ d, 1)
    away = _take(flat, jnp.array([1, 3, 5, 7], dtype=jnp.int32) ^ d, 1)
    got = lax.ppermute(away, "dp", [(i, i ^ 1) for i in range(NDP_FAST)])
    chip = home.astype(jnp.float32) + got.astype(jnp.float32)
    moved = lax.ppermute(
        chip[:, 3].astype(jnp.bfloat16),
        "dp",
        [(i, i ^ 2) if i % 2 == 0 else (i, i ^ 4) for i in range(NDP_FAST)],
    ).astype(jnp.float32)
    to_x = chip[:, 1] + jnp.where(c == 1, moved, 0.0)
    to_y = chip[:, 2] + jnp.where(c == 0, moved, 0.0)
    from_x = lax.ppermute(to_x.astype(jnp.bfloat16), "dp", [(i, i ^ 2) for i in range(NDP_FAST)])
    from_y = lax.ppermute(to_y.astype(jnp.bfloat16), "dp", [(i, i ^ 4) for i in range(NDP_FAST)])
    plane = chip[:, 0] + from_x.astype(jnp.float32) + from_y.astype(jnp.float32)
    total = lax.dynamic_index_in_dim(plane, f, 0, keepdims=False)
    for k in range(1, NF_FAST):
        part = lax.dynamic_index_in_dim(plane, (f + k) % NF_FAST, 0, keepdims=False)
        total = total + lax.ppermute(
            part.astype(jnp.bfloat16), "fsdp", [(i, (i + k) % NF_FAST) for i in range(NF_FAST)]
        ).astype(jnp.float32)
    x = _take(_plane_gather(total), jnp.arange(NDP_FAST, dtype=jnp.int32) ^ d, 0)
    out = []
    row = 0
    for m in mats:
        rows, cols = m.shape
        r = rows // n_shards
        n_rows = r * cols // LANES
        out.append(x[:, row : row + n_rows].reshape(NDP_FAST * r, cols))
        row += n_rows
    flat_out = x[:, row:].reshape(NDP_FAST, -1)
    offset = 0
    for g in gains:
        rows = g.shape[0]
        seg = flat_out[:, offset : offset + rows * gr].reshape(NDP_FAST, rows, gr)
        out.append(seg.transpose(1, 0, 2).reshape(rows, NDP_FAST * gr))
        offset += rows * gr
    return out


def on_device(
    fast, tokens, image_lengths, w_qkv, w_out, w_up, w_down, ln_gain, ln_bias, qk_gain, cotangent
):
    if fast:
        full_qkv, full_out, full_up, full_down, gain_all, bias_all, qk_all = fast_gather(
            (w_qkv, w_out, w_up, w_down), (ln_gain, ln_bias, qk_gain)
        )
    else:
        full_qkv, full_out, full_up, full_down, gain_all, bias_all, qk_all = (
            lax.all_gather(w_qkv, "fsdp", axis=0, tiled=True),
            lax.all_gather(w_out, "fsdp", axis=0, tiled=True),
            lax.all_gather(w_up, "fsdp", axis=0, tiled=True),
            lax.all_gather(w_down, "fsdp", axis=0, tiled=True),
            lax.all_gather(ln_gain, "fsdp", axis=1, tiled=True),
            lax.all_gather(ln_bias, "fsdp", axis=1, tiled=True),
            lax.all_gather(qk_gain, "fsdp", axis=1, tiled=True),
        )
    length = tokens.shape[0]
    model_width = tokens.shape[1]
    blocks = length // PATCH_BIG
    scaling = HEAD_DIM ** (-0.5)
    position = jnp.arange(length, dtype=jnp.int32)
    limits = jnp.cumsum(image_lengths[0])
    segment = jnp.sum((position[:, None] >= limits[None, :]).astype(jnp.int32), axis=1)
    valid_rows = (position < limits[-1]).astype(jnp.float32)[:, None]
    norm_gains = gain_all.astype(jnp.float32)
    biases = bias_all.astype(jnp.float32)
    qk_gains = qk_all.astype(jnp.float32).reshape(2, HEADS, HEAD_DIM)
    inputs = tokens.astype(jnp.float32)
    normed, first_back = jax.vjp(layer_norm, inputs, norm_gains[0], biases[0])
    normed_low = normed.astype(jnp.bfloat16)
    project = jnp.dot(normed_low, full_qkv, preferred_element_type=jnp.float32)
    queries = project[:, :model_width].reshape(length, HEADS, HEAD_DIM)
    keys_raw = project[:, model_width : 2 * model_width].reshape(length, HEADS, HEAD_DIM)
    values_raw = project[:, 2 * model_width :]
    (q_norm, k_norm), norms_back = jax.vjp(both_norms, queries, keys_raw, qk_gains[0], qk_gains[1])
    q_low = q_norm.astype(jnp.bfloat16).reshape(blocks, PATCH_BIG, HEADS, HEAD_DIM)
    k_low = k_norm.astype(jnp.bfloat16).reshape(blocks, PATCH_BIG, HEADS, HEAD_DIM)
    v_low = values_raw.astype(jnp.bfloat16).reshape(blocks, PATCH_BIG, HEADS, HEAD_DIM)
    s_blocks = segment.reshape(blocks, PATCH_BIG)

    def block_scores(q_block, k_block, s_block):
        scores = (
            jnp.einsum("qhd,khd->hqk", q_block, k_block, preferred_element_type=jnp.float32)
            * scaling
        )
        return jnp.where((s_block[:, None] == s_block[None, :])[None], scores, -1e30)

    def attend(members):
        q_block, k_block, v_block, s_block = members
        scores = block_scores(q_block, k_block, s_block)
        row_top = jnp.max(scores, axis=-1, keepdims=True)
        exp_scores = jnp.exp(scores - row_top)
        row_total = jnp.sum(exp_scores, axis=-1, keepdims=True)
        probability = (exp_scores / row_total).astype(jnp.bfloat16)
        mixed_block = jnp.einsum(
            "hqk,khd->qhd", probability, v_block, preferred_element_type=jnp.float32
        )
        return (mixed_block, row_top + jnp.log(row_total))

    mixed_heads, log_total = lax.map(attend, (q_low, k_low, v_low, s_blocks))
    mixed_low = mixed_heads.reshape(length, model_width).astype(jnp.bfloat16)
    residual = inputs + jnp.dot(mixed_low, full_out, preferred_element_type=jnp.float32)
    second, second_back = jax.vjp(layer_norm, residual, norm_gains[1], biases[1])
    second_low = second.astype(jnp.bfloat16)
    up_pre = jnp.dot(second_low, full_up, preferred_element_type=jnp.float32)
    active, gelu_back = jax.vjp(partial(jax.nn.gelu, approximate=False), up_pre)
    active_low = active.astype(jnp.bfloat16)
    output = residual + jnp.dot(active_low, full_down, preferred_element_type=jnp.float32)
    layer_out = (valid_rows * output).astype(jnp.bfloat16)
    back_qkv, back_out, back_up, back_down = full_qkv, full_out, full_up, full_down
    upstream = cotangent.astype(jnp.float32) * valid_rows
    up_low = upstream.astype(jnp.bfloat16)
    grad_down = jnp.dot(active_low.T, up_low, preferred_element_type=jnp.float32)
    grad_active = jnp.dot(up_low, back_down.T, preferred_element_type=jnp.float32)
    (grad_pre,) = gelu_back(grad_active)
    pre_low = grad_pre.astype(jnp.bfloat16)
    grad_up = jnp.dot(second_low.T, pre_low, preferred_element_type=jnp.float32)
    grad_second = jnp.dot(pre_low, back_up.T, preferred_element_type=jnp.float32)
    grad_resid, gain_two, bias_two = second_back(grad_second)
    grad_resid = grad_resid + upstream
    resid_low = grad_resid.astype(jnp.bfloat16)
    grad_outw = jnp.dot(mixed_low.T, resid_low, preferred_element_type=jnp.float32)
    grad_mixed = jnp.dot(resid_low, back_out.T, preferred_element_type=jnp.float32)
    grad_mixed = grad_mixed.astype(jnp.bfloat16).reshape(blocks, PATCH_BIG, HEADS, HEAD_DIM)

    def attend_back(members):
        q_block, k_block, v_block, s_block, l_block, d_block = members
        scores = block_scores(q_block, k_block, s_block)
        probability = jnp.exp(scores - l_block)
        prob_low = probability.astype(jnp.bfloat16)
        grad_v = jnp.einsum("hqk,qhd->khd", prob_low, d_block, preferred_element_type=jnp.float32)
        grad_p = jnp.einsum("qhd,khd->hqk", d_block, v_block, preferred_element_type=jnp.float32)
        grad_p = lax.optimization_barrier(grad_p.astype(jnp.bfloat16)).astype(jnp.float32)
        grad_s = probability * (grad_p - jnp.sum(probability * grad_p, axis=-1, keepdims=True))
        s_low = grad_s.astype(jnp.bfloat16)
        grad_q = (
            jnp.einsum("hqk,khd->qhd", s_low, k_block, preferred_element_type=jnp.float32) * scaling
        )
        grad_k = (
            jnp.einsum("hqk,qhd->khd", s_low, q_block, preferred_element_type=jnp.float32) * scaling
        )
        return (grad_q, grad_k, grad_v)

    grad_qn, grad_kn, grad_vn = lax.map(
        attend_back, (q_low, k_low, v_low, s_blocks, log_total, grad_mixed)
    )
    grad_q, grad_k, gain_q, gain_k = norms_back(
        (grad_qn.reshape(length, HEADS, HEAD_DIM), grad_kn.reshape(length, HEADS, HEAD_DIM))
    )
    grad_project = jnp.concatenate(
        [
            grad_q.reshape(length, model_width),
            grad_k.reshape(length, model_width),
            grad_vn.reshape(length, model_width),
        ],
        axis=1,
    ).astype(jnp.bfloat16)
    grad_qkv = jnp.dot(normed_low.T, grad_project, preferred_element_type=jnp.float32)
    grad_normed = jnp.dot(grad_project, back_qkv.T, preferred_element_type=jnp.float32)
    grad_input, gain_one, bias_one = first_back(grad_normed)
    grad_tokens = (grad_input + grad_resid).astype(jnp.bfloat16)
    grad_gain = jnp.stack([gain_one, gain_two])
    grad_bias = jnp.stack([bias_one, bias_two])
    grad_qk = jnp.stack([gain_q.reshape(model_width), gain_k.reshape(model_width)])
    summands = (grad_qkv, grad_outw, grad_up, grad_down, grad_gain, grad_bias, grad_qk)
    if fast:
        shares = fast_reduce(summands[:4], summands[4:])
    else:
        pieces = [
            lax.psum_scatter(
                s.astype(jnp.bfloat16), "fsdp", scatter_dimension=0 if k < 4 else 1, tiled=True
            ).astype(jnp.float32)
            for k, s in enumerate(summands)
        ]
        shares = [lax.psum(p.astype(jnp.bfloat16), "dp").astype(jnp.float32) for p in pieces]
    return (
        layer_out,
        grad_tokens,
        shares[0],
        shares[1],
        shares[2],
        shares[3],
        shares[4],
        shares[5],
        shares[6],
    )


def solution(mesh):
    in_specs = (
        P(("dp", "fsdp"), None),
        P(("dp", "fsdp"), None),
        P("fsdp", None),
        P("fsdp", None),
        P("fsdp", None),
        P("fsdp", None),
        P(None, "fsdp"),
        P(None, "fsdp"),
        P(None, "fsdp"),
        P(("dp", "fsdp"), None),
    )
    out_specs = (
        P(("dp", "fsdp"), None),
        P(("dp", "fsdp"), None),
        P("fsdp", None),
        P("fsdp", None),
        P("fsdp", None),
        P("fsdp", None),
        P(None, "fsdp"),
        P(None, "fsdp"),
        P(None, "fsdp"),
    )
    fast = dict(mesh.shape) == {"dp": NDP_FAST, "fsdp": NF_FAST}
    return jax.shard_map(
        partial(on_device, fast), mesh=mesh, in_specs=in_specs, out_specs=out_specs, check_vma=False
    )
```

```python
from functools import partial

import jax
import jax.numpy as jnp
from jax import lax
from jax.sharding import PartitionSpec as P

HEADS = 12
HEAD_DIM = 64
PATCH_BIG = 576


epsilon = 1e-06


def layer_norm(v, gain_row, bias_row):
    centre = v - jnp.mean(v, axis=-1, keepdims=True)
    spread = jnp.mean(centre * centre, axis=-1, keepdims=True)
    return centre * lax.rsqrt(spread + epsilon) * gain_row + bias_row


def head_norm(v, gain_row):
    centre = v - jnp.mean(v, axis=-1, keepdims=True)
    spread = jnp.mean(centre * centre, axis=-1, keepdims=True)
    return centre * lax.rsqrt(spread + epsilon) * gain_row


def both_norms(q_in, k_in, q_gain, k_gain):
    return (head_norm(q_in, q_gain), head_norm(k_in, k_gain))


NF_FAST = 4
NDP_FAST = 8


LANES = 128


def _to_rows(v):
    return v.reshape(-1, LANES)


def _gain_rows(gains, pick):
    flat = jnp.concatenate([pick(g).reshape(-1) for g in gains])
    pad = (-flat.shape[0]) % LANES
    return jnp.pad(flat, (0, pad)).reshape(-1, LANES)


def _plane_gather(z):
    d = lax.axis_index("dp")
    c = d % 2
    a = lax.ppermute(z, "dp", [(i, i ^ 2) for i in range(NDP_FAST)])
    b = lax.ppermute(z, "dp", [(i, i ^ 4) for i in range(NDP_FAST)])
    send = jnp.where(c == 0, b, a)
    diag = lax.ppermute(
        send, "dp", [(i, i ^ 2) if i % 2 == 0 else (i, i ^ 4) for i in range(NDP_FAST)]
    )
    mine = jnp.stack([z, a, b, diag])
    sib = lax.ppermute(mine, "dp", [(i, i ^ 1) for i in range(NDP_FAST)])
    return jnp.stack([mine[0], sib[0], mine[1], sib[1], mine[2], sib[2], mine[3], sib[3]])


def _take(x, idx, axis):
    return jnp.take(x, idx, axis=axis, mode="wrap")


def _z_gather(piece):
    f = lax.axis_index("fsdp")
    slots = [piece] + [
        lax.ppermute(piece, "fsdp", [(i, (i + k) % NF_FAST) for i in range(NF_FAST)])
        for k in range(1, NF_FAST)
    ]
    return _take(jnp.stack(slots), (f - jnp.arange(NF_FAST, dtype=jnp.int32)) % NF_FAST, 0)


def _gather_matrix(m):
    d = lax.axis_index("dp")
    j, c = d // 2, d % 2
    rows, cols = m.shape[0] // (NDP_FAST // 2), m.shape[1] // 2
    piece = lax.dynamic_slice(m, (j * rows, c * cols), (rows, cols))
    z = _z_gather(piece)
    x = lax.all_gather(z, "dp", axis=1, tiled=False)
    x = x.reshape(NF_FAST, NDP_FAST // 2, 2, rows, cols).transpose(0, 1, 3, 2, 4)
    return x.reshape(NF_FAST * m.shape[0], m.shape[1])


def fast_gather(mats, gains):
    out = [_gather_matrix(m) for m in mats]
    stacked = jnp.concatenate(gains, axis=0)
    z = _z_gather(stacked)
    full = z.transpose(1, 0, 2).reshape(stacked.shape[0], NF_FAST * stacked.shape[1])
    rows = 0
    for g in gains:
        out.append(full[rows : rows + g.shape[0]])
        rows += g.shape[0]
    return out


def _reduce_matrix(g):
    d = lax.axis_index("dp")
    f = lax.axis_index("fsdp")
    j, c = d // 2, d % 2
    n_chips = NDP_FAST // 2
    rows, cols = g.shape[0] // (NF_FAST * n_chips), g.shape[1] // 2

    def half(which):
        part = lax.dynamic_slice_in_dim(g, which * cols, cols, 1)
        return part.reshape(NF_FAST, n_chips, rows, cols)

    got = lax.ppermute(half(1 - c).astype(jnp.bfloat16), "dp", [(i, i ^ 1) for i in range(NDP_FAST)])
    chip = half(c) + got.astype(jnp.float32)

    def of_chip(k):
        return lax.dynamic_index_in_dim(chip, k, 1, keepdims=False)

    moved = lax.ppermute(
        of_chip(j ^ 3).astype(jnp.bfloat16),
        "dp",
        [(i, i ^ 2) if i % 2 == 0 else (i, i ^ 4) for i in range(NDP_FAST)],
    ).astype(jnp.float32)
    to_x = of_chip(j ^ 1) + jnp.where(c == 1, moved, 0.0)
    to_y = of_chip(j ^ 2) + jnp.where(c == 0, moved, 0.0)
    from_x = lax.ppermute(to_x.astype(jnp.bfloat16), "dp", [(i, i ^ 2) for i in range(NDP_FAST)])
    from_y = lax.ppermute(to_y.astype(jnp.bfloat16), "dp", [(i, i ^ 4) for i in range(NDP_FAST)])
    plane = of_chip(j) + from_x.astype(jnp.float32) + from_y.astype(jnp.float32)
    total = lax.dynamic_index_in_dim(plane, f, 0, keepdims=False)
    for k in range(1, NF_FAST):
        part = lax.dynamic_index_in_dim(plane, (f + k) % NF_FAST, 0, keepdims=False)
        total = total + lax.ppermute(
            part.astype(jnp.bfloat16), "fsdp", [(i, (i + k) % NF_FAST) for i in range(NF_FAST)]
        ).astype(jnp.float32)
    x = lax.all_gather(total, "dp", axis=0, tiled=False)
    x = x.reshape(n_chips, 2, rows, cols).transpose(0, 2, 1, 3)
    return x.reshape(n_chips * rows, 2 * cols)


def fast_reduce(mats, gains):
    out = [_reduce_matrix(m) for m in mats]
    stacked = lax.psum(jnp.concatenate(gains, axis=0), ("dp", "fsdp"))
    f = lax.axis_index("fsdp")
    width = stacked.shape[1] // NF_FAST
    mine = lax.dynamic_slice_in_dim(stacked, f * width, width, 1)
    rows = 0
    for g in gains:
        out.append(mine[rows : rows + g.shape[0]])
        rows += g.shape[0]
    return out


def on_device(
    fast, tokens, image_lengths, w_qkv, w_out, w_up, w_down, ln_gain, ln_bias, qk_gain, cotangent
):
    if fast:
        full_qkv, full_out, full_up, full_down, gain_all, bias_all, qk_all = fast_gather(
            (w_qkv, w_out, w_up, w_down), (ln_gain, ln_bias, qk_gain)
        )
    else:
        full_qkv, full_out, full_up, full_down, gain_all, bias_all, qk_all = (
            lax.all_gather(w_qkv, "fsdp", axis=0, tiled=True),
            lax.all_gather(w_out, "fsdp", axis=0, tiled=True),
            lax.all_gather(w_up, "fsdp", axis=0, tiled=True),
            lax.all_gather(w_down, "fsdp", axis=0, tiled=True),
            lax.all_gather(ln_gain, "fsdp", axis=1, tiled=True),
            lax.all_gather(ln_bias, "fsdp", axis=1, tiled=True),
            lax.all_gather(qk_gain, "fsdp", axis=1, tiled=True),
        )
    length = tokens.shape[0]
    model_width = tokens.shape[1]
    blocks = length // PATCH_BIG
    scaling = HEAD_DIM ** (-0.5)
    position = jnp.arange(length, dtype=jnp.int32)
    limits = jnp.cumsum(image_lengths[0])
    segment = jnp.sum((position[:, None] >= limits[None, :]).astype(jnp.int32), axis=1)
    valid_rows = (position < limits[-1]).astype(jnp.float32)[:, None]
    norm_gains = gain_all.astype(jnp.float32)
    biases = bias_all.astype(jnp.float32)
    qk_gains = qk_all.astype(jnp.float32).reshape(2, HEADS, HEAD_DIM)
    inputs = tokens.astype(jnp.float32)
    normed, first_back = jax.vjp(layer_norm, inputs, norm_gains[0], biases[0])
    normed_low = normed.astype(jnp.bfloat16)
    project = jnp.dot(normed_low, full_qkv, preferred_element_type=jnp.float32)
    queries = project[:, :model_width].reshape(length, HEADS, HEAD_DIM)
    keys_raw = project[:, model_width : 2 * model_width].reshape(length, HEADS, HEAD_DIM)
    values_raw = project[:, 2 * model_width :]
    (q_norm, k_norm), norms_back = jax.vjp(both_norms, queries, keys_raw, qk_gains[0], qk_gains[1])
    q_low = q_norm.astype(jnp.bfloat16).reshape(blocks, PATCH_BIG, HEADS, HEAD_DIM)
    k_low = k_norm.astype(jnp.bfloat16).reshape(blocks, PATCH_BIG, HEADS, HEAD_DIM)
    v_low = values_raw.astype(jnp.bfloat16).reshape(blocks, PATCH_BIG, HEADS, HEAD_DIM)
    s_blocks = segment.reshape(blocks, PATCH_BIG)

    def block_scores(q_block, k_block, s_block):
        scores = (
            jnp.einsum("qhd,khd->hqk", q_block, k_block, preferred_element_type=jnp.float32)
            * scaling
        )
        return jnp.where((s_block[:, None] == s_block[None, :])[None], scores, -1e30)

    def attend(members):
        q_block, k_block, v_block, s_block = members
        scores = block_scores(q_block, k_block, s_block)
        row_top = jnp.max(scores, axis=-1, keepdims=True)
        exp_scores = jnp.exp(scores - row_top)
        row_total = jnp.sum(exp_scores, axis=-1, keepdims=True)
        probability = (exp_scores / row_total).astype(jnp.bfloat16)
        mixed_block = jnp.einsum(
            "hqk,khd->qhd", probability, v_block, preferred_element_type=jnp.float32
        )
        return (mixed_block, row_top + jnp.log(row_total))

    mixed_heads, log_total = lax.map(attend, (q_low, k_low, v_low, s_blocks))
    mixed_low = mixed_heads.reshape(length, model_width).astype(jnp.bfloat16)
    residual = inputs + jnp.dot(mixed_low, full_out, preferred_element_type=jnp.float32)
    second, second_back = jax.vjp(layer_norm, residual, norm_gains[1], biases[1])
    second_low = second.astype(jnp.bfloat16)
    up_pre = jnp.dot(second_low, full_up, preferred_element_type=jnp.float32)
    active, gelu_back = jax.vjp(partial(jax.nn.gelu, approximate=False), up_pre)
    active_low = active.astype(jnp.bfloat16)
    output = residual + jnp.dot(active_low, full_down, preferred_element_type=jnp.float32)
    layer_out = (valid_rows * output).astype(jnp.bfloat16)
    back_qkv, back_out, back_up, back_down = full_qkv, full_out, full_up, full_down
    upstream = cotangent.astype(jnp.float32) * valid_rows
    up_low = upstream.astype(jnp.bfloat16)
    grad_down = jnp.dot(active_low.T, up_low, preferred_element_type=jnp.float32)
    grad_active = jnp.dot(up_low, back_down.T, preferred_element_type=jnp.float32)
    (grad_pre,) = gelu_back(grad_active)
    pre_low = grad_pre.astype(jnp.bfloat16)
    grad_up = jnp.dot(second_low.T, pre_low, preferred_element_type=jnp.float32)
    if fast:
        early = [_reduce_matrix(grad_up), _reduce_matrix(grad_down)]
    grad_second = jnp.dot(pre_low, back_up.T, preferred_element_type=jnp.float32)
    grad_resid, gain_two, bias_two = second_back(grad_second)
    grad_resid = grad_resid + upstream
    resid_low = grad_resid.astype(jnp.bfloat16)
    grad_outw = jnp.dot(mixed_low.T, resid_low, preferred_element_type=jnp.float32)
    grad_mixed = jnp.dot(resid_low, back_out.T, preferred_element_type=jnp.float32)
    grad_mixed = grad_mixed.astype(jnp.bfloat16).reshape(blocks, PATCH_BIG, HEADS, HEAD_DIM)

    def attend_back(members):
        q_block, k_block, v_block, s_block, l_block, d_block = members
        scores = block_scores(q_block, k_block, s_block)
        probability = jnp.exp(scores - l_block)
        prob_low = probability.astype(jnp.bfloat16)
        grad_v = jnp.einsum("hqk,qhd->khd", prob_low, d_block, preferred_element_type=jnp.float32)
        grad_p = jnp.einsum("qhd,khd->hqk", d_block, v_block, preferred_element_type=jnp.float32)
        grad_p = lax.optimization_barrier(grad_p.astype(jnp.bfloat16)).astype(jnp.float32)
        grad_s = probability * (grad_p - jnp.sum(probability * grad_p, axis=-1, keepdims=True))
        s_low = grad_s.astype(jnp.bfloat16)
        grad_q = (
            jnp.einsum("hqk,khd->qhd", s_low, k_block, preferred_element_type=jnp.float32) * scaling
        )
        grad_k = (
            jnp.einsum("hqk,qhd->khd", s_low, q_block, preferred_element_type=jnp.float32) * scaling
        )
        return (grad_q, grad_k, grad_v)

    grad_qn, grad_kn, grad_vn = lax.map(
        attend_back, (q_low, k_low, v_low, s_blocks, log_total, grad_mixed)
    )
    grad_q, grad_k, gain_q, gain_k = norms_back(
        (grad_qn.reshape(length, HEADS, HEAD_DIM), grad_kn.reshape(length, HEADS, HEAD_DIM))
    )
    grad_project = jnp.concatenate(
        [
            grad_q.reshape(length, model_width),
            grad_k.reshape(length, model_width),
            grad_vn.reshape(length, model_width),
        ],
        axis=1,
    ).astype(jnp.bfloat16)
    grad_qkv = jnp.dot(normed_low.T, grad_project, preferred_element_type=jnp.float32)
    grad_normed = jnp.dot(grad_project, back_qkv.T, preferred_element_type=jnp.float32)
    grad_input, gain_one, bias_one = first_back(grad_normed)
    grad_tokens = (grad_input + grad_resid).astype(jnp.bfloat16)
    grad_gain = jnp.stack([gain_one, gain_two])
    grad_bias = jnp.stack([bias_one, bias_two])
    grad_qk = jnp.stack([gain_q.reshape(model_width), gain_k.reshape(model_width)])
    summands = (grad_qkv, grad_outw, grad_up, grad_down, grad_gain, grad_bias, grad_qk)
    if fast:
        late = fast_reduce(summands[:2], summands[4:])
        shares = late[:2] + early + late[2:]
    else:
        pieces = [
            lax.psum_scatter(
                s.astype(jnp.bfloat16), "fsdp", scatter_dimension=0 if k < 4 else 1, tiled=True
            ).astype(jnp.float32)
            for k, s in enumerate(summands)
        ]
        shares = [lax.psum(p.astype(jnp.bfloat16), "dp").astype(jnp.float32) for p in pieces]
    return (
        layer_out,
        grad_tokens,
        shares[0],
        shares[1],
        shares[2],
        shares[3],
        shares[4],
        shares[5],
        shares[6],
    )


def solution(mesh):
    in_specs = (
        P(("dp", "fsdp"), None),
        P(("dp", "fsdp"), None),
        P("fsdp", None),
        P("fsdp", None),
        P("fsdp", None),
        P("fsdp", None),
        P(None, "fsdp"),
        P(None, "fsdp"),
        P(None, "fsdp"),
        P(("dp", "fsdp"), None),
    )
    out_specs = (
        P(("dp", "fsdp"), None),
        P(("dp", "fsdp"), None),
        P("fsdp", None),
        P("fsdp", None),
        P("fsdp", None),
        P("fsdp", None),
        P(None, "fsdp"),
        P(None, "fsdp"),
        P(None, "fsdp"),
    )
    fast = dict(mesh.shape) == {"dp": NDP_FAST, "fsdp": NF_FAST}
    return jax.shard_map(
        partial(on_device, fast), mesh=mesh, in_specs=in_specs, out_specs=out_specs, check_vma=False
    )
```

```python
from functools import partial

import jax
import jax.numpy as jnp
from jax import lax
from jax.sharding import PartitionSpec as P

HEADS = 12
HEAD_DIM = 64
PATCH_BIG = 576


epsilon = 1e-06


def layer_norm(v, gain_row, bias_row):
    centre = v - jnp.mean(v, axis=-1, keepdims=True)
    spread = jnp.mean(centre * centre, axis=-1, keepdims=True)
    return centre * lax.rsqrt(spread + epsilon) * gain_row + bias_row


def head_norm(v, gain_row):
    centre = v - jnp.mean(v, axis=-1, keepdims=True)
    spread = jnp.mean(centre * centre, axis=-1, keepdims=True)
    return centre * lax.rsqrt(spread + epsilon) * gain_row


def both_norms(q_in, k_in, q_gain, k_gain):
    return (head_norm(q_in, q_gain), head_norm(k_in, k_gain))


NF_FAST = 4
NDP_FAST = 8


LANES = 128


def _to_rows(v):
    return v.reshape(-1, LANES)


def _gain_rows(gains, pick):
    flat = jnp.concatenate([pick(g).reshape(-1) for g in gains])
    pad = (-flat.shape[0]) % LANES
    return jnp.pad(flat, (0, pad)).reshape(-1, LANES)


def _plane_gather(z):
    d = lax.axis_index("dp")
    c = d % 2
    a = lax.ppermute(z, "dp", [(i, i ^ 2) for i in range(NDP_FAST)])
    b = lax.ppermute(z, "dp", [(i, i ^ 4) for i in range(NDP_FAST)])
    send = jnp.where(c == 0, b, a)
    diag = lax.ppermute(
        send, "dp", [(i, i ^ 2) if i % 2 == 0 else (i, i ^ 4) for i in range(NDP_FAST)]
    )
    mine = jnp.stack([z, a, b, diag])
    sib = lax.ppermute(mine, "dp", [(i, i ^ 1) for i in range(NDP_FAST)])
    return jnp.stack([mine[0], sib[0], mine[1], sib[1], mine[2], sib[2], mine[3], sib[3]])


def _take(x, idx, axis):
    return jnp.take(x, idx, axis=axis, mode="wrap")


def _z_gather(piece):
    f = lax.axis_index("fsdp")
    slots = [piece] + [
        lax.ppermute(piece, "fsdp", [(i, (i + k) % NF_FAST) for i in range(NF_FAST)])
        for k in range(1, NF_FAST)
    ]
    return _take(jnp.stack(slots), (f - jnp.arange(NF_FAST, dtype=jnp.int32)) % NF_FAST, 0)


def _gather_full(z, rows, cols, out_rows):
    x = lax.all_gather(z, "dp", axis=1, tiled=False)
    x = x.reshape(NF_FAST, NDP_FAST // 2, 2, rows, cols).transpose(0, 1, 3, 2, 4)
    return x.reshape(out_rows, 2 * cols)


def fast_gather(mats, gains):
    d = lax.axis_index("dp")
    j, c = d // 2, d % 2
    n_chips = NDP_FAST // 2
    height = mats[0].shape[0] // n_chips
    blocks, shapes = [], []
    for m in mats:
        rows, cols = m.shape[0] // n_chips, m.shape[1] // 2
        piece = lax.dynamic_slice(m, (j * rows, c * cols), (rows, cols))
        shapes.append((rows, cols))
        blocks.append(piece.reshape(height, rows * cols // height))
    stacked = jnp.concatenate(gains, axis=0)
    flat = stacked.reshape(-1)
    blocks.append(jnp.pad(flat, (0, height * LANES - flat.shape[0])).reshape(height, LANES))
    z = _z_gather(jnp.concatenate(blocks, axis=1))
    out = []
    offset = 0
    for m, (rows, cols) in zip(mats, shapes):
        width = rows * cols // height
        part = z[:, :, offset : offset + width].reshape(NF_FAST, rows, cols)
        out.append(_gather_full(part, rows, cols, NF_FAST * m.shape[0]))
        offset += width
    g = z[:, :, offset:].reshape(NF_FAST, -1)[:, : flat.shape[0]]
    g = g.reshape(NF_FAST, stacked.shape[0], stacked.shape[1]).transpose(1, 0, 2)
    g = g.reshape(stacked.shape[0], NF_FAST * stacked.shape[1])
    row = 0
    for gain in gains:
        out.append(g[row : row + gain.shape[0]])
        row += gain.shape[0]
    return out


def _reduce_matrix(g):
    d = lax.axis_index("dp")
    f = lax.axis_index("fsdp")
    j, c = d // 2, d % 2
    n_chips = NDP_FAST // 2
    rows, cols = g.shape[0] // (NF_FAST * n_chips), g.shape[1] // 2

    def half(which):
        part = lax.dynamic_slice_in_dim(g, which * cols, cols, 1)
        return part.reshape(NF_FAST, n_chips, rows, cols)

    got = lax.ppermute(half(1 - c).astype(jnp.bfloat16), "dp", [(i, i ^ 1) for i in range(NDP_FAST)])
    chip = half(c) + got.astype(jnp.float32)

    def of_chip(k):
        return lax.dynamic_index_in_dim(chip, k, 1, keepdims=False)

    moved = lax.ppermute(
        of_chip(j ^ 3).astype(jnp.bfloat16),
        "dp",
        [(i, i ^ 2) if i % 2 == 0 else (i, i ^ 4) for i in range(NDP_FAST)],
    ).astype(jnp.float32)
    to_x = of_chip(j ^ 1) + jnp.where(c == 1, moved, 0.0)
    to_y = of_chip(j ^ 2) + jnp.where(c == 0, moved, 0.0)
    from_x = lax.ppermute(to_x.astype(jnp.bfloat16), "dp", [(i, i ^ 2) for i in range(NDP_FAST)])
    from_y = lax.ppermute(to_y.astype(jnp.bfloat16), "dp", [(i, i ^ 4) for i in range(NDP_FAST)])
    plane = of_chip(j) + from_x.astype(jnp.float32) + from_y.astype(jnp.float32)
    total = lax.dynamic_index_in_dim(plane, f, 0, keepdims=False)
    for k in range(1, NF_FAST):
        part = lax.dynamic_index_in_dim(plane, (f + k) % NF_FAST, 0, keepdims=False)
        total = total + lax.ppermute(
            part.astype(jnp.bfloat16), "fsdp", [(i, (i + k) % NF_FAST) for i in range(NF_FAST)]
        ).astype(jnp.float32)
    x = lax.all_gather(total, "dp", axis=0, tiled=False)
    x = x.reshape(n_chips, 2, rows, cols).transpose(0, 2, 1, 3)
    return x.reshape(n_chips * rows, 2 * cols)


def fast_reduce(mats, gains):
    stacked = jnp.concatenate(gains, axis=0)
    pad = 2 * LANES - stacked.shape[0]
    first = jnp.concatenate([mats[0], jnp.pad(stacked.T, ((0, 0), (0, pad)))], axis=1)
    shard = _reduce_matrix(first)
    width = mats[0].shape[1]
    out = [shard[:, :width]] + [_reduce_matrix(m) for m in mats[1:]]
    mine = shard[:, width : width + stacked.shape[0]].T
    rows = 0
    for g in gains:
        out.append(mine[rows : rows + g.shape[0]])
        rows += g.shape[0]
    return out


def on_device(
    fast, tokens, image_lengths, w_qkv, w_out, w_up, w_down, ln_gain, ln_bias, qk_gain, cotangent
):
    if fast:
        full_qkv, full_out, full_up, full_down, gain_all, bias_all, qk_all = fast_gather(
            (w_qkv, w_out, w_up, w_down), (ln_gain, ln_bias, qk_gain)
        )
    else:
        full_qkv, full_out, full_up, full_down, gain_all, bias_all, qk_all = (
            lax.all_gather(w_qkv, "fsdp", axis=0, tiled=True),
            lax.all_gather(w_out, "fsdp", axis=0, tiled=True),
            lax.all_gather(w_up, "fsdp", axis=0, tiled=True),
            lax.all_gather(w_down, "fsdp", axis=0, tiled=True),
            lax.all_gather(ln_gain, "fsdp", axis=1, tiled=True),
            lax.all_gather(ln_bias, "fsdp", axis=1, tiled=True),
            lax.all_gather(qk_gain, "fsdp", axis=1, tiled=True),
        )
    length = tokens.shape[0]
    model_width = tokens.shape[1]
    blocks = length // PATCH_BIG
    scaling = HEAD_DIM ** (-0.5)
    position = jnp.arange(length, dtype=jnp.int32)
    limits = jnp.cumsum(image_lengths[0])
    segment = jnp.sum((position[:, None] >= limits[None, :]).astype(jnp.int32), axis=1)
    valid_rows = (position < limits[-1]).astype(jnp.float32)[:, None]
    norm_gains = gain_all.astype(jnp.float32)
    biases = bias_all.astype(jnp.float32)
    qk_gains = qk_all.astype(jnp.float32).reshape(2, HEADS, HEAD_DIM)
    inputs = tokens.astype(jnp.float32)
    normed, first_back = jax.vjp(layer_norm, inputs, norm_gains[0], biases[0])
    normed_low = normed.astype(jnp.bfloat16)
    project = jnp.dot(normed_low, full_qkv, preferred_element_type=jnp.float32)
    queries = project[:, :model_width].reshape(length, HEADS, HEAD_DIM)
    keys_raw = project[:, model_width : 2 * model_width].reshape(length, HEADS, HEAD_DIM)
    values_raw = project[:, 2 * model_width :]
    (q_norm, k_norm), norms_back = jax.vjp(both_norms, queries, keys_raw, qk_gains[0], qk_gains[1])
    q_low = q_norm.astype(jnp.bfloat16).reshape(blocks, PATCH_BIG, HEADS, HEAD_DIM)
    k_low = k_norm.astype(jnp.bfloat16).reshape(blocks, PATCH_BIG, HEADS, HEAD_DIM)
    v_low = values_raw.astype(jnp.bfloat16).reshape(blocks, PATCH_BIG, HEADS, HEAD_DIM)
    s_blocks = segment.reshape(blocks, PATCH_BIG)

    def block_scores(q_block, k_block, s_block):
        scores = (
            jnp.einsum("qhd,khd->hqk", q_block, k_block, preferred_element_type=jnp.float32)
            * scaling
        )
        return jnp.where((s_block[:, None] == s_block[None, :])[None], scores, -1e30)

    def attend(members):
        q_block, k_block, v_block, s_block = members
        scores = block_scores(q_block, k_block, s_block)
        row_top = jnp.max(scores, axis=-1, keepdims=True)
        exp_scores = jnp.exp(scores - row_top)
        row_total = jnp.sum(exp_scores, axis=-1, keepdims=True)
        probability = (exp_scores / row_total).astype(jnp.bfloat16)
        mixed_block = jnp.einsum(
            "hqk,khd->qhd", probability, v_block, preferred_element_type=jnp.float32
        )
        return (mixed_block, row_top + jnp.log(row_total))

    mixed_heads, log_total = lax.map(attend, (q_low, k_low, v_low, s_blocks))
    mixed_low = mixed_heads.reshape(length, model_width).astype(jnp.bfloat16)
    residual = inputs + jnp.dot(mixed_low, full_out, preferred_element_type=jnp.float32)
    second, second_back = jax.vjp(layer_norm, residual, norm_gains[1], biases[1])
    second_low = second.astype(jnp.bfloat16)
    up_pre = jnp.dot(second_low, full_up, preferred_element_type=jnp.float32)
    active, gelu_back = jax.vjp(partial(jax.nn.gelu, approximate=False), up_pre)
    active_low = active.astype(jnp.bfloat16)
    output = residual + jnp.dot(active_low, full_down, preferred_element_type=jnp.float32)
    layer_out = (valid_rows * output).astype(jnp.bfloat16)
    back_qkv, back_out, back_up, back_down = full_qkv, full_out, full_up, full_down
    upstream = cotangent.astype(jnp.float32) * valid_rows
    up_low = upstream.astype(jnp.bfloat16)
    grad_down = jnp.dot(active_low.T, up_low, preferred_element_type=jnp.float32)
    grad_active = jnp.dot(up_low, back_down.T, preferred_element_type=jnp.float32)
    (grad_pre,) = gelu_back(grad_active)
    pre_low = grad_pre.astype(jnp.bfloat16)
    grad_up = jnp.dot(second_low.T, pre_low, preferred_element_type=jnp.float32)
    if fast:
        early = [_reduce_matrix(grad_up), _reduce_matrix(grad_down)]
    grad_second = jnp.dot(pre_low, back_up.T, preferred_element_type=jnp.float32)
    grad_resid, gain_two, bias_two = second_back(grad_second)
    grad_resid = grad_resid + upstream
    resid_low = grad_resid.astype(jnp.bfloat16)
    grad_outw = jnp.dot(mixed_low.T, resid_low, preferred_element_type=jnp.float32)
    grad_mixed = jnp.dot(resid_low, back_out.T, preferred_element_type=jnp.float32)
    grad_mixed = grad_mixed.astype(jnp.bfloat16).reshape(blocks, PATCH_BIG, HEADS, HEAD_DIM)

    def attend_back(members):
        q_block, k_block, v_block, s_block, l_block, d_block = members
        scores = block_scores(q_block, k_block, s_block)
        probability = jnp.exp(scores - l_block)
        prob_low = probability.astype(jnp.bfloat16)
        grad_v = jnp.einsum("hqk,qhd->khd", prob_low, d_block, preferred_element_type=jnp.float32)
        grad_p = jnp.einsum("qhd,khd->hqk", d_block, v_block, preferred_element_type=jnp.float32)
        grad_p = lax.optimization_barrier(grad_p.astype(jnp.bfloat16)).astype(jnp.float32)
        grad_s = probability * (grad_p - jnp.sum(probability * grad_p, axis=-1, keepdims=True))
        s_low = grad_s.astype(jnp.bfloat16)
        grad_q = (
            jnp.einsum("hqk,khd->qhd", s_low, k_block, preferred_element_type=jnp.float32) * scaling
        )
        grad_k = (
            jnp.einsum("hqk,qhd->khd", s_low, q_block, preferred_element_type=jnp.float32) * scaling
        )
        return (grad_q, grad_k, grad_v)

    grad_qn, grad_kn, grad_vn = lax.map(
        attend_back, (q_low, k_low, v_low, s_blocks, log_total, grad_mixed)
    )
    grad_q, grad_k, gain_q, gain_k = norms_back(
        (grad_qn.reshape(length, HEADS, HEAD_DIM), grad_kn.reshape(length, HEADS, HEAD_DIM))
    )
    grad_project = jnp.concatenate(
        [
            grad_q.reshape(length, model_width),
            grad_k.reshape(length, model_width),
            grad_vn.reshape(length, model_width),
        ],
        axis=1,
    ).astype(jnp.bfloat16)
    grad_qkv = jnp.dot(normed_low.T, grad_project, preferred_element_type=jnp.float32)
    grad_normed = jnp.dot(grad_project, back_qkv.T, preferred_element_type=jnp.float32)
    grad_input, gain_one, bias_one = first_back(grad_normed)
    grad_tokens = (grad_input + grad_resid).astype(jnp.bfloat16)
    grad_gain = jnp.stack([gain_one, gain_two])
    grad_bias = jnp.stack([bias_one, bias_two])
    grad_qk = jnp.stack([gain_q.reshape(model_width), gain_k.reshape(model_width)])
    summands = (grad_qkv, grad_outw, grad_up, grad_down, grad_gain, grad_bias, grad_qk)
    if fast:
        late = fast_reduce(summands[:2], summands[4:])
        shares = late[:2] + early + late[2:]
    else:
        pieces = [
            lax.psum_scatter(
                s.astype(jnp.bfloat16), "fsdp", scatter_dimension=0 if k < 4 else 1, tiled=True
            ).astype(jnp.float32)
            for k, s in enumerate(summands)
        ]
        shares = [lax.psum(p.astype(jnp.bfloat16), "dp").astype(jnp.float32) for p in pieces]
    return (
        layer_out,
        grad_tokens,
        shares[0],
        shares[1],
        shares[2],
        shares[3],
        shares[4],
        shares[5],
        shares[6],
    )


def solution(mesh):
    in_specs = (
        P(("dp", "fsdp"), None),
        P(("dp", "fsdp"), None),
        P("fsdp", None),
        P("fsdp", None),
        P("fsdp", None),
        P("fsdp", None),
        P(None, "fsdp"),
        P(None, "fsdp"),
        P(None, "fsdp"),
        P(("dp", "fsdp"), None),
    )
    out_specs = (
        P(("dp", "fsdp"), None),
        P(("dp", "fsdp"), None),
        P("fsdp", None),
        P("fsdp", None),
        P("fsdp", None),
        P("fsdp", None),
        P(None, "fsdp"),
        P(None, "fsdp"),
        P(None, "fsdp"),
    )
    fast = dict(mesh.shape) == {"dp": NDP_FAST, "fsdp": NF_FAST}
    return jax.shard_map(
        partial(on_device, fast), mesh=mesh, in_specs=in_specs, out_specs=out_specs, check_vma=False
    )
```

```python
from functools import partial

import jax
import jax.numpy as jnp
from jax import lax
from jax.sharding import PartitionSpec as P

HEADS = 12
HEAD_DIM = 64
PATCH_BIG = 576


epsilon = 1e-06


def layer_norm(v, gain_row, bias_row):
    centre = v - jnp.mean(v, axis=-1, keepdims=True)
    spread = jnp.mean(centre * centre, axis=-1, keepdims=True)
    return centre * lax.rsqrt(spread + epsilon) * gain_row + bias_row


def head_norm(v, gain_row):
    centre = v - jnp.mean(v, axis=-1, keepdims=True)
    spread = jnp.mean(centre * centre, axis=-1, keepdims=True)
    return centre * lax.rsqrt(spread + epsilon) * gain_row


def both_norms(q_in, k_in, q_gain, k_gain):
    return (head_norm(q_in, q_gain), head_norm(k_in, k_gain))


NF_FAST = 4
NDP_FAST = 8


LANES = 128


def _to_rows(v):
    return v.reshape(-1, LANES)


def _gain_rows(gains, pick):
    flat = jnp.concatenate([pick(g).reshape(-1) for g in gains])
    pad = (-flat.shape[0]) % LANES
    return jnp.pad(flat, (0, pad)).reshape(-1, LANES)


def _plane_gather(z):
    d = lax.axis_index("dp")
    c = d % 2
    a = lax.ppermute(z, "dp", [(i, i ^ 2) for i in range(NDP_FAST)])
    b = lax.ppermute(z, "dp", [(i, i ^ 4) for i in range(NDP_FAST)])
    send = jnp.where(c == 0, b, a)
    diag = lax.ppermute(
        send, "dp", [(i, i ^ 2) if i % 2 == 0 else (i, i ^ 4) for i in range(NDP_FAST)]
    )
    mine = jnp.stack([z, a, b, diag])
    sib = lax.ppermute(mine, "dp", [(i, i ^ 1) for i in range(NDP_FAST)])
    return jnp.stack([mine[0], sib[0], mine[1], sib[1], mine[2], sib[2], mine[3], sib[3]])


def _take(x, idx, axis):
    return jnp.take(x, idx, axis=axis, mode="wrap")


def _z_gather(piece):
    f = lax.axis_index("fsdp")
    slots = [piece] + [
        lax.ppermute(piece, "fsdp", [(i, (i + k) % NF_FAST) for i in range(NF_FAST)])
        for k in range(1, NF_FAST)
    ]
    return _take(jnp.stack(slots), (f - jnp.arange(NF_FAST, dtype=jnp.int32)) % NF_FAST, 0)


def _gather_full(z, rows, cols, out_rows):
    x = lax.all_gather(z, "dp", axis=1, tiled=False)
    x = x.reshape(NF_FAST, NDP_FAST // 2, 2, rows, cols).transpose(0, 1, 3, 2, 4)
    return x.reshape(out_rows, 2 * cols)


def _gather_group(mats, gains):
    d = lax.axis_index("dp")
    j, c = d // 2, d % 2
    n_chips = NDP_FAST // 2
    height = mats[0].shape[0] // n_chips
    blocks, shapes = [], []
    for m in mats:
        rows, cols = m.shape[0] // n_chips, m.shape[1] // 2
        piece = lax.dynamic_slice(m, (j * rows, c * cols), (rows, cols))
        shapes.append((rows, cols))
        blocks.append(piece.reshape(height, rows * cols // height))
    if gains:
        stacked = jnp.concatenate(gains, axis=0)
        flat = stacked.reshape(-1)
        blocks.append(jnp.pad(flat, (0, height * LANES - flat.shape[0])).reshape(height, LANES))
    z = _z_gather(jnp.concatenate(blocks, axis=1) if len(blocks) > 1 else blocks[0])
    out = []
    offset = 0
    for m, (rows, cols) in zip(mats, shapes):
        width = rows * cols // height
        part = z[:, :, offset : offset + width].reshape(NF_FAST, rows, cols)
        out.append(_gather_full(part, rows, cols, NF_FAST * m.shape[0]))
        offset += width
    if gains:
        g = z[:, :, offset:].reshape(NF_FAST, -1)[:, : flat.shape[0]]
        g = g.reshape(NF_FAST, stacked.shape[0], stacked.shape[1]).transpose(1, 0, 2)
        g = g.reshape(stacked.shape[0], NF_FAST * stacked.shape[1])
        row = 0
        for gain in gains:
            out.append(g[row : row + gain.shape[0]])
            row += gain.shape[0]
    return out


def fast_gather(mats, gains):
    return _gather_group(mats[:1], ()) + _gather_group(mats[1:], gains)


def _reduce_matrix(g):
    d = lax.axis_index("dp")
    f = lax.axis_index("fsdp")
    j, c = d // 2, d % 2
    n_chips = NDP_FAST // 2
    rows, cols = g.shape[0] // (NF_FAST * n_chips), g.shape[1] // 2

    def half(which):
        part = lax.dynamic_slice_in_dim(g, which * cols, cols, 1)
        return part.reshape(NF_FAST, n_chips, rows, cols)

    got = lax.ppermute(half(1 - c).astype(jnp.bfloat16), "dp", [(i, i ^ 1) for i in range(NDP_FAST)])
    chip = half(c) + got.astype(jnp.float32)

    def of_chip(k):
        return lax.dynamic_index_in_dim(chip, k, 1, keepdims=False)

    moved = lax.ppermute(
        of_chip(j ^ 3).astype(jnp.bfloat16),
        "dp",
        [(i, i ^ 2) if i % 2 == 0 else (i, i ^ 4) for i in range(NDP_FAST)],
    ).astype(jnp.float32)
    to_x = of_chip(j ^ 1) + jnp.where(c == 1, moved, 0.0)
    to_y = of_chip(j ^ 2) + jnp.where(c == 0, moved, 0.0)
    from_x = lax.ppermute(to_x.astype(jnp.bfloat16), "dp", [(i, i ^ 2) for i in range(NDP_FAST)])
    from_y = lax.ppermute(to_y.astype(jnp.bfloat16), "dp", [(i, i ^ 4) for i in range(NDP_FAST)])
    plane = of_chip(j) + from_x.astype(jnp.float32) + from_y.astype(jnp.float32)
    total = lax.dynamic_index_in_dim(plane, f, 0, keepdims=False)
    for k in range(1, NF_FAST):
        part = lax.dynamic_index_in_dim(plane, (f + k) % NF_FAST, 0, keepdims=False)
        total = total + lax.ppermute(
            part.astype(jnp.bfloat16), "fsdp", [(i, (i + k) % NF_FAST) for i in range(NF_FAST)]
        ).astype(jnp.float32)
    x = lax.all_gather(total, "dp", axis=0, tiled=False)
    x = x.reshape(n_chips, 2, rows, cols).transpose(0, 2, 1, 3)
    return x.reshape(n_chips * rows, 2 * cols)


def fast_reduce(mats, gains):
    stacked = jnp.concatenate(gains, axis=0)
    pad = 2 * LANES - stacked.shape[0]
    first = jnp.concatenate([mats[0], jnp.pad(stacked.T, ((0, 0), (0, pad)))], axis=1)
    shard = _reduce_matrix(first)
    width = mats[0].shape[1]
    out = [shard[:, :width]] + [_reduce_matrix(m) for m in mats[1:]]
    mine = shard[:, width : width + stacked.shape[0]].T
    rows = 0
    for g in gains:
        out.append(mine[rows : rows + g.shape[0]])
        rows += g.shape[0]
    return out


def map_blocks(fn, members):
    if members[0].shape[0] == 1:
        return jax.tree.map(lambda v: v[None], fn(tuple(m[0] for m in members)))
    return lax.map(fn, members)


def on_device(
    fast, tokens, image_lengths, w_qkv, w_out, w_up, w_down, ln_gain, ln_bias, qk_gain, cotangent
):
    if fast:
        full_qkv, full_out, full_up, full_down, gain_all, bias_all, qk_all = fast_gather(
            (w_qkv, w_out, w_up, w_down), (ln_gain, ln_bias, qk_gain)
        )
    else:
        full_qkv, full_out, full_up, full_down, gain_all, bias_all, qk_all = (
            lax.all_gather(w_qkv, "fsdp", axis=0, tiled=True),
            lax.all_gather(w_out, "fsdp", axis=0, tiled=True),
            lax.all_gather(w_up, "fsdp", axis=0, tiled=True),
            lax.all_gather(w_down, "fsdp", axis=0, tiled=True),
            lax.all_gather(ln_gain, "fsdp", axis=1, tiled=True),
            lax.all_gather(ln_bias, "fsdp", axis=1, tiled=True),
            lax.all_gather(qk_gain, "fsdp", axis=1, tiled=True),
        )
    length = tokens.shape[0]
    model_width = tokens.shape[1]
    blocks = length // PATCH_BIG
    scaling = HEAD_DIM ** (-0.5)
    position = jnp.arange(length, dtype=jnp.int32)
    limits = jnp.cumsum(image_lengths[0])
    segment = jnp.sum((position[:, None] >= limits[None, :]).astype(jnp.int32), axis=1)
    valid_rows = (position < limits[-1]).astype(jnp.float32)[:, None]
    norm_gains = gain_all.astype(jnp.float32)
    biases = bias_all.astype(jnp.float32)
    qk_gains = qk_all.astype(jnp.float32).reshape(2, HEADS, HEAD_DIM)
    inputs = tokens.astype(jnp.float32)
    normed, first_back = jax.vjp(layer_norm, inputs, norm_gains[0], biases[0])
    normed_low = normed.astype(jnp.bfloat16)
    project = jnp.dot(normed_low, full_qkv, preferred_element_type=jnp.float32)
    queries = project[:, :model_width].reshape(length, HEADS, HEAD_DIM)
    keys_raw = project[:, model_width : 2 * model_width].reshape(length, HEADS, HEAD_DIM)
    values_raw = project[:, 2 * model_width :]
    (q_norm, k_norm), norms_back = jax.vjp(both_norms, queries, keys_raw, qk_gains[0], qk_gains[1])
    q_low = q_norm.astype(jnp.bfloat16).reshape(blocks, PATCH_BIG, HEADS, HEAD_DIM)
    k_low = k_norm.astype(jnp.bfloat16).reshape(blocks, PATCH_BIG, HEADS, HEAD_DIM)
    v_low = values_raw.astype(jnp.bfloat16).reshape(blocks, PATCH_BIG, HEADS, HEAD_DIM)
    s_blocks = segment.reshape(blocks, PATCH_BIG)

    def block_scores(q_block, k_block, s_block):
        scores = (
            jnp.einsum("qhd,khd->hqk", q_block, k_block, preferred_element_type=jnp.float32)
            * scaling
        )
        return jnp.where((s_block[:, None] == s_block[None, :])[None], scores, -1e30)

    def attend(members):
        q_block, k_block, v_block, s_block = members
        scores = block_scores(q_block, k_block, s_block)
        row_top = jnp.max(scores, axis=-1, keepdims=True)
        exp_scores = jnp.exp(scores - row_top)
        row_total = jnp.sum(exp_scores, axis=-1, keepdims=True)
        probability = (exp_scores / row_total).astype(jnp.bfloat16)
        mixed_block = jnp.einsum(
            "hqk,khd->qhd", probability, v_block, preferred_element_type=jnp.float32
        )
        return (mixed_block, row_top + jnp.log(row_total))

    mixed_heads, log_total = map_blocks(attend, (q_low, k_low, v_low, s_blocks))
    mixed_low = mixed_heads.reshape(length, model_width).astype(jnp.bfloat16)
    residual = inputs + jnp.dot(mixed_low, full_out, preferred_element_type=jnp.float32)
    second, second_back = jax.vjp(layer_norm, residual, norm_gains[1], biases[1])
    second_low = second.astype(jnp.bfloat16)
    up_pre = jnp.dot(second_low, full_up, preferred_element_type=jnp.float32)
    active, gelu_back = jax.vjp(partial(jax.nn.gelu, approximate=False), up_pre)
    active_low = active.astype(jnp.bfloat16)
    output = residual + jnp.dot(active_low, full_down, preferred_element_type=jnp.float32)
    layer_out = (valid_rows * output).astype(jnp.bfloat16)
    back_qkv, back_out, back_up, back_down = full_qkv, full_out, full_up, full_down
    upstream = cotangent.astype(jnp.float32) * valid_rows
    up_low = upstream.astype(jnp.bfloat16)
    grad_down = jnp.dot(active_low.T, up_low, preferred_element_type=jnp.float32)
    grad_active = jnp.dot(up_low, back_down.T, preferred_element_type=jnp.float32)
    (grad_pre,) = gelu_back(grad_active)
    pre_low = grad_pre.astype(jnp.bfloat16)
    grad_up = jnp.dot(second_low.T, pre_low, preferred_element_type=jnp.float32)
    if fast:
        early = [_reduce_matrix(grad_up), _reduce_matrix(grad_down)]
    grad_second = jnp.dot(pre_low, back_up.T, preferred_element_type=jnp.float32)
    grad_resid, gain_two, bias_two = second_back(grad_second)
    grad_resid = grad_resid + upstream
    resid_low = grad_resid.astype(jnp.bfloat16)
    grad_outw = jnp.dot(mixed_low.T, resid_low, preferred_element_type=jnp.float32)
    if fast:
        early = [_reduce_matrix(grad_outw)] + early
    grad_mixed = jnp.dot(resid_low, back_out.T, preferred_element_type=jnp.float32)
    grad_mixed = grad_mixed.astype(jnp.bfloat16).reshape(blocks, PATCH_BIG, HEADS, HEAD_DIM)

    def attend_back(members):
        q_block, k_block, v_block, s_block, l_block, d_block = members
        scores = block_scores(q_block, k_block, s_block)
        probability = jnp.exp(scores - l_block)
        prob_low = probability.astype(jnp.bfloat16)
        grad_v = jnp.einsum("hqk,qhd->khd", prob_low, d_block, preferred_element_type=jnp.float32)
        grad_p = jnp.einsum("qhd,khd->hqk", d_block, v_block, preferred_element_type=jnp.float32)
        grad_p = lax.optimization_barrier(grad_p.astype(jnp.bfloat16)).astype(jnp.float32)
        grad_s = probability * (grad_p - jnp.sum(probability * grad_p, axis=-1, keepdims=True))
        s_low = grad_s.astype(jnp.bfloat16)
        grad_q = (
            jnp.einsum("hqk,khd->qhd", s_low, k_block, preferred_element_type=jnp.float32) * scaling
        )
        grad_k = (
            jnp.einsum("hqk,qhd->khd", s_low, q_block, preferred_element_type=jnp.float32) * scaling
        )
        return (grad_q, grad_k, grad_v)

    grad_qn, grad_kn, grad_vn = map_blocks(
        attend_back, (q_low, k_low, v_low, s_blocks, log_total, grad_mixed)
    )
    if fast:
        early, grad_qn, grad_kn, grad_vn = lax.optimization_barrier(
            (early, grad_qn, grad_kn, grad_vn)
        )
    grad_q, grad_k, gain_q, gain_k = norms_back(
        (grad_qn.reshape(length, HEADS, HEAD_DIM), grad_kn.reshape(length, HEADS, HEAD_DIM))
    )
    grad_project = jnp.concatenate(
        [
            grad_q.reshape(length, model_width),
            grad_k.reshape(length, model_width),
            grad_vn.reshape(length, model_width),
        ],
        axis=1,
    ).astype(jnp.bfloat16)
    grad_qkv = jnp.dot(normed_low.T, grad_project, preferred_element_type=jnp.float32)
    grad_normed = jnp.dot(grad_project, back_qkv.T, preferred_element_type=jnp.float32)
    grad_input, gain_one, bias_one = first_back(grad_normed)
    grad_tokens = (grad_input + grad_resid).astype(jnp.bfloat16)
    grad_gain = jnp.stack([gain_one, gain_two])
    grad_bias = jnp.stack([bias_one, bias_two])
    grad_qk = jnp.stack([gain_q.reshape(model_width), gain_k.reshape(model_width)])
    summands = (grad_qkv, grad_outw, grad_up, grad_down, grad_gain, grad_bias, grad_qk)
    if fast:
        late = fast_reduce(summands[:1], summands[4:])
        shares = late[:1] + early + late[1:]
    else:
        pieces = [
            lax.psum_scatter(
                s.astype(jnp.bfloat16), "fsdp", scatter_dimension=0 if k < 4 else 1, tiled=True
            ).astype(jnp.float32)
            for k, s in enumerate(summands)
        ]
        shares = [lax.psum(p.astype(jnp.bfloat16), "dp").astype(jnp.float32) for p in pieces]
    return (
        layer_out,
        grad_tokens,
        shares[0],
        shares[1],
        shares[2],
        shares[3],
        shares[4],
        shares[5],
        shares[6],
    )


def solution(mesh):
    in_specs = (
        P(("dp", "fsdp"), None),
        P(("dp", "fsdp"), None),
        P("fsdp", None),
        P("fsdp", None),
        P("fsdp", None),
        P("fsdp", None),
        P(None, "fsdp"),
        P(None, "fsdp"),
        P(None, "fsdp"),
        P(("dp", "fsdp"), None),
    )
    out_specs = (
        P(("dp", "fsdp"), None),
        P(("dp", "fsdp"), None),
        P("fsdp", None),
        P("fsdp", None),
        P("fsdp", None),
        P("fsdp", None),
        P(None, "fsdp"),
        P(None, "fsdp"),
        P(None, "fsdp"),
    )
    fast = dict(mesh.shape) == {"dp": NDP_FAST, "fsdp": NF_FAST}
    return jax.shard_map(
        partial(on_device, fast), mesh=mesh, in_specs=in_specs, out_specs=out_specs, check_vma=False
    )
```

```python
from functools import partial

import jax
import jax.numpy as jnp
from jax import lax
from jax.sharding import PartitionSpec as P

HEADS = 12
HEAD_DIM = 64
PATCH_BIG = 576


epsilon = 1e-06


def layer_norm(v, gain_row, bias_row):
    centre = v - jnp.mean(v, axis=-1, keepdims=True)
    spread = jnp.mean(centre * centre, axis=-1, keepdims=True)
    return centre * lax.rsqrt(spread + epsilon) * gain_row + bias_row


def head_norm(v, gain_row):
    centre = v - jnp.mean(v, axis=-1, keepdims=True)
    spread = jnp.mean(centre * centre, axis=-1, keepdims=True)
    return centre * lax.rsqrt(spread + epsilon) * gain_row


def both_norms(q_in, k_in, q_gain, k_gain):
    return (head_norm(q_in, q_gain), head_norm(k_in, k_gain))


NF_FAST = 4
NDP_FAST = 8


LANES = 128


def _to_rows(v):
    return v.reshape(-1, LANES)


def _gain_rows(gains, pick):
    flat = jnp.concatenate([pick(g).reshape(-1) for g in gains])
    pad = (-flat.shape[0]) % LANES
    return jnp.pad(flat, (0, pad)).reshape(-1, LANES)


def _plane_gather(z):
    d = lax.axis_index("dp")
    c = d % 2
    a = lax.ppermute(z, "dp", [(i, i ^ 2) for i in range(NDP_FAST)])
    b = lax.ppermute(z, "dp", [(i, i ^ 4) for i in range(NDP_FAST)])
    send = jnp.where(c == 0, b, a)
    diag = lax.ppermute(
        send, "dp", [(i, i ^ 2) if i % 2 == 0 else (i, i ^ 4) for i in range(NDP_FAST)]
    )
    mine = jnp.stack([z, a, b, diag])
    sib = lax.ppermute(mine, "dp", [(i, i ^ 1) for i in range(NDP_FAST)])
    return jnp.stack([mine[0], sib[0], mine[1], sib[1], mine[2], sib[2], mine[3], sib[3]])


def _take(x, idx, axis):
    return jnp.take(x, idx, axis=axis, mode="wrap")


def _z_gather(piece):
    f = lax.axis_index("fsdp")
    slots = [piece] + [
        lax.ppermute(piece, "fsdp", [(i, (i + k) % NF_FAST) for i in range(NF_FAST)])
        for k in range(1, NF_FAST)
    ]
    return _take(jnp.stack(slots), (f - jnp.arange(NF_FAST, dtype=jnp.int32)) % NF_FAST, 0)


def _gather_matrix(m):
    d = lax.axis_index("dp")
    j, c = d // 2, d % 2
    rows, cols = m.shape[0] // (NDP_FAST // 2), m.shape[1] // 2
    piece = lax.dynamic_slice(m, (j * rows, c * cols), (rows, cols))
    z = _z_gather(piece)
    x = lax.all_gather(z, "dp", axis=1, tiled=False)
    x = x.reshape(NF_FAST, NDP_FAST // 2, 2, rows, cols).transpose(0, 1, 3, 2, 4)
    return x.reshape(NF_FAST * m.shape[0], m.shape[1])


def fast_gather(mats, gains):
    out = [_gather_matrix(m) for m in mats]
    stacked = jnp.concatenate(gains, axis=0)
    z = _z_gather(stacked)
    full = z.transpose(1, 0, 2).reshape(stacked.shape[0], NF_FAST * stacked.shape[1])
    rows = 0
    for g in gains:
        out.append(full[rows : rows + g.shape[0]])
        rows += g.shape[0]
    return out


def _reduce_matrix(g):
    d = lax.axis_index("dp")
    f = lax.axis_index("fsdp")
    j, c = d // 2, d % 2
    n_chips = NDP_FAST // 2
    rows, cols = g.shape[0] // (NF_FAST * n_chips), g.shape[1] // 2

    def half(which):
        part = lax.dynamic_slice_in_dim(g, which * cols, cols, 1)
        return part.reshape(NF_FAST, n_chips, rows, cols)

    got = lax.ppermute(half(1 - c).astype(jnp.bfloat16), "dp", [(i, i ^ 1) for i in range(NDP_FAST)])
    chip = half(c) + got.astype(jnp.float32)

    def of_chip(k):
        return lax.dynamic_index_in_dim(chip, k, 1, keepdims=False)

    moved = lax.ppermute(
        of_chip(j ^ 3).astype(jnp.bfloat16),
        "dp",
        [(i, i ^ 2) if i % 2 == 0 else (i, i ^ 4) for i in range(NDP_FAST)],
    ).astype(jnp.float32)
    to_x = of_chip(j ^ 1) + jnp.where(c == 1, moved, 0.0)
    to_y = of_chip(j ^ 2) + jnp.where(c == 0, moved, 0.0)
    from_x = lax.ppermute(to_x.astype(jnp.bfloat16), "dp", [(i, i ^ 2) for i in range(NDP_FAST)])
    from_y = lax.ppermute(to_y.astype(jnp.bfloat16), "dp", [(i, i ^ 4) for i in range(NDP_FAST)])
    plane = of_chip(j) + from_x.astype(jnp.float32) + from_y.astype(jnp.float32)
    total = lax.dynamic_index_in_dim(plane, f, 0, keepdims=False)
    for k in range(1, NF_FAST):
        part = lax.dynamic_index_in_dim(plane, (f + k) % NF_FAST, 0, keepdims=False)
        total = total + lax.ppermute(
            part.astype(jnp.bfloat16), "fsdp", [(i, (i + k) % NF_FAST) for i in range(NF_FAST)]
        ).astype(jnp.float32)
    x = lax.all_gather(total, "dp", axis=0, tiled=False)
    x = x.reshape(n_chips, 2, rows, cols).transpose(0, 2, 1, 3)
    return x.reshape(n_chips * rows, 2 * cols)


def fast_reduce(mats, gains):
    stacked = jnp.concatenate(gains, axis=0)
    pad = 2 * LANES - stacked.shape[0]
    first = jnp.concatenate([mats[0], jnp.pad(stacked.T, ((0, 0), (0, pad)))], axis=1)
    shard = _reduce_matrix(first)
    width = mats[0].shape[1]
    out = [shard[:, :width]] + [_reduce_matrix(m) for m in mats[1:]]
    mine = shard[:, width : width + stacked.shape[0]].T
    rows = 0
    for g in gains:
        out.append(mine[rows : rows + g.shape[0]])
        rows += g.shape[0]
    return out


def on_device(
    fast, tokens, image_lengths, w_qkv, w_out, w_up, w_down, ln_gain, ln_bias, qk_gain, cotangent
):
    if fast:
        full_qkv, full_out, full_up, full_down, gain_all, bias_all, qk_all = fast_gather(
            (w_qkv, w_out, w_up, w_down), (ln_gain, ln_bias, qk_gain)
        )
    else:
        full_qkv, full_out, full_up, full_down, gain_all, bias_all, qk_all = (
            lax.all_gather(w_qkv, "fsdp", axis=0, tiled=True),
            lax.all_gather(w_out, "fsdp", axis=0, tiled=True),
            lax.all_gather(w_up, "fsdp", axis=0, tiled=True),
            lax.all_gather(w_down, "fsdp", axis=0, tiled=True),
            lax.all_gather(ln_gain, "fsdp", axis=1, tiled=True),
            lax.all_gather(ln_bias, "fsdp", axis=1, tiled=True),
            lax.all_gather(qk_gain, "fsdp", axis=1, tiled=True),
        )
    length = tokens.shape[0]
    model_width = tokens.shape[1]
    blocks = length // PATCH_BIG
    scaling = HEAD_DIM ** (-0.5)
    position = jnp.arange(length, dtype=jnp.int32)
    limits = jnp.cumsum(image_lengths[0])
    segment = jnp.sum((position[:, None] >= limits[None, :]).astype(jnp.int32), axis=1)
    valid_rows = (position < limits[-1]).astype(jnp.float32)[:, None]
    norm_gains = gain_all.astype(jnp.float32)
    biases = bias_all.astype(jnp.float32)
    qk_gains = qk_all.astype(jnp.float32).reshape(2, HEADS, HEAD_DIM)
    inputs = tokens.astype(jnp.float32)
    normed, first_back = jax.vjp(layer_norm, inputs, norm_gains[0], biases[0])
    normed_low = normed.astype(jnp.bfloat16)
    project = jnp.dot(normed_low, full_qkv, preferred_element_type=jnp.float32)
    queries = project[:, :model_width].reshape(length, HEADS, HEAD_DIM)
    keys_raw = project[:, model_width : 2 * model_width].reshape(length, HEADS, HEAD_DIM)
    values_raw = project[:, 2 * model_width :]
    (q_norm, k_norm), norms_back = jax.vjp(both_norms, queries, keys_raw, qk_gains[0], qk_gains[1])
    q_low = q_norm.astype(jnp.bfloat16).reshape(blocks, PATCH_BIG, HEADS, HEAD_DIM)
    k_low = k_norm.astype(jnp.bfloat16).reshape(blocks, PATCH_BIG, HEADS, HEAD_DIM)
    v_low = values_raw.astype(jnp.bfloat16).reshape(blocks, PATCH_BIG, HEADS, HEAD_DIM)
    s_blocks = segment.reshape(blocks, PATCH_BIG)

    def block_scores(q_block, k_block, s_block):
        scores = (
            jnp.einsum("qhd,khd->hqk", q_block, k_block, preferred_element_type=jnp.float32)
            * scaling
        )
        return jnp.where((s_block[:, None] == s_block[None, :])[None], scores, -1e30)

    def attend(members):
        q_block, k_block, v_block, s_block = members
        scores = block_scores(q_block, k_block, s_block)
        row_top = jnp.max(scores, axis=-1, keepdims=True)
        exp_scores = jnp.exp(scores - row_top)
        row_total = jnp.sum(exp_scores, axis=-1, keepdims=True)
        probability = (exp_scores / row_total).astype(jnp.bfloat16)
        mixed_block = jnp.einsum(
            "hqk,khd->qhd", probability, v_block, preferred_element_type=jnp.float32
        )
        return (mixed_block, row_top + jnp.log(row_total))

    mixed_heads, log_total = lax.map(attend, (q_low, k_low, v_low, s_blocks))
    mixed_low = mixed_heads.reshape(length, model_width).astype(jnp.bfloat16)
    residual = inputs + jnp.dot(mixed_low, full_out, preferred_element_type=jnp.float32)
    second, second_back = jax.vjp(layer_norm, residual, norm_gains[1], biases[1])
    second_low = second.astype(jnp.bfloat16)
    up_pre = jnp.dot(second_low, full_up, preferred_element_type=jnp.float32)
    active, gelu_back = jax.vjp(partial(jax.nn.gelu, approximate=False), up_pre)
    active_low = active.astype(jnp.bfloat16)
    output = residual + jnp.dot(active_low, full_down, preferred_element_type=jnp.float32)
    layer_out = (valid_rows * output).astype(jnp.bfloat16)
    back_qkv, back_out, back_up, back_down = full_qkv, full_out, full_up, full_down
    upstream = cotangent.astype(jnp.float32) * valid_rows
    up_low = upstream.astype(jnp.bfloat16)
    grad_down = jnp.dot(active_low.T, up_low, preferred_element_type=jnp.float32)
    grad_active = jnp.dot(up_low, back_down.T, preferred_element_type=jnp.float32)
    (grad_pre,) = gelu_back(grad_active)
    pre_low = grad_pre.astype(jnp.bfloat16)
    grad_up = jnp.dot(second_low.T, pre_low, preferred_element_type=jnp.float32)
    if fast:
        early = [_reduce_matrix(grad_up), _reduce_matrix(grad_down)]
    grad_second = jnp.dot(pre_low, back_up.T, preferred_element_type=jnp.float32)
    grad_resid, gain_two, bias_two = second_back(grad_second)
    grad_resid = grad_resid + upstream
    resid_low = grad_resid.astype(jnp.bfloat16)
    grad_outw = jnp.dot(mixed_low.T, resid_low, preferred_element_type=jnp.float32)
    grad_mixed = jnp.dot(resid_low, back_out.T, preferred_element_type=jnp.float32)
    grad_mixed = grad_mixed.astype(jnp.bfloat16).reshape(blocks, PATCH_BIG, HEADS, HEAD_DIM)

    def attend_back(members):
        q_block, k_block, v_block, s_block, l_block, d_block = members
        scores = block_scores(q_block, k_block, s_block)
        probability = jnp.exp(scores - l_block)
        prob_low = probability.astype(jnp.bfloat16)
        grad_v = jnp.einsum("hqk,qhd->khd", prob_low, d_block, preferred_element_type=jnp.float32)
        grad_p = jnp.einsum("qhd,khd->hqk", d_block, v_block, preferred_element_type=jnp.float32)
        grad_p = lax.optimization_barrier(grad_p.astype(jnp.bfloat16)).astype(jnp.float32)
        grad_s = probability * (grad_p - jnp.sum(probability * grad_p, axis=-1, keepdims=True))
        s_low = grad_s.astype(jnp.bfloat16)
        grad_q = (
            jnp.einsum("hqk,khd->qhd", s_low, k_block, preferred_element_type=jnp.float32) * scaling
        )
        grad_k = (
            jnp.einsum("hqk,qhd->khd", s_low, q_block, preferred_element_type=jnp.float32) * scaling
        )
        return (grad_q, grad_k, grad_v)

    grad_qn, grad_kn, grad_vn = lax.map(
        attend_back, (q_low, k_low, v_low, s_blocks, log_total, grad_mixed)
    )
    grad_q, grad_k, gain_q, gain_k = norms_back(
        (grad_qn.reshape(length, HEADS, HEAD_DIM), grad_kn.reshape(length, HEADS, HEAD_DIM))
    )
    grad_project = jnp.concatenate(
        [
            grad_q.reshape(length, model_width),
            grad_k.reshape(length, model_width),
            grad_vn.reshape(length, model_width),
        ],
        axis=1,
    ).astype(jnp.bfloat16)
    grad_qkv = jnp.dot(normed_low.T, grad_project, preferred_element_type=jnp.float32)
    grad_normed = jnp.dot(grad_project, back_qkv.T, preferred_element_type=jnp.float32)
    grad_input, gain_one, bias_one = first_back(grad_normed)
    grad_tokens = (grad_input + grad_resid).astype(jnp.bfloat16)
    grad_gain = jnp.stack([gain_one, gain_two])
    grad_bias = jnp.stack([bias_one, bias_two])
    grad_qk = jnp.stack([gain_q.reshape(model_width), gain_k.reshape(model_width)])
    summands = (grad_qkv, grad_outw, grad_up, grad_down, grad_gain, grad_bias, grad_qk)
    if fast:
        late = fast_reduce(summands[:2], summands[4:])
        shares = late[:2] + early + late[2:]
    else:
        pieces = [
            lax.psum_scatter(
                s.astype(jnp.bfloat16), "fsdp", scatter_dimension=0 if k < 4 else 1, tiled=True
            ).astype(jnp.float32)
            for k, s in enumerate(summands)
        ]
        shares = [lax.psum(p.astype(jnp.bfloat16), "dp").astype(jnp.float32) for p in pieces]
    return (
        layer_out,
        grad_tokens,
        shares[0],
        shares[1],
        shares[2],
        shares[3],
        shares[4],
        shares[5],
        shares[6],
    )


def solution(mesh):
    in_specs = (
        P(("dp", "fsdp"), None),
        P(("dp", "fsdp"), None),
        P("fsdp", None),
        P("fsdp", None),
        P("fsdp", None),
        P("fsdp", None),
        P(None, "fsdp"),
        P(None, "fsdp"),
        P(None, "fsdp"),
        P(("dp", "fsdp"), None),
    )
    out_specs = (
        P(("dp", "fsdp"), None),
        P(("dp", "fsdp"), None),
        P("fsdp", None),
        P("fsdp", None),
        P("fsdp", None),
        P("fsdp", None),
        P(None, "fsdp"),
        P(None, "fsdp"),
        P(None, "fsdp"),
    )
    fast = dict(mesh.shape) == {"dp": NDP_FAST, "fsdp": NF_FAST}
    return jax.shard_map(
        partial(on_device, fast), mesh=mesh, in_specs=in_specs, out_specs=out_specs, check_vma=False
    )
```

```python
from functools import partial

import jax
import jax.numpy as jnp
from jax import lax
from jax.sharding import PartitionSpec as P

HEADS = 12
HEAD_DIM = 64
PATCH_BIG = 576


epsilon = 1e-06


def layer_norm(v, gain_row, bias_row):
    centre = v - jnp.mean(v, axis=-1, keepdims=True)
    spread = jnp.mean(centre * centre, axis=-1, keepdims=True)
    return centre * lax.rsqrt(spread + epsilon) * gain_row + bias_row


def head_norm(v, gain_row):
    centre = v - jnp.mean(v, axis=-1, keepdims=True)
    spread = jnp.mean(centre * centre, axis=-1, keepdims=True)
    return centre * lax.rsqrt(spread + epsilon) * gain_row


def both_norms(q_in, k_in, q_gain, k_gain):
    return (head_norm(q_in, q_gain), head_norm(k_in, k_gain))


NF_FAST = 4
NDP_FAST = 8


LANES = 128


def _to_rows(v):
    return v.reshape(-1, LANES)


def _gain_rows(gains, pick):
    flat = jnp.concatenate([pick(g).reshape(-1) for g in gains])
    pad = (-flat.shape[0]) % LANES
    return jnp.pad(flat, (0, pad)).reshape(-1, LANES)


def _plane_gather(z):
    d = lax.axis_index("dp")
    c = d % 2
    a = lax.ppermute(z, "dp", [(i, i ^ 2) for i in range(NDP_FAST)])
    b = lax.ppermute(z, "dp", [(i, i ^ 4) for i in range(NDP_FAST)])
    send = jnp.where(c == 0, b, a)
    diag = lax.ppermute(
        send, "dp", [(i, i ^ 2) if i % 2 == 0 else (i, i ^ 4) for i in range(NDP_FAST)]
    )
    mine = jnp.stack([z, a, b, diag])
    sib = lax.ppermute(mine, "dp", [(i, i ^ 1) for i in range(NDP_FAST)])
    return jnp.stack([mine[0], sib[0], mine[1], sib[1], mine[2], sib[2], mine[3], sib[3]])


def _take(x, idx, axis):
    return jnp.take(x, idx, axis=axis, mode="wrap")


def _z_gather(piece):
    f = lax.axis_index("fsdp")
    slots = [piece] + [
        lax.ppermute(piece, "fsdp", [(i, (i + k) % NF_FAST) for i in range(NF_FAST)])
        for k in range(1, NF_FAST)
    ]
    return _take(jnp.stack(slots), (f - jnp.arange(NF_FAST, dtype=jnp.int32)) % NF_FAST, 0)


def _gather_matrix(m):
    d = lax.axis_index("dp")
    j, c = d // 2, d % 2
    rows, cols = m.shape[0] // (NDP_FAST // 2), m.shape[1] // 2
    piece = lax.dynamic_slice(m, (j * rows, c * cols), (rows, cols))
    z = _z_gather(piece)
    x = lax.all_gather(z, "dp", axis=1, tiled=False)
    x = x.reshape(NF_FAST, NDP_FAST // 2, 2, rows, cols)
    x = jnp.concatenate([x[:, :, 0], x[:, :, 1]], axis=-1)
    return x.reshape(NF_FAST * m.shape[0], m.shape[1])


def fast_gather(mats, gains):
    out = [_gather_matrix(m) for m in mats]
    stacked = jnp.concatenate(gains, axis=0)
    z = _z_gather(stacked)
    full = z.transpose(1, 0, 2).reshape(stacked.shape[0], NF_FAST * stacked.shape[1])
    rows = 0
    for g in gains:
        out.append(full[rows : rows + g.shape[0]])
        rows += g.shape[0]
    return out


def _reduce_matrix(g):
    d = lax.axis_index("dp")
    f = lax.axis_index("fsdp")
    j, c = d // 2, d % 2
    n_chips = NDP_FAST // 2
    rows, cols = g.shape[0] // (NF_FAST * n_chips), g.shape[1] // 2

    def half(which):
        part = lax.dynamic_slice_in_dim(g, which * cols, cols, 1)
        return part.reshape(NF_FAST, n_chips, rows, cols)

    got = lax.ppermute(half(1 - c).astype(jnp.bfloat16), "dp", [(i, i ^ 1) for i in range(NDP_FAST)])
    chip = half(c) + got.astype(jnp.float32)

    def of_chip(k):
        return lax.dynamic_index_in_dim(chip, k, 1, keepdims=False)

    moved = lax.ppermute(
        of_chip(j ^ 3).astype(jnp.bfloat16),
        "dp",
        [(i, i ^ 2) if i % 2 == 0 else (i, i ^ 4) for i in range(NDP_FAST)],
    ).astype(jnp.float32)
    to_x = of_chip(j ^ 1) + jnp.where(c == 1, moved, 0.0)
    to_y = of_chip(j ^ 2) + jnp.where(c == 0, moved, 0.0)
    from_x = lax.ppermute(to_x.astype(jnp.bfloat16), "dp", [(i, i ^ 2) for i in range(NDP_FAST)])
    from_y = lax.ppermute(to_y.astype(jnp.bfloat16), "dp", [(i, i ^ 4) for i in range(NDP_FAST)])
    plane = of_chip(j) + from_x.astype(jnp.float32) + from_y.astype(jnp.float32)
    total = lax.dynamic_index_in_dim(plane, f, 0, keepdims=False)
    for k in range(1, NF_FAST):
        part = lax.dynamic_index_in_dim(plane, (f + k) % NF_FAST, 0, keepdims=False)
        total = total + lax.ppermute(
            part.astype(jnp.bfloat16), "fsdp", [(i, (i + k) % NF_FAST) for i in range(NF_FAST)]
        ).astype(jnp.float32)
    x = lax.all_gather(total, "dp", axis=0, tiled=False)
    x = x.reshape(n_chips, 2, rows, cols)
    x = jnp.concatenate([x[:, 0], x[:, 1]], axis=-1)
    return x.reshape(n_chips * rows, 2 * cols)


def fast_reduce(mats, gains):
    stacked = jnp.concatenate(gains, axis=0)
    pad = 2 * LANES - stacked.shape[0]
    first = jnp.concatenate([mats[0], jnp.pad(stacked.T, ((0, 0), (0, pad)))], axis=1)
    shard = _reduce_matrix(first)
    width = mats[0].shape[1]
    out = [shard[:, :width]] + [_reduce_matrix(m) for m in mats[1:]]
    mine = shard[:, width : width + stacked.shape[0]].T
    rows = 0
    for g in gains:
        out.append(mine[rows : rows + g.shape[0]])
        rows += g.shape[0]
    return out


def on_device(
    fast, tokens, image_lengths, w_qkv, w_out, w_up, w_down, ln_gain, ln_bias, qk_gain, cotangent
):
    if fast:
        full_qkv, full_out, full_up, full_down, gain_all, bias_all, qk_all = fast_gather(
            (w_qkv, w_out, w_up, w_down), (ln_gain, ln_bias, qk_gain)
        )
    else:
        full_qkv, full_out, full_up, full_down, gain_all, bias_all, qk_all = (
            lax.all_gather(w_qkv, "fsdp", axis=0, tiled=True),
            lax.all_gather(w_out, "fsdp", axis=0, tiled=True),
            lax.all_gather(w_up, "fsdp", axis=0, tiled=True),
            lax.all_gather(w_down, "fsdp", axis=0, tiled=True),
            lax.all_gather(ln_gain, "fsdp", axis=1, tiled=True),
            lax.all_gather(ln_bias, "fsdp", axis=1, tiled=True),
            lax.all_gather(qk_gain, "fsdp", axis=1, tiled=True),
        )
    length = tokens.shape[0]
    model_width = tokens.shape[1]
    blocks = length // PATCH_BIG
    scaling = HEAD_DIM ** (-0.5)
    position = jnp.arange(length, dtype=jnp.int32)
    limits = jnp.cumsum(image_lengths[0])
    segment = jnp.sum((position[:, None] >= limits[None, :]).astype(jnp.int32), axis=1)
    valid_rows = (position < limits[-1]).astype(jnp.float32)[:, None]
    norm_gains = gain_all.astype(jnp.float32)
    biases = bias_all.astype(jnp.float32)
    qk_gains = qk_all.astype(jnp.float32).reshape(2, HEADS, HEAD_DIM)
    inputs = tokens.astype(jnp.float32)
    normed, first_back = jax.vjp(layer_norm, inputs, norm_gains[0], biases[0])
    normed_low = normed.astype(jnp.bfloat16)
    project = jnp.dot(normed_low, full_qkv, preferred_element_type=jnp.float32)
    queries = project[:, :model_width].reshape(length, HEADS, HEAD_DIM)
    keys_raw = project[:, model_width : 2 * model_width].reshape(length, HEADS, HEAD_DIM)
    values_raw = project[:, 2 * model_width :]
    (q_norm, k_norm), norms_back = jax.vjp(both_norms, queries, keys_raw, qk_gains[0], qk_gains[1])
    q_low = q_norm.astype(jnp.bfloat16).reshape(blocks, PATCH_BIG, HEADS, HEAD_DIM)
    k_low = k_norm.astype(jnp.bfloat16).reshape(blocks, PATCH_BIG, HEADS, HEAD_DIM)
    v_low = values_raw.astype(jnp.bfloat16).reshape(blocks, PATCH_BIG, HEADS, HEAD_DIM)
    s_blocks = segment.reshape(blocks, PATCH_BIG)

    def block_scores(q_block, k_block, s_block):
        scores = (
            jnp.einsum("qhd,khd->hqk", q_block, k_block, preferred_element_type=jnp.float32)
            * scaling
        )
        return jnp.where((s_block[:, None] == s_block[None, :])[None], scores, -1e30)

    def attend(members):
        q_block, k_block, v_block, s_block = members
        scores = block_scores(q_block, k_block, s_block)
        row_top = jnp.max(scores, axis=-1, keepdims=True)
        exp_scores = jnp.exp(scores - row_top)
        row_total = jnp.sum(exp_scores, axis=-1, keepdims=True)
        probability = (exp_scores / row_total).astype(jnp.bfloat16)
        mixed_block = jnp.einsum(
            "hqk,khd->qhd", probability, v_block, preferred_element_type=jnp.float32
        )
        return (mixed_block, row_top + jnp.log(row_total))

    mixed_heads, log_total = lax.map(attend, (q_low, k_low, v_low, s_blocks))
    mixed_low = mixed_heads.reshape(length, model_width).astype(jnp.bfloat16)
    residual = inputs + jnp.dot(mixed_low, full_out, preferred_element_type=jnp.float32)
    second, second_back = jax.vjp(layer_norm, residual, norm_gains[1], biases[1])
    second_low = second.astype(jnp.bfloat16)
    up_pre = jnp.dot(second_low, full_up, preferred_element_type=jnp.float32)
    active, gelu_back = jax.vjp(partial(jax.nn.gelu, approximate=False), up_pre)
    active_low = active.astype(jnp.bfloat16)
    output = residual + jnp.dot(active_low, full_down, preferred_element_type=jnp.float32)
    layer_out = (valid_rows * output).astype(jnp.bfloat16)
    back_qkv, back_out, back_up, back_down = full_qkv, full_out, full_up, full_down
    upstream = cotangent.astype(jnp.float32) * valid_rows
    up_low = upstream.astype(jnp.bfloat16)
    grad_down = jnp.dot(active_low.T, up_low, preferred_element_type=jnp.float32)
    grad_active = jnp.dot(up_low, back_down.T, preferred_element_type=jnp.float32)
    (grad_pre,) = gelu_back(grad_active)
    pre_low = grad_pre.astype(jnp.bfloat16)
    grad_up = jnp.dot(second_low.T, pre_low, preferred_element_type=jnp.float32)
    if fast:
        early = [_reduce_matrix(grad_up), _reduce_matrix(grad_down)]
    grad_second = jnp.dot(pre_low, back_up.T, preferred_element_type=jnp.float32)
    grad_resid, gain_two, bias_two = second_back(grad_second)
    grad_resid = grad_resid + upstream
    resid_low = grad_resid.astype(jnp.bfloat16)
    grad_outw = jnp.dot(mixed_low.T, resid_low, preferred_element_type=jnp.float32)
    grad_mixed = jnp.dot(resid_low, back_out.T, preferred_element_type=jnp.float32)
    grad_mixed = grad_mixed.astype(jnp.bfloat16).reshape(blocks, PATCH_BIG, HEADS, HEAD_DIM)

    def attend_back(members):
        q_block, k_block, v_block, s_block, l_block, d_block = members
        scores = block_scores(q_block, k_block, s_block)
        probability = jnp.exp(scores - l_block)
        prob_low = probability.astype(jnp.bfloat16)
        grad_v = jnp.einsum("hqk,qhd->khd", prob_low, d_block, preferred_element_type=jnp.float32)
        grad_p = jnp.einsum("qhd,khd->hqk", d_block, v_block, preferred_element_type=jnp.float32)
        grad_p = lax.optimization_barrier(grad_p.astype(jnp.bfloat16)).astype(jnp.float32)
        grad_s = probability * (grad_p - jnp.sum(probability * grad_p, axis=-1, keepdims=True))
        s_low = grad_s.astype(jnp.bfloat16)
        grad_q = (
            jnp.einsum("hqk,khd->qhd", s_low, k_block, preferred_element_type=jnp.float32) * scaling
        )
        grad_k = (
            jnp.einsum("hqk,qhd->khd", s_low, q_block, preferred_element_type=jnp.float32) * scaling
        )
        return (grad_q, grad_k, grad_v)

    grad_qn, grad_kn, grad_vn = lax.map(
        attend_back, (q_low, k_low, v_low, s_blocks, log_total, grad_mixed)
    )
    grad_q, grad_k, gain_q, gain_k = norms_back(
        (grad_qn.reshape(length, HEADS, HEAD_DIM), grad_kn.reshape(length, HEADS, HEAD_DIM))
    )
    grad_project = jnp.concatenate(
        [
            grad_q.reshape(length, model_width),
            grad_k.reshape(length, model_width),
            grad_vn.reshape(length, model_width),
        ],
        axis=1,
    ).astype(jnp.bfloat16)
    grad_qkv = jnp.dot(normed_low.T, grad_project, preferred_element_type=jnp.float32)
    grad_normed = jnp.dot(grad_project, back_qkv.T, preferred_element_type=jnp.float32)
    grad_input, gain_one, bias_one = first_back(grad_normed)
    grad_tokens = (grad_input + grad_resid).astype(jnp.bfloat16)
    grad_gain = jnp.stack([gain_one, gain_two])
    grad_bias = jnp.stack([bias_one, bias_two])
    grad_qk = jnp.stack([gain_q.reshape(model_width), gain_k.reshape(model_width)])
    summands = (grad_qkv, grad_outw, grad_up, grad_down, grad_gain, grad_bias, grad_qk)
    if fast:
        late = fast_reduce(summands[:2], summands[4:])
        shares = late[:2] + early + late[2:]
    else:
        pieces = [
            lax.psum_scatter(
                s.astype(jnp.bfloat16), "fsdp", scatter_dimension=0 if k < 4 else 1, tiled=True
            ).astype(jnp.float32)
            for k, s in enumerate(summands)
        ]
        shares = [lax.psum(p.astype(jnp.bfloat16), "dp").astype(jnp.float32) for p in pieces]
    return (
        layer_out,
        grad_tokens,
        shares[0],
        shares[1],
        shares[2],
        shares[3],
        shares[4],
        shares[5],
        shares[6],
    )


def solution(mesh):
    in_specs = (
        P(("dp", "fsdp"), None),
        P(("dp", "fsdp"), None),
        P("fsdp", None),
        P("fsdp", None),
        P("fsdp", None),
        P("fsdp", None),
        P(None, "fsdp"),
        P(None, "fsdp"),
        P(None, "fsdp"),
        P(("dp", "fsdp"), None),
    )
    out_specs = (
        P(("dp", "fsdp"), None),
        P(("dp", "fsdp"), None),
        P("fsdp", None),
        P("fsdp", None),
        P("fsdp", None),
        P("fsdp", None),
        P(None, "fsdp"),
        P(None, "fsdp"),
        P(None, "fsdp"),
    )
    fast = dict(mesh.shape) == {"dp": NDP_FAST, "fsdp": NF_FAST}
    return jax.shard_map(
        partial(on_device, fast), mesh=mesh, in_specs=in_specs, out_specs=out_specs, check_vma=False
    )
```

```python
from functools import partial

import jax
import jax.numpy as jnp
from jax import lax
from jax.sharding import PartitionSpec as P


HEADS = 12
HEAD_DIM = 64
PATCH_BIG = 576


epsilon = 1e-06


def layer_norm(v, gain_row, bias_row):
    centre = v - jnp.mean(v, axis=-1, keepdims=True)
    spread = jnp.mean(centre * centre, axis=-1, keepdims=True)
    return centre * lax.rsqrt(spread + epsilon) * gain_row + bias_row


def head_norm(v, gain_row):
    centre = v - jnp.mean(v, axis=-1, keepdims=True)
    spread = jnp.mean(centre * centre, axis=-1, keepdims=True)
    return centre * lax.rsqrt(spread + epsilon) * gain_row


def both_norms(q_in, k_in, q_gain, k_gain):
    return (head_norm(q_in, q_gain), head_norm(k_in, k_gain))


NF_FAST = 4
NDP_FAST = 8


LANES = 128


def _take(x, idx, axis):
    return jnp.take(x, idx, axis=axis, mode="wrap")


def _z_gather(piece):
    f = lax.axis_index("fsdp")
    slots = [piece] + [
        lax.ppermute(piece, "fsdp", [(i, (i + k) % NF_FAST) for i in range(NF_FAST)])
        for k in range(1, NF_FAST)
    ]
    return _take(jnp.stack(slots), (f - jnp.arange(NF_FAST, dtype=jnp.int32)) % NF_FAST, 0)


def _gather_matrix(m):
    d = lax.axis_index("dp")
    j, c = d // 2, d % 2
    rows, cols = m.shape[0] // (NDP_FAST // 2), m.shape[1] // 2
    piece = lax.dynamic_slice(m, (j * rows, c * cols), (rows, cols))
    z = _z_gather(piece)
    x = lax.all_gather(z, "dp", axis=1, tiled=False)
    x = x.reshape(NF_FAST, NDP_FAST // 2, 2, rows, cols)
    x = jnp.concatenate([x[:, :, 0], x[:, :, 1]], axis=-1)
    return x.reshape(NF_FAST * m.shape[0], m.shape[1])


def fast_gather(mats, gains):
    out = [_gather_matrix(m) for m in mats]
    stacked = jnp.concatenate(gains, axis=0)
    z = _z_gather(stacked)
    full = z.transpose(1, 0, 2).reshape(stacked.shape[0], NF_FAST * stacked.shape[1])
    rows = 0
    for g in gains:
        out.append(full[rows : rows + g.shape[0]])
        rows += g.shape[0]
    return out


def _reduce_matrix(g):
    d = lax.axis_index("dp")
    f = lax.axis_index("fsdp")
    j, c = d // 2, d % 2
    n_chips = NDP_FAST // 2
    rows, cols = g.shape[0] // (NF_FAST * n_chips), g.shape[1] // 2

    def half(which):
        part = lax.dynamic_slice_in_dim(g, which * cols, cols, 1)
        return part.reshape(NF_FAST, n_chips, rows, cols)

    got = lax.ppermute(half(1 - c).astype(jnp.bfloat16), "dp", [(i, i ^ 1) for i in range(NDP_FAST)])
    chip = half(c) + got.astype(jnp.float32)

    def of_chip(k):
        return lax.dynamic_index_in_dim(chip, k, 1, keepdims=False)

    moved = lax.ppermute(
        of_chip(j ^ 3).astype(jnp.bfloat16),
        "dp",
        [(i, i ^ 2) if i % 2 == 0 else (i, i ^ 4) for i in range(NDP_FAST)],
    ).astype(jnp.float32)
    to_x = of_chip(j ^ 1) + jnp.where(c == 1, moved, 0.0)
    to_y = of_chip(j ^ 2) + jnp.where(c == 0, moved, 0.0)
    from_x = lax.ppermute(to_x.astype(jnp.bfloat16), "dp", [(i, i ^ 2) for i in range(NDP_FAST)])
    from_y = lax.ppermute(to_y.astype(jnp.bfloat16), "dp", [(i, i ^ 4) for i in range(NDP_FAST)])
    plane = of_chip(j) + from_x.astype(jnp.float32) + from_y.astype(jnp.float32)
    total = lax.dynamic_index_in_dim(plane, f, 0, keepdims=False)
    for k in range(1, NF_FAST):
        part = lax.dynamic_index_in_dim(plane, (f + k) % NF_FAST, 0, keepdims=False)
        total = total + lax.ppermute(
            part.astype(jnp.bfloat16), "fsdp", [(i, (i + k) % NF_FAST) for i in range(NF_FAST)]
        ).astype(jnp.float32)
    x = lax.all_gather(total, "dp", axis=0, tiled=False)
    x = x.reshape(n_chips, 2, rows, cols)
    x = jnp.concatenate([x[:, 0], x[:, 1]], axis=-1)
    return x.reshape(n_chips * rows, 2 * cols)


def fast_reduce(mats, gains):
    stacked = jnp.concatenate(gains, axis=0)
    pad = 2 * LANES - stacked.shape[0]
    first = jnp.concatenate([mats[0], jnp.pad(stacked.T, ((0, 0), (0, pad)))], axis=1)
    shard = _reduce_matrix(first)
    width = mats[0].shape[1]
    out = [shard[:, :width]] + [_reduce_matrix(m) for m in mats[1:]]
    mine = shard[:, width : width + stacked.shape[0]].T
    rows = 0
    for g in gains:
        out.append(mine[rows : rows + g.shape[0]])
        rows += g.shape[0]
    return out


def map_blocks(fn, members):
    if members[0].shape[0] == 1:
        return jax.tree.map(lambda v: v[None], fn(tuple(m[0] for m in members)))
    return lax.map(fn, members)


def on_device(fast, *args):
    return layer(fast, *args)


def layer(
    fast, tokens, image_lengths, w_qkv, w_out, w_up, w_down, ln_gain, ln_bias, qk_gain, cotangent
):
    if fast:
        full_qkv, full_out, full_up, full_down, gain_all, bias_all, qk_all = fast_gather(
            (w_qkv, w_out, w_up, w_down), (ln_gain, ln_bias, qk_gain)
        )
    else:
        full_qkv, full_out, full_up, full_down, gain_all, bias_all, qk_all = (
            lax.all_gather(w_qkv, "fsdp", axis=0, tiled=True),
            lax.all_gather(w_out, "fsdp", axis=0, tiled=True),
            lax.all_gather(w_up, "fsdp", axis=0, tiled=True),
            lax.all_gather(w_down, "fsdp", axis=0, tiled=True),
            lax.all_gather(ln_gain, "fsdp", axis=1, tiled=True),
            lax.all_gather(ln_bias, "fsdp", axis=1, tiled=True),
            lax.all_gather(qk_gain, "fsdp", axis=1, tiled=True),
        )
    length = tokens.shape[0]
    model_width = tokens.shape[1]
    blocks = length // PATCH_BIG
    scaling = HEAD_DIM ** (-0.5)
    position = jnp.arange(length, dtype=jnp.int32)
    limits = jnp.cumsum(image_lengths[0])
    segment = jnp.sum((position[:, None] >= limits[None, :]).astype(jnp.int32), axis=1)
    valid_rows = (position < limits[-1]).astype(jnp.float32)[:, None]
    norm_gains = gain_all.astype(jnp.float32)
    biases = bias_all.astype(jnp.float32)
    qk_gains = qk_all.astype(jnp.float32).reshape(2, HEADS, HEAD_DIM)
    inputs = tokens.astype(jnp.float32)
    normed, first_back = jax.vjp(layer_norm, inputs, norm_gains[0], biases[0])
    normed_low = normed.astype(jnp.bfloat16)
    project = jnp.dot(normed_low, full_qkv, preferred_element_type=jnp.float32)
    queries = project[:, :model_width].reshape(length, HEADS, HEAD_DIM)
    keys_raw = project[:, model_width : 2 * model_width].reshape(length, HEADS, HEAD_DIM)
    values_raw = project[:, 2 * model_width :]
    (q_norm, k_norm), norms_back = jax.vjp(both_norms, queries, keys_raw, qk_gains[0], qk_gains[1])
    q_low = q_norm.astype(jnp.bfloat16).reshape(blocks, PATCH_BIG, HEADS, HEAD_DIM)
    k_low = k_norm.astype(jnp.bfloat16).reshape(blocks, PATCH_BIG, HEADS, HEAD_DIM)
    v_low = values_raw.astype(jnp.bfloat16).reshape(blocks, PATCH_BIG, HEADS, HEAD_DIM)
    s_blocks = segment.reshape(blocks, PATCH_BIG)

    def block_scores(q_block, k_block, s_block):
        scores = (
            jnp.einsum("qhd,khd->hqk", q_block, k_block, preferred_element_type=jnp.float32)
            * scaling
        )
        return jnp.where((s_block[:, None] == s_block[None, :])[None], scores, -1e30)

    def attend(members):
        q_block, k_block, v_block, s_block = members
        scores = block_scores(q_block, k_block, s_block)
        row_top = jnp.max(scores, axis=-1, keepdims=True)
        exp_scores = jnp.exp(scores - row_top)
        row_total = jnp.sum(exp_scores, axis=-1, keepdims=True)
        probability = (exp_scores / row_total).astype(jnp.bfloat16)
        mixed_block = jnp.einsum(
            "hqk,khd->qhd", probability, v_block, preferred_element_type=jnp.float32
        )
        return (mixed_block, row_top + jnp.log(row_total))

    mixed_heads, log_total = lax.map(attend, (q_low, k_low, v_low, s_blocks))
    mixed_low = mixed_heads.reshape(length, model_width).astype(jnp.bfloat16)
    residual = inputs + jnp.dot(mixed_low, full_out, preferred_element_type=jnp.float32)
    second, second_back = jax.vjp(layer_norm, residual, norm_gains[1], biases[1])
    second_low = second.astype(jnp.bfloat16)
    up_pre = jnp.dot(second_low, full_up, preferred_element_type=jnp.float32)
    active, gelu_back = jax.vjp(partial(jax.nn.gelu, approximate=False), up_pre)
    active_low = active.astype(jnp.bfloat16)
    output = residual + jnp.dot(active_low, full_down, preferred_element_type=jnp.float32)
    layer_out = (valid_rows * output).astype(jnp.bfloat16)
    back_qkv, back_out, back_up, back_down = full_qkv, full_out, full_up, full_down
    upstream = cotangent.astype(jnp.float32) * valid_rows
    up_low = upstream.astype(jnp.bfloat16)
    grad_down = jnp.dot(active_low.T, up_low, preferred_element_type=jnp.float32)
    grad_active = jnp.dot(up_low, back_down.T, preferred_element_type=jnp.float32)
    (grad_pre,) = gelu_back(grad_active)
    pre_low = grad_pre.astype(jnp.bfloat16)
    grad_up = jnp.dot(second_low.T, pre_low, preferred_element_type=jnp.float32)
    if fast:
        early = [_reduce_matrix(grad_up), _reduce_matrix(grad_down)]
    grad_second = jnp.dot(pre_low, back_up.T, preferred_element_type=jnp.float32)
    grad_resid, gain_two, bias_two = second_back(grad_second)
    grad_resid = grad_resid + upstream
    resid_low = grad_resid.astype(jnp.bfloat16)
    grad_outw = jnp.dot(mixed_low.T, resid_low, preferred_element_type=jnp.float32)
    grad_mixed = jnp.dot(resid_low, back_out.T, preferred_element_type=jnp.float32)
    grad_mixed = grad_mixed.astype(jnp.bfloat16).reshape(blocks, PATCH_BIG, HEADS, HEAD_DIM)

    def attend_back(members):
        q_block, k_block, v_block, s_block, l_block, d_block = members
        scores = block_scores(q_block, k_block, s_block)
        probability = jnp.exp(scores - l_block)
        prob_low = probability.astype(jnp.bfloat16)
        grad_v = jnp.einsum("hqk,qhd->khd", prob_low, d_block, preferred_element_type=jnp.float32)
        grad_p = jnp.einsum("qhd,khd->hqk", d_block, v_block, preferred_element_type=jnp.float32)
        grad_p = lax.optimization_barrier(grad_p.astype(jnp.bfloat16)).astype(jnp.float32)
        grad_s = probability * (grad_p - jnp.sum(probability * grad_p, axis=-1, keepdims=True))
        s_low = grad_s.astype(jnp.bfloat16)
        grad_q = (
            jnp.einsum("hqk,khd->qhd", s_low, k_block, preferred_element_type=jnp.float32) * scaling
        )
        grad_k = (
            jnp.einsum("hqk,qhd->khd", s_low, q_block, preferred_element_type=jnp.float32) * scaling
        )
        return (grad_q, grad_k, grad_v)

    grad_qn, grad_kn, grad_vn = map_blocks(
        attend_back, (q_low, k_low, v_low, s_blocks, log_total, grad_mixed)
    )
    grad_q, grad_k, gain_q, gain_k = norms_back(
        (grad_qn.reshape(length, HEADS, HEAD_DIM), grad_kn.reshape(length, HEADS, HEAD_DIM))
    )
    grad_project = jnp.concatenate(
        [
            grad_q.reshape(length, model_width),
            grad_k.reshape(length, model_width),
            grad_vn.reshape(length, model_width),
        ],
        axis=1,
    ).astype(jnp.bfloat16)
    grad_qkv = jnp.dot(normed_low.T, grad_project, preferred_element_type=jnp.float32)
    grad_normed = jnp.dot(grad_project, back_qkv.T, preferred_element_type=jnp.float32)
    grad_input, gain_one, bias_one = first_back(grad_normed)
    grad_tokens = (grad_input + grad_resid).astype(jnp.bfloat16)
    grad_gain = jnp.stack([gain_one, gain_two])
    grad_bias = jnp.stack([bias_one, bias_two])
    grad_qk = jnp.stack([gain_q.reshape(model_width), gain_k.reshape(model_width)])
    summands = (grad_qkv, grad_outw, grad_up, grad_down, grad_gain, grad_bias, grad_qk)
    if fast:
        late = fast_reduce(summands[:2], summands[4:])
        shares = late[:2] + early + late[2:]
    else:
        pieces = [
            lax.psum_scatter(
                s.astype(jnp.bfloat16), "fsdp", scatter_dimension=0 if k < 4 else 1, tiled=True
            ).astype(jnp.float32)
            for k, s in enumerate(summands)
        ]
        shares = [lax.psum(p.astype(jnp.bfloat16), "dp").astype(jnp.float32) for p in pieces]
    return (
        layer_out,
        grad_tokens,
        shares[0],
        shares[1],
        shares[2],
        shares[3],
        shares[4],
        shares[5],
        shares[6],
    )


def solution(mesh):
    in_specs = (
        P(("dp", "fsdp"), None),
        P(("dp", "fsdp"), None),
        P("fsdp", None),
        P("fsdp", None),
        P("fsdp", None),
        P("fsdp", None),
        P(None, "fsdp"),
        P(None, "fsdp"),
        P(None, "fsdp"),
        P(("dp", "fsdp"), None),
    )
    out_specs = (
        P(("dp", "fsdp"), None),
        P(("dp", "fsdp"), None),
        P("fsdp", None),
        P("fsdp", None),
        P("fsdp", None),
        P("fsdp", None),
        P(None, "fsdp"),
        P(None, "fsdp"),
        P(None, "fsdp"),
    )
    fast = dict(mesh.shape) == {"dp": NDP_FAST, "fsdp": NF_FAST}
    return jax.shard_map(
        partial(on_device, fast), mesh=mesh, in_specs=in_specs, out_specs=out_specs, check_vma=False
    )
```

```python
from functools import partial

import jax
import jax.numpy as jnp
from jax import lax
from jax.sharding import PartitionSpec as P


HEADS = 12
HEAD_DIM = 64
PATCH_BIG = 576


epsilon = 1e-06


def layer_norm(v, gain_row, bias_row):
    centre = v - jnp.mean(v, axis=-1, keepdims=True)
    spread = jnp.mean(centre * centre, axis=-1, keepdims=True)
    return centre * lax.rsqrt(spread + epsilon) * gain_row + bias_row


def head_norm(v, gain_row):
    centre = v - jnp.mean(v, axis=-1, keepdims=True)
    spread = jnp.mean(centre * centre, axis=-1, keepdims=True)
    return centre * lax.rsqrt(spread + epsilon) * gain_row


def both_norms(q_in, k_in, q_gain, k_gain):
    return (head_norm(q_in, q_gain), head_norm(k_in, k_gain))


NF_FAST = 4
NDP_FAST = 8


LANES = 128


def _plane_gather(z):
    d = lax.axis_index("dp")
    c = d % 2
    a = lax.ppermute(z, "dp", [(i, i ^ 2) for i in range(NDP_FAST)])
    b = lax.ppermute(z, "dp", [(i, i ^ 4) for i in range(NDP_FAST)])
    send = jnp.where(c == 0, b, a)
    diag = lax.ppermute(
        send, "dp", [(i, i ^ 2) if i % 2 == 0 else (i, i ^ 4) for i in range(NDP_FAST)]
    )
    mine = jnp.stack([z, a, b, diag])
    sib = lax.ppermute(mine, "dp", [(i, i ^ 1) for i in range(NDP_FAST)])
    return jnp.stack([mine[0], sib[0], mine[1], sib[1], mine[2], sib[2], mine[3], sib[3]])


def _take(x, idx, axis):
    return jnp.take(x, idx, axis=axis, mode="wrap")


def _z_gather(piece):
    f = lax.axis_index("fsdp")
    slots = [piece] + [
        lax.ppermute(piece, "fsdp", [(i, (i + k) % NF_FAST) for i in range(NF_FAST)])
        for k in range(1, NF_FAST)
    ]
    return _take(jnp.stack(slots), (f - jnp.arange(NF_FAST, dtype=jnp.int32)) % NF_FAST, 0)


def _gather_matrix(m):
    d = lax.axis_index("dp")
    j, c = d // 2, d % 2
    rows, cols = m.shape[0] // (NDP_FAST // 2), m.shape[1] // 2
    piece = lax.dynamic_slice(m, (j * rows, c * cols), (rows, cols))
    z = _z_gather(piece)
    x = lax.all_gather(z, "dp", axis=1, tiled=False)
    x = x.reshape(NF_FAST, NDP_FAST // 2, 2, rows, cols)
    x = jnp.concatenate([x[:, :, 0], x[:, :, 1]], axis=-1)
    return x.reshape(NF_FAST * m.shape[0], m.shape[1])


def fast_gather(mats, gains):
    out = [_gather_matrix(m) for m in mats]
    stacked = jnp.concatenate(gains, axis=0)
    z = _z_gather(stacked)
    full = z.transpose(1, 0, 2).reshape(stacked.shape[0], NF_FAST * stacked.shape[1])
    rows = 0
    for g in gains:
        out.append(full[rows : rows + g.shape[0]])
        rows += g.shape[0]
    return out


def _reduce_matrix(g):
    d = lax.axis_index("dp")
    f = lax.axis_index("fsdp")
    j, c = d // 2, d % 2
    n_chips = NDP_FAST // 2
    rows, cols = g.shape[0] // (NF_FAST * n_chips), g.shape[1] // 2

    def half(which):
        part = lax.dynamic_slice_in_dim(g, which * cols, cols, 1)
        return part.reshape(NF_FAST, n_chips, rows, cols)

    got = lax.ppermute(half(1 - c).astype(jnp.bfloat16), "dp", [(i, i ^ 1) for i in range(NDP_FAST)])
    chip = half(c) + got.astype(jnp.float32)

    def of_chip(k):
        return lax.dynamic_index_in_dim(chip, k, 1, keepdims=False)

    moved = lax.ppermute(
        of_chip(j ^ 3).astype(jnp.bfloat16),
        "dp",
        [(i, i ^ 2) if i % 2 == 0 else (i, i ^ 4) for i in range(NDP_FAST)],
    ).astype(jnp.float32)
    to_x = of_chip(j ^ 1) + jnp.where(c == 1, moved, 0.0)
    to_y = of_chip(j ^ 2) + jnp.where(c == 0, moved, 0.0)
    from_x = lax.ppermute(to_x.astype(jnp.bfloat16), "dp", [(i, i ^ 2) for i in range(NDP_FAST)])
    from_y = lax.ppermute(to_y.astype(jnp.bfloat16), "dp", [(i, i ^ 4) for i in range(NDP_FAST)])
    plane = of_chip(j) + from_x.astype(jnp.float32) + from_y.astype(jnp.float32)
    total = lax.dynamic_index_in_dim(plane, f, 0, keepdims=False)
    for k in range(1, NF_FAST):
        part = lax.dynamic_index_in_dim(plane, (f + k) % NF_FAST, 0, keepdims=False)
        total = total + lax.ppermute(
            part.astype(jnp.bfloat16), "fsdp", [(i, (i + k) % NF_FAST) for i in range(NF_FAST)]
        ).astype(jnp.float32)
    x = _take(_plane_gather(total), jnp.arange(NDP_FAST, dtype=jnp.int32) ^ d, 0)
    x = x.reshape(n_chips, 2, rows, cols)
    x = jnp.concatenate([x[:, 0], x[:, 1]], axis=-1)
    return x.reshape(n_chips * rows, 2 * cols)


def fast_reduce(mats, gains):
    stacked = jnp.concatenate(gains, axis=0)
    pad = 2 * LANES - stacked.shape[0]
    first = jnp.concatenate([mats[0], jnp.pad(stacked.T, ((0, 0), (0, pad)))], axis=1)
    shard = _reduce_matrix(first)
    width = mats[0].shape[1]
    out = [shard[:, :width]] + [_reduce_matrix(m) for m in mats[1:]]
    mine = shard[:, width : width + stacked.shape[0]].T
    rows = 0
    for g in gains:
        out.append(mine[rows : rows + g.shape[0]])
        rows += g.shape[0]
    return out


def map_blocks(fn, members):
    if members[0].shape[0] == 1:
        return jax.tree.map(lambda v: v[None], fn(tuple(m[0] for m in members)))
    return lax.map(fn, members)


def on_device(fast, *args):
    return layer(fast, *args)


def layer(
    fast, tokens, image_lengths, w_qkv, w_out, w_up, w_down, ln_gain, ln_bias, qk_gain, cotangent
):
    if fast:
        full_qkv, full_out, full_up, full_down, gain_all, bias_all, qk_all = fast_gather(
            (w_qkv, w_out, w_up, w_down), (ln_gain, ln_bias, qk_gain)
        )
    else:
        full_qkv, full_out, full_up, full_down, gain_all, bias_all, qk_all = (
            lax.all_gather(w_qkv, "fsdp", axis=0, tiled=True),
            lax.all_gather(w_out, "fsdp", axis=0, tiled=True),
            lax.all_gather(w_up, "fsdp", axis=0, tiled=True),
            lax.all_gather(w_down, "fsdp", axis=0, tiled=True),
            lax.all_gather(ln_gain, "fsdp", axis=1, tiled=True),
            lax.all_gather(ln_bias, "fsdp", axis=1, tiled=True),
            lax.all_gather(qk_gain, "fsdp", axis=1, tiled=True),
        )
    length = tokens.shape[0]
    model_width = tokens.shape[1]
    blocks = length // PATCH_BIG
    scaling = HEAD_DIM ** (-0.5)
    position = jnp.arange(length, dtype=jnp.int32)
    limits = jnp.cumsum(image_lengths[0])
    segment = jnp.sum((position[:, None] >= limits[None, :]).astype(jnp.int32), axis=1)
    valid_rows = (position < limits[-1]).astype(jnp.float32)[:, None]
    norm_gains = gain_all.astype(jnp.float32)
    biases = bias_all.astype(jnp.float32)
    qk_gains = qk_all.astype(jnp.float32).reshape(2, HEADS, HEAD_DIM)
    inputs = tokens.astype(jnp.float32)
    normed, first_back = jax.vjp(layer_norm, inputs, norm_gains[0], biases[0])
    normed_low = normed.astype(jnp.bfloat16)
    project = jnp.dot(normed_low, full_qkv, preferred_element_type=jnp.float32)
    queries = project[:, :model_width].reshape(length, HEADS, HEAD_DIM)
    keys_raw = project[:, model_width : 2 * model_width].reshape(length, HEADS, HEAD_DIM)
    values_raw = project[:, 2 * model_width :]
    (q_norm, k_norm), norms_back = jax.vjp(both_norms, queries, keys_raw, qk_gains[0], qk_gains[1])
    q_low = q_norm.astype(jnp.bfloat16).reshape(blocks, PATCH_BIG, HEADS, HEAD_DIM)
    k_low = k_norm.astype(jnp.bfloat16).reshape(blocks, PATCH_BIG, HEADS, HEAD_DIM)
    v_low = values_raw.astype(jnp.bfloat16).reshape(blocks, PATCH_BIG, HEADS, HEAD_DIM)
    s_blocks = segment.reshape(blocks, PATCH_BIG)

    def block_scores(q_block, k_block, s_block):
        scores = (
            jnp.einsum("qhd,khd->hqk", q_block, k_block, preferred_element_type=jnp.float32)
            * scaling
        )
        return jnp.where((s_block[:, None] == s_block[None, :])[None], scores, -1e30)

    def attend(members):
        q_block, k_block, v_block, s_block = members
        scores = block_scores(q_block, k_block, s_block)
        row_top = jnp.max(scores, axis=-1, keepdims=True)
        exp_scores = jnp.exp(scores - row_top)
        row_total = jnp.sum(exp_scores, axis=-1, keepdims=True)
        probability = (exp_scores / row_total).astype(jnp.bfloat16)
        mixed_block = jnp.einsum(
            "hqk,khd->qhd", probability, v_block, preferred_element_type=jnp.float32
        )
        return (mixed_block, row_top + jnp.log(row_total))

    mixed_heads, log_total = lax.map(attend, (q_low, k_low, v_low, s_blocks))
    mixed_low = mixed_heads.reshape(length, model_width).astype(jnp.bfloat16)
    residual = inputs + jnp.dot(mixed_low, full_out, preferred_element_type=jnp.float32)
    second, second_back = jax.vjp(layer_norm, residual, norm_gains[1], biases[1])
    second_low = second.astype(jnp.bfloat16)
    up_pre = jnp.dot(second_low, full_up, preferred_element_type=jnp.float32)
    active, gelu_back = jax.vjp(partial(jax.nn.gelu, approximate=False), up_pre)
    active_low = active.astype(jnp.bfloat16)
    output = residual + jnp.dot(active_low, full_down, preferred_element_type=jnp.float32)
    layer_out = (valid_rows * output).astype(jnp.bfloat16)
    back_qkv, back_out, back_up, back_down = full_qkv, full_out, full_up, full_down
    upstream = cotangent.astype(jnp.float32) * valid_rows
    up_low = upstream.astype(jnp.bfloat16)
    grad_down = jnp.dot(active_low.T, up_low, preferred_element_type=jnp.float32)
    grad_active = jnp.dot(up_low, back_down.T, preferred_element_type=jnp.float32)
    (grad_pre,) = gelu_back(grad_active)
    pre_low = grad_pre.astype(jnp.bfloat16)
    grad_up = jnp.dot(second_low.T, pre_low, preferred_element_type=jnp.float32)
    if fast:
        early = [_reduce_matrix(grad_up), _reduce_matrix(grad_down)]
    grad_second = jnp.dot(pre_low, back_up.T, preferred_element_type=jnp.float32)
    grad_resid, gain_two, bias_two = second_back(grad_second)
    grad_resid = grad_resid + upstream
    resid_low = grad_resid.astype(jnp.bfloat16)
    grad_outw = jnp.dot(mixed_low.T, resid_low, preferred_element_type=jnp.float32)
    grad_mixed = jnp.dot(resid_low, back_out.T, preferred_element_type=jnp.float32)
    grad_mixed = grad_mixed.astype(jnp.bfloat16).reshape(blocks, PATCH_BIG, HEADS, HEAD_DIM)

    def attend_back(members):
        q_block, k_block, v_block, s_block, l_block, d_block = members
        scores = block_scores(q_block, k_block, s_block)
        probability = jnp.exp(scores - l_block)
        prob_low = probability.astype(jnp.bfloat16)
        grad_v = jnp.einsum("hqk,qhd->khd", prob_low, d_block, preferred_element_type=jnp.float32)
        grad_p = jnp.einsum("qhd,khd->hqk", d_block, v_block, preferred_element_type=jnp.float32)
        grad_p = lax.optimization_barrier(grad_p.astype(jnp.bfloat16)).astype(jnp.float32)
        grad_s = probability * (grad_p - jnp.sum(probability * grad_p, axis=-1, keepdims=True))
        s_low = grad_s.astype(jnp.bfloat16)
        grad_q = (
            jnp.einsum("hqk,khd->qhd", s_low, k_block, preferred_element_type=jnp.float32) * scaling
        )
        grad_k = (
            jnp.einsum("hqk,qhd->khd", s_low, q_block, preferred_element_type=jnp.float32) * scaling
        )
        return (grad_q, grad_k, grad_v)

    grad_qn, grad_kn, grad_vn = map_blocks(
        attend_back, (q_low, k_low, v_low, s_blocks, log_total, grad_mixed)
    )
    grad_q, grad_k, gain_q, gain_k = norms_back(
        (grad_qn.reshape(length, HEADS, HEAD_DIM), grad_kn.reshape(length, HEADS, HEAD_DIM))
    )
    grad_project = jnp.concatenate(
        [
            grad_q.reshape(length, model_width),
            grad_k.reshape(length, model_width),
            grad_vn.reshape(length, model_width),
        ],
        axis=1,
    ).astype(jnp.bfloat16)
    grad_qkv = jnp.dot(normed_low.T, grad_project, preferred_element_type=jnp.float32)
    grad_normed = jnp.dot(grad_project, back_qkv.T, preferred_element_type=jnp.float32)
    grad_input, gain_one, bias_one = first_back(grad_normed)
    grad_tokens = (grad_input + grad_resid).astype(jnp.bfloat16)
    grad_gain = jnp.stack([gain_one, gain_two])
    grad_bias = jnp.stack([bias_one, bias_two])
    grad_qk = jnp.stack([gain_q.reshape(model_width), gain_k.reshape(model_width)])
    summands = (grad_qkv, grad_outw, grad_up, grad_down, grad_gain, grad_bias, grad_qk)
    if fast:
        late = fast_reduce(summands[:2], summands[4:])
        shares = late[:2] + early + late[2:]
    else:
        pieces = [
            lax.psum_scatter(
                s.astype(jnp.bfloat16), "fsdp", scatter_dimension=0 if k < 4 else 1, tiled=True
            ).astype(jnp.float32)
            for k, s in enumerate(summands)
        ]
        shares = [lax.psum(p.astype(jnp.bfloat16), "dp").astype(jnp.float32) for p in pieces]
    return (
        layer_out,
        grad_tokens,
        shares[0],
        shares[1],
        shares[2],
        shares[3],
        shares[4],
        shares[5],
        shares[6],
    )


def solution(mesh):
    in_specs = (
        P(("dp", "fsdp"), None),
        P(("dp", "fsdp"), None),
        P("fsdp", None),
        P("fsdp", None),
        P("fsdp", None),
        P("fsdp", None),
        P(None, "fsdp"),
        P(None, "fsdp"),
        P(None, "fsdp"),
        P(("dp", "fsdp"), None),
    )
    out_specs = (
        P(("dp", "fsdp"), None),
        P(("dp", "fsdp"), None),
        P("fsdp", None),
        P("fsdp", None),
        P("fsdp", None),
        P("fsdp", None),
        P(None, "fsdp"),
        P(None, "fsdp"),
        P(None, "fsdp"),
    )
    fast = dict(mesh.shape) == {"dp": NDP_FAST, "fsdp": NF_FAST}
    return jax.shard_map(
        partial(on_device, fast), mesh=mesh, in_specs=in_specs, out_specs=out_specs, check_vma=False
    )
```

```python
from functools import partial

import jax
import jax.numpy as jnp
from jax import lax
from jax.sharding import PartitionSpec as P


HEADS = 12
HEAD_DIM = 64
PATCH_BIG = 576


epsilon = 1e-06


def layer_norm(v, gain_row, bias_row):
    centre = v - jnp.mean(v, axis=-1, keepdims=True)
    spread = jnp.mean(centre * centre, axis=-1, keepdims=True)
    return centre * lax.rsqrt(spread + epsilon) * gain_row + bias_row


def head_norm(v, gain_row):
    centre = v - jnp.mean(v, axis=-1, keepdims=True)
    spread = jnp.mean(centre * centre, axis=-1, keepdims=True)
    return centre * lax.rsqrt(spread + epsilon) * gain_row


def both_norms(q_in, k_in, q_gain, k_gain):
    return (head_norm(q_in, q_gain), head_norm(k_in, k_gain))


NF_FAST = 4
NDP_FAST = 8


LANES = 128


def _take(x, idx, axis):
    return jnp.take(x, idx, axis=axis, mode="wrap")


def _z_gather(piece):
    f = lax.axis_index("fsdp")
    slots = [piece] + [
        lax.ppermute(piece, "fsdp", [(i, (i + k) % NF_FAST) for i in range(NF_FAST)])
        for k in range(1, NF_FAST)
    ]
    return _take(jnp.stack(slots), (f - jnp.arange(NF_FAST, dtype=jnp.int32)) % NF_FAST, 0)


def _gather_matrix(m):
    d = lax.axis_index("dp")
    j, c = d // 2, d % 2
    rows, cols = m.shape[0] // (NDP_FAST // 2), m.shape[1] // 2
    piece = lax.dynamic_slice(m, (j * rows, c * cols), (rows, cols))
    z = _z_gather(piece)
    x = lax.all_gather(z, "dp", axis=1, tiled=False)
    x = x.reshape(NF_FAST, NDP_FAST // 2, 2, rows, cols)
    x = jnp.concatenate([x[:, :, 0], x[:, :, 1]], axis=-1)
    return x.reshape(NF_FAST * m.shape[0], m.shape[1])


def fast_gather(mats, gains):
    out = [_gather_matrix(m) for m in mats]
    stacked = jnp.concatenate(gains, axis=0)
    z = _z_gather(stacked)
    full = z.transpose(1, 0, 2).reshape(stacked.shape[0], NF_FAST * stacked.shape[1])
    rows = 0
    for g in gains:
        out.append(full[rows : rows + g.shape[0]])
        rows += g.shape[0]
    return out


def _reduce_matrix(g):
    d = lax.axis_index("dp")
    f = lax.axis_index("fsdp")
    j, c = d // 2, d % 2
    n_chips = NDP_FAST // 2
    rows, cols = g.shape[0] // (NF_FAST * n_chips), g.shape[1] // 2

    def half(which):
        part = lax.dynamic_slice_in_dim(g, which * cols, cols, 1)
        return part.reshape(NF_FAST, n_chips, rows, cols)

    got = lax.ppermute(half(1 - c).astype(jnp.bfloat16), "dp", [(i, i ^ 1) for i in range(NDP_FAST)])
    chip = half(c) + got.astype(jnp.float32)

    def of_chip(k):
        return lax.dynamic_index_in_dim(chip, k, 1, keepdims=False)

    moved = lax.ppermute(
        of_chip(j ^ 3).astype(jnp.bfloat16),
        "dp",
        [(i, i ^ 2) if i % 2 == 0 else (i, i ^ 4) for i in range(NDP_FAST)],
    ).astype(jnp.float32)
    to_x = of_chip(j ^ 1) + jnp.where(c == 1, moved, 0.0)
    to_y = of_chip(j ^ 2) + jnp.where(c == 0, moved, 0.0)
    from_x = lax.ppermute(to_x.astype(jnp.bfloat16), "dp", [(i, i ^ 2) for i in range(NDP_FAST)])
    from_y = lax.ppermute(to_y.astype(jnp.bfloat16), "dp", [(i, i ^ 4) for i in range(NDP_FAST)])
    plane = of_chip(j) + from_x.astype(jnp.float32) + from_y.astype(jnp.float32)
    total = lax.dynamic_index_in_dim(plane, f, 0, keepdims=False)
    for k in range(1, NF_FAST):
        part = lax.dynamic_index_in_dim(plane, (f + k) % NF_FAST, 0, keepdims=False)
        total = total + lax.ppermute(
            part.astype(jnp.bfloat16), "fsdp", [(i, (i + k) % NF_FAST) for i in range(NF_FAST)]
        ).astype(jnp.float32)
    x = lax.all_gather(total, "dp", axis=0, tiled=False)
    x = x.reshape(n_chips, 2, rows, cols)
    x = jnp.concatenate([x[:, 0], x[:, 1]], axis=-1)
    return x.reshape(n_chips * rows, 2 * cols)


def fast_reduce(mats, gains):
    stacked = jnp.concatenate(gains, axis=0)
    pad = 2 * LANES - stacked.shape[0]
    first = jnp.concatenate([mats[0], jnp.pad(stacked.T, ((0, 0), (0, pad)))], axis=1)
    shard = _reduce_matrix(first)
    width = mats[0].shape[1]
    out = [shard[:, :width]] + [_reduce_matrix(m) for m in mats[1:]]
    mine = shard[:, width : width + stacked.shape[0]].T
    rows = 0
    for g in gains:
        out.append(mine[rows : rows + g.shape[0]])
        rows += g.shape[0]
    return out


def map_blocks(fn, members):
    if members[0].shape[0] == 1:
        return jax.tree.map(lambda v: v[None], fn(tuple(m[0] for m in members)))
    return lax.map(fn, members)


def on_device(fast, *args):
    return layer(fast, *args)


def layer(
    fast, tokens, image_lengths, w_qkv, w_out, w_up, w_down, ln_gain, ln_bias, qk_gain, cotangent
):
    if fast:
        full_qkv, full_out, full_up, full_down, gain_all, bias_all, qk_all = fast_gather(
            (w_qkv, w_out, w_up, w_down), (ln_gain, ln_bias, qk_gain)
        )
    else:
        full_qkv, full_out, full_up, full_down, gain_all, bias_all, qk_all = (
            lax.all_gather(w_qkv, "fsdp", axis=0, tiled=True),
            lax.all_gather(w_out, "fsdp", axis=0, tiled=True),
            lax.all_gather(w_up, "fsdp", axis=0, tiled=True),
            lax.all_gather(w_down, "fsdp", axis=0, tiled=True),
            lax.all_gather(ln_gain, "fsdp", axis=1, tiled=True),
            lax.all_gather(ln_bias, "fsdp", axis=1, tiled=True),
            lax.all_gather(qk_gain, "fsdp", axis=1, tiled=True),
        )
    length = tokens.shape[0]
    model_width = tokens.shape[1]
    blocks = length // PATCH_BIG
    scaling = HEAD_DIM ** (-0.5)
    position = jnp.arange(length, dtype=jnp.int32)
    limits = jnp.cumsum(image_lengths[0])
    segment = jnp.sum((position[:, None] >= limits[None, :]).astype(jnp.int32), axis=1)
    valid_rows = (position < limits[-1]).astype(jnp.float32)[:, None]
    norm_gains = gain_all.astype(jnp.float32)
    biases = bias_all.astype(jnp.float32)
    qk_gains = qk_all.astype(jnp.float32).reshape(2, HEADS, HEAD_DIM)
    inputs = tokens.astype(jnp.float32)
    normed, first_back = jax.vjp(layer_norm, inputs, norm_gains[0], biases[0])
    normed_low = normed.astype(jnp.bfloat16)
    project = jnp.dot(normed_low, full_qkv, preferred_element_type=jnp.float32)
    queries = project[:, :model_width].reshape(length, HEADS, HEAD_DIM)
    keys_raw = project[:, model_width : 2 * model_width].reshape(length, HEADS, HEAD_DIM)
    values_raw = project[:, 2 * model_width :]
    (q_norm, k_norm), norms_back = jax.vjp(both_norms, queries, keys_raw, qk_gains[0], qk_gains[1])
    q_low = q_norm.astype(jnp.bfloat16).reshape(blocks, PATCH_BIG, HEADS, HEAD_DIM)
    k_low = k_norm.astype(jnp.bfloat16).reshape(blocks, PATCH_BIG, HEADS, HEAD_DIM)
    v_low = values_raw.astype(jnp.bfloat16).reshape(blocks, PATCH_BIG, HEADS, HEAD_DIM)
    s_blocks = segment.reshape(blocks, PATCH_BIG)

    def block_scores(q_block, k_block, s_block):
        scores = (
            jnp.einsum("qhd,khd->hqk", q_block, k_block, preferred_element_type=jnp.float32)
            * scaling
        )
        return jnp.where((s_block[:, None] == s_block[None, :])[None], scores, -1e30)

    def attend(members):
        q_block, k_block, v_block, s_block = members
        scores = block_scores(q_block, k_block, s_block)
        row_top = jnp.max(scores, axis=-1, keepdims=True)
        exp_scores = jnp.exp(scores - row_top)
        row_total = jnp.sum(exp_scores, axis=-1, keepdims=True)
        probability = (exp_scores / row_total).astype(jnp.bfloat16)
        mixed_block = jnp.einsum(
            "hqk,khd->qhd", probability, v_block, preferred_element_type=jnp.float32
        )
        return (mixed_block, row_top + jnp.log(row_total))

    mixed_heads, log_total = lax.map(attend, (q_low, k_low, v_low, s_blocks))
    mixed_low = mixed_heads.reshape(length, model_width).astype(jnp.bfloat16)
    residual = inputs + jnp.dot(mixed_low, full_out, preferred_element_type=jnp.float32)
    second, second_back = jax.vjp(layer_norm, residual, norm_gains[1], biases[1])
    second_low = second.astype(jnp.bfloat16)
    up_pre = jnp.dot(second_low, full_up, preferred_element_type=jnp.float32)
    active, gelu_back = jax.vjp(partial(jax.nn.gelu, approximate=False), up_pre)
    active_low = active.astype(jnp.bfloat16)
    output = residual + jnp.dot(active_low, full_down, preferred_element_type=jnp.float32)
    layer_out = (valid_rows * output).astype(jnp.bfloat16)
    back_qkv, back_out, back_up, back_down = full_qkv, full_out, full_up, full_down
    upstream = cotangent.astype(jnp.float32) * valid_rows
    up_low = upstream.astype(jnp.bfloat16)
    grad_down = jnp.dot(active_low.T, up_low, preferred_element_type=jnp.float32)
    grad_active = jnp.dot(up_low, back_down.T, preferred_element_type=jnp.float32)
    (grad_pre,) = gelu_back(grad_active)
    pre_low = grad_pre.astype(jnp.bfloat16)
    grad_up = jnp.dot(second_low.T, pre_low, preferred_element_type=jnp.float32)
    if fast:
        early = [_reduce_matrix(grad_up), _reduce_matrix(grad_down)]
    grad_second = jnp.dot(pre_low, back_up.T, preferred_element_type=jnp.float32)
    grad_resid, gain_two, bias_two = second_back(grad_second)
    grad_resid = grad_resid + upstream
    resid_low = grad_resid.astype(jnp.bfloat16)
    grad_outw = jnp.dot(mixed_low.T, resid_low, preferred_element_type=jnp.float32)
    if fast:
        early = [_reduce_matrix(grad_outw)] + early
    grad_mixed = jnp.dot(resid_low, back_out.T, preferred_element_type=jnp.float32)
    grad_mixed = grad_mixed.astype(jnp.bfloat16).reshape(blocks, PATCH_BIG, HEADS, HEAD_DIM)

    def attend_back(members):
        q_block, k_block, v_block, s_block, l_block, d_block = members
        scores = block_scores(q_block, k_block, s_block)
        probability = jnp.exp(scores - l_block)
        prob_low = probability.astype(jnp.bfloat16)
        grad_v = jnp.einsum("hqk,qhd->khd", prob_low, d_block, preferred_element_type=jnp.float32)
        grad_p = jnp.einsum("qhd,khd->hqk", d_block, v_block, preferred_element_type=jnp.float32)
        grad_p = lax.optimization_barrier(grad_p.astype(jnp.bfloat16)).astype(jnp.float32)
        grad_s = probability * (grad_p - jnp.sum(probability * grad_p, axis=-1, keepdims=True))
        s_low = grad_s.astype(jnp.bfloat16)
        grad_q = (
            jnp.einsum("hqk,khd->qhd", s_low, k_block, preferred_element_type=jnp.float32) * scaling
        )
        grad_k = (
            jnp.einsum("hqk,qhd->khd", s_low, q_block, preferred_element_type=jnp.float32) * scaling
        )
        return (grad_q, grad_k, grad_v)

    grad_qn, grad_kn, grad_vn = map_blocks(
        attend_back, (q_low, k_low, v_low, s_blocks, log_total, grad_mixed)
    )
    grad_q, grad_k, gain_q, gain_k = norms_back(
        (grad_qn.reshape(length, HEADS, HEAD_DIM), grad_kn.reshape(length, HEADS, HEAD_DIM))
    )
    grad_project = jnp.concatenate(
        [
            grad_q.reshape(length, model_width),
            grad_k.reshape(length, model_width),
            grad_vn.reshape(length, model_width),
        ],
        axis=1,
    ).astype(jnp.bfloat16)
    grad_qkv = jnp.dot(normed_low.T, grad_project, preferred_element_type=jnp.float32)
    grad_normed = jnp.dot(grad_project, back_qkv.T, preferred_element_type=jnp.float32)
    grad_input, gain_one, bias_one = first_back(grad_normed)
    grad_tokens = (grad_input + grad_resid).astype(jnp.bfloat16)
    grad_gain = jnp.stack([gain_one, gain_two])
    grad_bias = jnp.stack([bias_one, bias_two])
    grad_qk = jnp.stack([gain_q.reshape(model_width), gain_k.reshape(model_width)])
    summands = (grad_qkv, grad_outw, grad_up, grad_down, grad_gain, grad_bias, grad_qk)
    if fast:
        late = fast_reduce(summands[:1], summands[4:])
        shares = late[:1] + early + late[1:]
    else:
        pieces = [
            lax.psum_scatter(
                s.astype(jnp.bfloat16), "fsdp", scatter_dimension=0 if k < 4 else 1, tiled=True
            ).astype(jnp.float32)
            for k, s in enumerate(summands)
        ]
        shares = [lax.psum(p.astype(jnp.bfloat16), "dp").astype(jnp.float32) for p in pieces]
    return (
        layer_out,
        grad_tokens,
        shares[0],
        shares[1],
        shares[2],
        shares[3],
        shares[4],
        shares[5],
        shares[6],
    )


def solution(mesh):
    in_specs = (
        P(("dp", "fsdp"), None),
        P(("dp", "fsdp"), None),
        P("fsdp", None),
        P("fsdp", None),
        P("fsdp", None),
        P("fsdp", None),
        P(None, "fsdp"),
        P(None, "fsdp"),
        P(None, "fsdp"),
        P(("dp", "fsdp"), None),
    )
    out_specs = (
        P(("dp", "fsdp"), None),
        P(("dp", "fsdp"), None),
        P("fsdp", None),
        P("fsdp", None),
        P("fsdp", None),
        P("fsdp", None),
        P(None, "fsdp"),
        P(None, "fsdp"),
        P(None, "fsdp"),
    )
    fast = dict(mesh.shape) == {"dp": NDP_FAST, "fsdp": NF_FAST}
    return jax.shard_map(
        partial(on_device, fast), mesh=mesh, in_specs=in_specs, out_specs=out_specs, check_vma=False
    )
```

```python
from functools import partial

import jax
import jax.numpy as jnp
from jax import lax
from jax.sharding import PartitionSpec as P


HEADS = 12
HEAD_DIM = 64
PATCH_BIG = 576


epsilon = 1e-06


def layer_norm(v, gain_row, bias_row):
    centre = v - jnp.mean(v, axis=-1, keepdims=True)
    spread = jnp.mean(centre * centre, axis=-1, keepdims=True)
    return centre * lax.rsqrt(spread + epsilon) * gain_row + bias_row


def head_norm(v, gain_row):
    centre = v - jnp.mean(v, axis=-1, keepdims=True)
    spread = jnp.mean(centre * centre, axis=-1, keepdims=True)
    return centre * lax.rsqrt(spread + epsilon) * gain_row


def both_norms(q_in, k_in, q_gain, k_gain):
    return (head_norm(q_in, q_gain), head_norm(k_in, k_gain))


NF_FAST = 4
NDP_FAST = 8


LANES = 128


def _plane_gather(z):
    d = lax.axis_index("dp")
    c = d % 2
    a = lax.ppermute(z, "dp", [(i, i ^ 2) for i in range(NDP_FAST)])
    b = lax.ppermute(z, "dp", [(i, i ^ 4) for i in range(NDP_FAST)])
    send = jnp.where(c == 0, b, a)
    diag = lax.ppermute(
        send, "dp", [(i, i ^ 2) if i % 2 == 0 else (i, i ^ 4) for i in range(NDP_FAST)]
    )
    mine = jnp.stack([z, a, b, diag])
    sib = lax.ppermute(mine, "dp", [(i, i ^ 1) for i in range(NDP_FAST)])
    return jnp.stack([mine[0], sib[0], mine[1], sib[1], mine[2], sib[2], mine[3], sib[3]])


def _take(x, idx, axis):
    return jnp.take(x, idx, axis=axis, mode="wrap")


def _z_gather(piece):
    f = lax.axis_index("fsdp")
    slots = [piece] + [
        lax.ppermute(piece, "fsdp", [(i, (i + k) % NF_FAST) for i in range(NF_FAST)])
        for k in range(1, NF_FAST)
    ]
    return _take(jnp.stack(slots), (f - jnp.arange(NF_FAST, dtype=jnp.int32)) % NF_FAST, 0)


def _gather_matrix(m):
    d = lax.axis_index("dp")
    j, c = d // 2, d % 2
    rows, cols = m.shape[0] // (NDP_FAST // 2), m.shape[1] // 2
    piece = lax.dynamic_slice(m, (j * rows, c * cols), (rows, cols))
    z = _z_gather(piece)
    x = lax.all_gather(z, "dp", axis=1, tiled=False)
    x = x.reshape(NF_FAST, NDP_FAST // 2, 2, rows, cols)
    x = jnp.concatenate([x[:, :, 0], x[:, :, 1]], axis=-1)
    return x.reshape(NF_FAST * m.shape[0], m.shape[1])


def _gather_rows(m):
    d = lax.axis_index("dp")
    rows = m.shape[0] // NDP_FAST
    z = _z_gather(lax.dynamic_slice_in_dim(m, d * rows, rows, 0))
    x = _take(_plane_gather(z), jnp.arange(NDP_FAST, dtype=jnp.int32) ^ d, 0)
    return x.transpose(1, 0, 2, 3).reshape(NF_FAST * m.shape[0], m.shape[1])


def fast_gather(mats, gains):
    out = [_gather_matrix(m) for m in mats[:-1]] + [_gather_rows(mats[-1])]
    stacked = jnp.concatenate(gains, axis=0)
    z = _z_gather(stacked)
    full = z.transpose(1, 0, 2).reshape(stacked.shape[0], NF_FAST * stacked.shape[1])
    rows = 0
    for g in gains:
        out.append(full[rows : rows + g.shape[0]])
        rows += g.shape[0]
    return out


def _reduce_matrix(g):
    d = lax.axis_index("dp")
    f = lax.axis_index("fsdp")
    j, c = d // 2, d % 2
    n_chips = NDP_FAST // 2
    rows, cols = g.shape[0] // (NF_FAST * n_chips), g.shape[1] // 2

    def half(which):
        part = lax.dynamic_slice_in_dim(g, which * cols, cols, 1)
        return part.reshape(NF_FAST, n_chips, rows, cols)

    got = lax.ppermute(half(1 - c).astype(jnp.bfloat16), "dp", [(i, i ^ 1) for i in range(NDP_FAST)])
    chip = half(c) + got.astype(jnp.float32)

    def of_chip(k):
        return lax.dynamic_index_in_dim(chip, k, 1, keepdims=False)

    moved = lax.ppermute(
        of_chip(j ^ 3).astype(jnp.bfloat16),
        "dp",
        [(i, i ^ 2) if i % 2 == 0 else (i, i ^ 4) for i in range(NDP_FAST)],
    ).astype(jnp.float32)
    to_x = of_chip(j ^ 1) + jnp.where(c == 1, moved, 0.0)
    to_y = of_chip(j ^ 2) + jnp.where(c == 0, moved, 0.0)
    from_x = lax.ppermute(to_x.astype(jnp.bfloat16), "dp", [(i, i ^ 2) for i in range(NDP_FAST)])
    from_y = lax.ppermute(to_y.astype(jnp.bfloat16), "dp", [(i, i ^ 4) for i in range(NDP_FAST)])
    plane = of_chip(j) + from_x.astype(jnp.float32) + from_y.astype(jnp.float32)
    total = lax.dynamic_index_in_dim(plane, f, 0, keepdims=False)
    for k in range(1, NF_FAST):
        part = lax.dynamic_index_in_dim(plane, (f + k) % NF_FAST, 0, keepdims=False)
        total = total + lax.ppermute(
            part.astype(jnp.bfloat16), "fsdp", [(i, (i + k) % NF_FAST) for i in range(NF_FAST)]
        ).astype(jnp.float32)
    x = lax.all_gather(total, "dp", axis=0, tiled=False)
    x = x.reshape(n_chips, 2, rows, cols)
    x = jnp.concatenate([x[:, 0], x[:, 1]], axis=-1)
    return x.reshape(n_chips * rows, 2 * cols)


def fast_reduce(mats, gains):
    stacked = jnp.concatenate(gains, axis=0)
    pad = 2 * LANES - stacked.shape[0]
    first = jnp.concatenate([mats[0], jnp.pad(stacked.T, ((0, 0), (0, pad)))], axis=1)
    shard = _reduce_matrix(first)
    width = mats[0].shape[1]
    out = [shard[:, :width]] + [_reduce_matrix(m) for m in mats[1:]]
    mine = shard[:, width : width + stacked.shape[0]].T
    rows = 0
    for g in gains:
        out.append(mine[rows : rows + g.shape[0]])
        rows += g.shape[0]
    return out


def map_blocks(fn, members):
    if members[0].shape[0] == 1:
        return jax.tree.map(lambda v: v[None], fn(tuple(m[0] for m in members)))
    return lax.map(fn, members)


def on_device(fast, *args):
    return layer(fast, *args)


def layer(
    fast, tokens, image_lengths, w_qkv, w_out, w_up, w_down, ln_gain, ln_bias, qk_gain, cotangent
):
    if fast:
        full_qkv, full_out, full_up, full_down, gain_all, bias_all, qk_all = fast_gather(
            (w_qkv, w_out, w_up, w_down), (ln_gain, ln_bias, qk_gain)
        )
    else:
        full_qkv, full_out, full_up, full_down, gain_all, bias_all, qk_all = (
            lax.all_gather(w_qkv, "fsdp", axis=0, tiled=True),
            lax.all_gather(w_out, "fsdp", axis=0, tiled=True),
            lax.all_gather(w_up, "fsdp", axis=0, tiled=True),
            lax.all_gather(w_down, "fsdp", axis=0, tiled=True),
            lax.all_gather(ln_gain, "fsdp", axis=1, tiled=True),
            lax.all_gather(ln_bias, "fsdp", axis=1, tiled=True),
            lax.all_gather(qk_gain, "fsdp", axis=1, tiled=True),
        )
    length = tokens.shape[0]
    model_width = tokens.shape[1]
    blocks = length // PATCH_BIG
    scaling = HEAD_DIM ** (-0.5)
    position = jnp.arange(length, dtype=jnp.int32)
    limits = jnp.cumsum(image_lengths[0])
    segment = jnp.sum((position[:, None] >= limits[None, :]).astype(jnp.int32), axis=1)
    valid_rows = (position < limits[-1]).astype(jnp.float32)[:, None]
    norm_gains = gain_all.astype(jnp.float32)
    biases = bias_all.astype(jnp.float32)
    qk_gains = qk_all.astype(jnp.float32).reshape(2, HEADS, HEAD_DIM)
    inputs = tokens.astype(jnp.float32)
    normed, first_back = jax.vjp(layer_norm, inputs, norm_gains[0], biases[0])
    normed_low = normed.astype(jnp.bfloat16)
    project = jnp.dot(normed_low, full_qkv, preferred_element_type=jnp.float32)
    queries = project[:, :model_width].reshape(length, HEADS, HEAD_DIM)
    keys_raw = project[:, model_width : 2 * model_width].reshape(length, HEADS, HEAD_DIM)
    values_raw = project[:, 2 * model_width :]
    (q_norm, k_norm), norms_back = jax.vjp(both_norms, queries, keys_raw, qk_gains[0], qk_gains[1])
    q_low = q_norm.astype(jnp.bfloat16).reshape(blocks, PATCH_BIG, HEADS, HEAD_DIM)
    k_low = k_norm.astype(jnp.bfloat16).reshape(blocks, PATCH_BIG, HEADS, HEAD_DIM)
    v_low = values_raw.astype(jnp.bfloat16).reshape(blocks, PATCH_BIG, HEADS, HEAD_DIM)
    s_blocks = segment.reshape(blocks, PATCH_BIG)

    def block_scores(q_block, k_block, s_block):
        scores = (
            jnp.einsum("qhd,khd->hqk", q_block, k_block, preferred_element_type=jnp.float32)
            * scaling
        )
        return jnp.where((s_block[:, None] == s_block[None, :])[None], scores, -1e30)

    def attend(members):
        q_block, k_block, v_block, s_block = members
        scores = block_scores(q_block, k_block, s_block)
        row_top = jnp.max(scores, axis=-1, keepdims=True)
        exp_scores = jnp.exp(scores - row_top)
        row_total = jnp.sum(exp_scores, axis=-1, keepdims=True)
        probability = (exp_scores / row_total).astype(jnp.bfloat16)
        mixed_block = jnp.einsum(
            "hqk,khd->qhd", probability, v_block, preferred_element_type=jnp.float32
        )
        return (mixed_block, row_top + jnp.log(row_total))

    mixed_heads, log_total = lax.map(attend, (q_low, k_low, v_low, s_blocks))
    mixed_low = mixed_heads.reshape(length, model_width).astype(jnp.bfloat16)
    residual = inputs + jnp.dot(mixed_low, full_out, preferred_element_type=jnp.float32)
    second, second_back = jax.vjp(layer_norm, residual, norm_gains[1], biases[1])
    second_low = second.astype(jnp.bfloat16)
    up_pre = jnp.dot(second_low, full_up, preferred_element_type=jnp.float32)
    active, gelu_back = jax.vjp(partial(jax.nn.gelu, approximate=False), up_pre)
    active_low = active.astype(jnp.bfloat16)
    output = residual + jnp.dot(active_low, full_down, preferred_element_type=jnp.float32)
    layer_out = (valid_rows * output).astype(jnp.bfloat16)
    back_qkv, back_out, back_up, back_down = full_qkv, full_out, full_up, full_down
    upstream = cotangent.astype(jnp.float32) * valid_rows
    up_low = upstream.astype(jnp.bfloat16)
    grad_down = jnp.dot(active_low.T, up_low, preferred_element_type=jnp.float32)
    grad_active = jnp.dot(up_low, back_down.T, preferred_element_type=jnp.float32)
    (grad_pre,) = gelu_back(grad_active)
    pre_low = grad_pre.astype(jnp.bfloat16)
    grad_up = jnp.dot(second_low.T, pre_low, preferred_element_type=jnp.float32)
    if fast:
        early = [_reduce_matrix(grad_up), _reduce_matrix(grad_down)]
    grad_second = jnp.dot(pre_low, back_up.T, preferred_element_type=jnp.float32)
    grad_resid, gain_two, bias_two = second_back(grad_second)
    grad_resid = grad_resid + upstream
    resid_low = grad_resid.astype(jnp.bfloat16)
    grad_outw = jnp.dot(mixed_low.T, resid_low, preferred_element_type=jnp.float32)
    grad_mixed = jnp.dot(resid_low, back_out.T, preferred_element_type=jnp.float32)
    grad_mixed = grad_mixed.astype(jnp.bfloat16).reshape(blocks, PATCH_BIG, HEADS, HEAD_DIM)

    def attend_back(members):
        q_block, k_block, v_block, s_block, l_block, d_block = members
        scores = block_scores(q_block, k_block, s_block)
        probability = jnp.exp(scores - l_block)
        prob_low = probability.astype(jnp.bfloat16)
        grad_v = jnp.einsum("hqk,qhd->khd", prob_low, d_block, preferred_element_type=jnp.float32)
        grad_p = jnp.einsum("qhd,khd->hqk", d_block, v_block, preferred_element_type=jnp.float32)
        grad_p = lax.optimization_barrier(grad_p.astype(jnp.bfloat16)).astype(jnp.float32)
        grad_s = probability * (grad_p - jnp.sum(probability * grad_p, axis=-1, keepdims=True))
        s_low = grad_s.astype(jnp.bfloat16)
        grad_q = (
            jnp.einsum("hqk,khd->qhd", s_low, k_block, preferred_element_type=jnp.float32) * scaling
        )
        grad_k = (
            jnp.einsum("hqk,qhd->khd", s_low, q_block, preferred_element_type=jnp.float32) * scaling
        )
        return (grad_q, grad_k, grad_v)

    grad_qn, grad_kn, grad_vn = map_blocks(
        attend_back, (q_low, k_low, v_low, s_blocks, log_total, grad_mixed)
    )
    grad_q, grad_k, gain_q, gain_k = norms_back(
        (grad_qn.reshape(length, HEADS, HEAD_DIM), grad_kn.reshape(length, HEADS, HEAD_DIM))
    )
    grad_project = jnp.concatenate(
        [
            grad_q.reshape(length, model_width),
            grad_k.reshape(length, model_width),
            grad_vn.reshape(length, model_width),
        ],
        axis=1,
    ).astype(jnp.bfloat16)
    grad_qkv = jnp.dot(normed_low.T, grad_project, preferred_element_type=jnp.float32)
    grad_normed = jnp.dot(grad_project, back_qkv.T, preferred_element_type=jnp.float32)
    grad_input, gain_one, bias_one = first_back(grad_normed)
    grad_tokens = (grad_input + grad_resid).astype(jnp.bfloat16)
    grad_gain = jnp.stack([gain_one, gain_two])
    grad_bias = jnp.stack([bias_one, bias_two])
    grad_qk = jnp.stack([gain_q.reshape(model_width), gain_k.reshape(model_width)])
    summands = (grad_qkv, grad_outw, grad_up, grad_down, grad_gain, grad_bias, grad_qk)
    if fast:
        late = fast_reduce(summands[:2], summands[4:])
        shares = late[:2] + early + late[2:]
    else:
        pieces = [
            lax.psum_scatter(
                s.astype(jnp.bfloat16), "fsdp", scatter_dimension=0 if k < 4 else 1, tiled=True
            ).astype(jnp.float32)
            for k, s in enumerate(summands)
        ]
        shares = [lax.psum(p.astype(jnp.bfloat16), "dp").astype(jnp.float32) for p in pieces]
    return (
        layer_out,
        grad_tokens,
        shares[0],
        shares[1],
        shares[2],
        shares[3],
        shares[4],
        shares[5],
        shares[6],
    )


def solution(mesh):
    in_specs = (
        P(("dp", "fsdp"), None),
        P(("dp", "fsdp"), None),
        P("fsdp", None),
        P("fsdp", None),
        P("fsdp", None),
        P("fsdp", None),
        P(None, "fsdp"),
        P(None, "fsdp"),
        P(None, "fsdp"),
        P(("dp", "fsdp"), None),
    )
    out_specs = (
        P(("dp", "fsdp"), None),
        P(("dp", "fsdp"), None),
        P("fsdp", None),
        P("fsdp", None),
        P("fsdp", None),
        P("fsdp", None),
        P(None, "fsdp"),
        P(None, "fsdp"),
        P(None, "fsdp"),
    )
    fast = dict(mesh.shape) == {"dp": NDP_FAST, "fsdp": NF_FAST}
    return jax.shard_map(
        partial(on_device, fast), mesh=mesh, in_specs=in_specs, out_specs=out_specs, check_vma=False
    )
```

```python
from functools import partial

import jax
import jax.numpy as jnp
from jax import lax
from jax.sharding import PartitionSpec as P


HEADS = 12
HEAD_DIM = 64
PATCH_BIG = 576


epsilon = 1e-06


def layer_norm(v, gain_row, bias_row):
    centre = v - jnp.mean(v, axis=-1, keepdims=True)
    spread = jnp.mean(centre * centre, axis=-1, keepdims=True)
    return centre * lax.rsqrt(spread + epsilon) * gain_row + bias_row


def head_norm(v, gain_row):
    centre = v - jnp.mean(v, axis=-1, keepdims=True)
    spread = jnp.mean(centre * centre, axis=-1, keepdims=True)
    return centre * lax.rsqrt(spread + epsilon) * gain_row


def both_norms(q_in, k_in, q_gain, k_gain):
    return (head_norm(q_in, q_gain), head_norm(k_in, k_gain))


NF_FAST = 4
NDP_FAST = 8


LANES = 128


def _take(x, idx, axis):
    return jnp.take(x, idx, axis=axis, mode="wrap")


def _z_gather(piece):
    f = lax.axis_index("fsdp")
    slots = [piece] + [
        lax.ppermute(piece, "fsdp", [(i, (i + k) % NF_FAST) for i in range(NF_FAST)])
        for k in range(1, NF_FAST)
    ]
    return _take(jnp.stack(slots), (f - jnp.arange(NF_FAST, dtype=jnp.int32)) % NF_FAST, 0)


def _gather_matrix(m):
    d = lax.axis_index("dp")
    j, c = d // 2, d % 2
    rows, cols = m.shape[0] // (NDP_FAST // 2), m.shape[1] // 2
    piece = lax.dynamic_slice(m, (j * rows, c * cols), (rows, cols))
    z = _z_gather(piece)
    x = lax.all_gather(z, "dp", axis=1, tiled=False)
    x = x.reshape(NF_FAST, NDP_FAST // 2, 2, rows, cols)
    x = jnp.concatenate([x[:, :, 0], x[:, :, 1]], axis=-1)
    return x.reshape(NF_FAST * m.shape[0], m.shape[1])


def _gather_side_by_side(mats):
    d = lax.axis_index("dp")
    j, c = d // 2, d % 2
    n_chips = NDP_FAST // 2
    rows = mats[0].shape[0] // n_chips
    halves = [m.shape[1] // 2 for m in mats]
    piece = jnp.concatenate(
        [lax.dynamic_slice(m, (j * rows, c * h), (rows, h)) for m, h in zip(mats, halves)], axis=1
    )
    x = lax.all_gather(_z_gather(piece), "dp", axis=1, tiled=False)
    x = x.reshape(NF_FAST, n_chips, 2, rows, sum(halves))
    out = []
    offset = 0
    for m, h in zip(mats, halves):
        part = x[..., offset : offset + h]
        full = jnp.concatenate([part[:, :, 0], part[:, :, 1]], axis=-1)
        out.append(full.reshape(NF_FAST * m.shape[0], m.shape[1]))
        offset += h
    return out


def fast_gather(mats, gains):
    out = _gather_side_by_side(mats[:2]) + [_gather_matrix(m) for m in mats[2:]]
    stacked = jnp.concatenate(gains, axis=0)
    z = _z_gather(stacked)
    full = z.transpose(1, 0, 2).reshape(stacked.shape[0], NF_FAST * stacked.shape[1])
    rows = 0
    for g in gains:
        out.append(full[rows : rows + g.shape[0]])
        rows += g.shape[0]
    return out


def _reduce_matrix(g):
    d = lax.axis_index("dp")
    f = lax.axis_index("fsdp")
    j, c = d // 2, d % 2
    n_chips = NDP_FAST // 2
    rows, cols = g.shape[0] // (NF_FAST * n_chips), g.shape[1] // 2

    def half(which):
        part = lax.dynamic_slice_in_dim(g, which * cols, cols, 1)
        return part.reshape(NF_FAST, n_chips, rows, cols)

    got = lax.ppermute(half(1 - c).astype(jnp.bfloat16), "dp", [(i, i ^ 1) for i in range(NDP_FAST)])
    chip = half(c) + got.astype(jnp.float32)

    def of_chip(k):
        return lax.dynamic_index_in_dim(chip, k, 1, keepdims=False)

    moved = lax.ppermute(
        of_chip(j ^ 3).astype(jnp.bfloat16),
        "dp",
        [(i, i ^ 2) if i % 2 == 0 else (i, i ^ 4) for i in range(NDP_FAST)],
    ).astype(jnp.float32)
    to_x = of_chip(j ^ 1) + jnp.where(c == 1, moved, 0.0)
    to_y = of_chip(j ^ 2) + jnp.where(c == 0, moved, 0.0)
    from_x = lax.ppermute(to_x.astype(jnp.bfloat16), "dp", [(i, i ^ 2) for i in range(NDP_FAST)])
    from_y = lax.ppermute(to_y.astype(jnp.bfloat16), "dp", [(i, i ^ 4) for i in range(NDP_FAST)])
    plane = of_chip(j) + from_x.astype(jnp.float32) + from_y.astype(jnp.float32)
    total = lax.dynamic_index_in_dim(plane, f, 0, keepdims=False)
    for k in range(1, NF_FAST):
        part = lax.dynamic_index_in_dim(plane, (f + k) % NF_FAST, 0, keepdims=False)
        total = total + lax.ppermute(
            part.astype(jnp.bfloat16), "fsdp", [(i, (i + k) % NF_FAST) for i in range(NF_FAST)]
        ).astype(jnp.float32)
    x = lax.all_gather(total, "dp", axis=0, tiled=False)
    x = x.reshape(n_chips, 2, rows, cols)
    x = jnp.concatenate([x[:, 0], x[:, 1]], axis=-1)
    return x.reshape(n_chips * rows, 2 * cols)


def fast_reduce(mats, gains):
    stacked = jnp.concatenate(gains, axis=0)
    pad = 2 * LANES - stacked.shape[0]
    first = jnp.concatenate([mats[0], jnp.pad(stacked.T, ((0, 0), (0, pad)))], axis=1)
    shard = _reduce_matrix(first)
    width = mats[0].shape[1]
    out = [shard[:, :width]] + [_reduce_matrix(m) for m in mats[1:]]
    mine = shard[:, width : width + stacked.shape[0]].T
    rows = 0
    for g in gains:
        out.append(mine[rows : rows + g.shape[0]])
        rows += g.shape[0]
    return out


def map_blocks(fn, members):
    if members[0].shape[0] == 1:
        return jax.tree.map(lambda v: v[None], fn(tuple(m[0] for m in members)))
    return lax.map(fn, members)


def on_device(fast, *args):
    return layer(fast, *args)


def layer(
    fast, tokens, image_lengths, w_qkv, w_out, w_up, w_down, ln_gain, ln_bias, qk_gain, cotangent
):
    if fast:
        full_qkv, full_out, full_up, full_down, gain_all, bias_all, qk_all = fast_gather(
            (w_qkv, w_out, w_up, w_down), (ln_gain, ln_bias, qk_gain)
        )
    else:
        full_qkv, full_out, full_up, full_down, gain_all, bias_all, qk_all = (
            lax.all_gather(w_qkv, "fsdp", axis=0, tiled=True),
            lax.all_gather(w_out, "fsdp", axis=0, tiled=True),
            lax.all_gather(w_up, "fsdp", axis=0, tiled=True),
            lax.all_gather(w_down, "fsdp", axis=0, tiled=True),
            lax.all_gather(ln_gain, "fsdp", axis=1, tiled=True),
            lax.all_gather(ln_bias, "fsdp", axis=1, tiled=True),
            lax.all_gather(qk_gain, "fsdp", axis=1, tiled=True),
        )
    length = tokens.shape[0]
    model_width = tokens.shape[1]
    blocks = length // PATCH_BIG
    scaling = HEAD_DIM ** (-0.5)
    position = jnp.arange(length, dtype=jnp.int32)
    limits = jnp.cumsum(image_lengths[0])
    segment = jnp.sum((position[:, None] >= limits[None, :]).astype(jnp.int32), axis=1)
    valid_rows = (position < limits[-1]).astype(jnp.float32)[:, None]
    norm_gains = gain_all.astype(jnp.float32)
    biases = bias_all.astype(jnp.float32)
    qk_gains = qk_all.astype(jnp.float32).reshape(2, HEADS, HEAD_DIM)
    inputs = tokens.astype(jnp.float32)
    normed, first_back = jax.vjp(layer_norm, inputs, norm_gains[0], biases[0])
    normed_low = normed.astype(jnp.bfloat16)
    project = jnp.dot(normed_low, full_qkv, preferred_element_type=jnp.float32)
    queries = project[:, :model_width].reshape(length, HEADS, HEAD_DIM)
    keys_raw = project[:, model_width : 2 * model_width].reshape(length, HEADS, HEAD_DIM)
    values_raw = project[:, 2 * model_width :]
    (q_norm, k_norm), norms_back = jax.vjp(both_norms, queries, keys_raw, qk_gains[0], qk_gains[1])
    q_low = q_norm.astype(jnp.bfloat16).reshape(blocks, PATCH_BIG, HEADS, HEAD_DIM)
    k_low = k_norm.astype(jnp.bfloat16).reshape(blocks, PATCH_BIG, HEADS, HEAD_DIM)
    v_low = values_raw.astype(jnp.bfloat16).reshape(blocks, PATCH_BIG, HEADS, HEAD_DIM)
    s_blocks = segment.reshape(blocks, PATCH_BIG)

    def block_scores(q_block, k_block, s_block):
        scores = (
            jnp.einsum("qhd,khd->hqk", q_block, k_block, preferred_element_type=jnp.float32)
            * scaling
        )
        return jnp.where((s_block[:, None] == s_block[None, :])[None], scores, -1e30)

    def attend(members):
        q_block, k_block, v_block, s_block = members
        scores = block_scores(q_block, k_block, s_block)
        row_top = jnp.max(scores, axis=-1, keepdims=True)
        exp_scores = jnp.exp(scores - row_top)
        row_total = jnp.sum(exp_scores, axis=-1, keepdims=True)
        probability = (exp_scores / row_total).astype(jnp.bfloat16)
        mixed_block = jnp.einsum(
            "hqk,khd->qhd", probability, v_block, preferred_element_type=jnp.float32
        )
        return (mixed_block, row_top + jnp.log(row_total))

    mixed_heads, log_total = lax.map(attend, (q_low, k_low, v_low, s_blocks))
    mixed_low = mixed_heads.reshape(length, model_width).astype(jnp.bfloat16)
    residual = inputs + jnp.dot(mixed_low, full_out, preferred_element_type=jnp.float32)
    second, second_back = jax.vjp(layer_norm, residual, norm_gains[1], biases[1])
    second_low = second.astype(jnp.bfloat16)
    up_pre = jnp.dot(second_low, full_up, preferred_element_type=jnp.float32)
    active, gelu_back = jax.vjp(partial(jax.nn.gelu, approximate=False), up_pre)
    active_low = active.astype(jnp.bfloat16)
    output = residual + jnp.dot(active_low, full_down, preferred_element_type=jnp.float32)
    layer_out = (valid_rows * output).astype(jnp.bfloat16)
    back_qkv, back_out, back_up, back_down = full_qkv, full_out, full_up, full_down
    upstream = cotangent.astype(jnp.float32) * valid_rows
    up_low = upstream.astype(jnp.bfloat16)
    grad_down = jnp.dot(active_low.T, up_low, preferred_element_type=jnp.float32)
    grad_active = jnp.dot(up_low, back_down.T, preferred_element_type=jnp.float32)
    (grad_pre,) = gelu_back(grad_active)
    pre_low = grad_pre.astype(jnp.bfloat16)
    grad_up = jnp.dot(second_low.T, pre_low, preferred_element_type=jnp.float32)
    if fast:
        early = [_reduce_matrix(grad_up), _reduce_matrix(grad_down)]
    grad_second = jnp.dot(pre_low, back_up.T, preferred_element_type=jnp.float32)
    grad_resid, gain_two, bias_two = second_back(grad_second)
    grad_resid = grad_resid + upstream
    resid_low = grad_resid.astype(jnp.bfloat16)
    grad_outw = jnp.dot(mixed_low.T, resid_low, preferred_element_type=jnp.float32)
    grad_mixed = jnp.dot(resid_low, back_out.T, preferred_element_type=jnp.float32)
    grad_mixed = grad_mixed.astype(jnp.bfloat16).reshape(blocks, PATCH_BIG, HEADS, HEAD_DIM)

    def attend_back(members):
        q_block, k_block, v_block, s_block, l_block, d_block = members
        scores = block_scores(q_block, k_block, s_block)
        probability = jnp.exp(scores - l_block)
        prob_low = probability.astype(jnp.bfloat16)
        grad_v = jnp.einsum("hqk,qhd->khd", prob_low, d_block, preferred_element_type=jnp.float32)
        grad_p = jnp.einsum("qhd,khd->hqk", d_block, v_block, preferred_element_type=jnp.float32)
        grad_p = lax.optimization_barrier(grad_p.astype(jnp.bfloat16)).astype(jnp.float32)
        grad_s = probability * (grad_p - jnp.sum(probability * grad_p, axis=-1, keepdims=True))
        s_low = grad_s.astype(jnp.bfloat16)
        grad_q = (
            jnp.einsum("hqk,khd->qhd", s_low, k_block, preferred_element_type=jnp.float32) * scaling
        )
        grad_k = (
            jnp.einsum("hqk,qhd->khd", s_low, q_block, preferred_element_type=jnp.float32) * scaling
        )
        return (grad_q, grad_k, grad_v)

    grad_qn, grad_kn, grad_vn = map_blocks(
        attend_back, (q_low, k_low, v_low, s_blocks, log_total, grad_mixed)
    )
    grad_q, grad_k, gain_q, gain_k = norms_back(
        (grad_qn.reshape(length, HEADS, HEAD_DIM), grad_kn.reshape(length, HEADS, HEAD_DIM))
    )
    grad_project = jnp.concatenate(
        [
            grad_q.reshape(length, model_width),
            grad_k.reshape(length, model_width),
            grad_vn.reshape(length, model_width),
        ],
        axis=1,
    ).astype(jnp.bfloat16)
    grad_qkv = jnp.dot(normed_low.T, grad_project, preferred_element_type=jnp.float32)
    grad_normed = jnp.dot(grad_project, back_qkv.T, preferred_element_type=jnp.float32)
    grad_input, gain_one, bias_one = first_back(grad_normed)
    grad_tokens = (grad_input + grad_resid).astype(jnp.bfloat16)
    grad_gain = jnp.stack([gain_one, gain_two])
    grad_bias = jnp.stack([bias_one, bias_two])
    grad_qk = jnp.stack([gain_q.reshape(model_width), gain_k.reshape(model_width)])
    summands = (grad_qkv, grad_outw, grad_up, grad_down, grad_gain, grad_bias, grad_qk)
    if fast:
        late = fast_reduce(summands[:2], summands[4:])
        shares = late[:2] + early + late[2:]
    else:
        pieces = [
            lax.psum_scatter(
                s.astype(jnp.bfloat16), "fsdp", scatter_dimension=0 if k < 4 else 1, tiled=True
            ).astype(jnp.float32)
            for k, s in enumerate(summands)
        ]
        shares = [lax.psum(p.astype(jnp.bfloat16), "dp").astype(jnp.float32) for p in pieces]
    return (
        layer_out,
        grad_tokens,
        shares[0],
        shares[1],
        shares[2],
        shares[3],
        shares[4],
        shares[5],
        shares[6],
    )


def solution(mesh):
    in_specs = (
        P(("dp", "fsdp"), None),
        P(("dp", "fsdp"), None),
        P("fsdp", None),
        P("fsdp", None),
        P("fsdp", None),
        P("fsdp", None),
        P(None, "fsdp"),
        P(None, "fsdp"),
        P(None, "fsdp"),
        P(("dp", "fsdp"), None),
    )
    out_specs = (
        P(("dp", "fsdp"), None),
        P(("dp", "fsdp"), None),
        P("fsdp", None),
        P("fsdp", None),
        P("fsdp", None),
        P("fsdp", None),
        P(None, "fsdp"),
        P(None, "fsdp"),
        P(None, "fsdp"),
    )
    fast = dict(mesh.shape) == {"dp": NDP_FAST, "fsdp": NF_FAST}
    return jax.shard_map(
        partial(on_device, fast), mesh=mesh, in_specs=in_specs, out_specs=out_specs, check_vma=False
    )
```

```python
from functools import partial

import jax
import jax.numpy as jnp
from jax import lax
from jax.sharding import PartitionSpec as P


HEADS = 12
HEAD_DIM = 64
PATCH_BIG = 576


epsilon = 1e-06


def layer_norm(v, gain_row, bias_row):
    centre = v - jnp.mean(v, axis=-1, keepdims=True)
    spread = jnp.mean(centre * centre, axis=-1, keepdims=True)
    return centre * lax.rsqrt(spread + epsilon) * gain_row + bias_row


def head_norm(v, gain_row):
    centre = v - jnp.mean(v, axis=-1, keepdims=True)
    spread = jnp.mean(centre * centre, axis=-1, keepdims=True)
    return centre * lax.rsqrt(spread + epsilon) * gain_row


def both_norms(q_in, k_in, q_gain, k_gain):
    return (head_norm(q_in, q_gain), head_norm(k_in, k_gain))


NF_FAST = 4
NDP_FAST = 8


LANES = 128


def _take(x, idx, axis):
    return jnp.take(x, idx, axis=axis, mode="wrap")


def _z_gather(piece):
    f = lax.axis_index("fsdp")
    slots = [piece] + [
        lax.ppermute(piece, "fsdp", [(i, (i + k) % NF_FAST) for i in range(NF_FAST)])
        for k in range(1, NF_FAST)
    ]
    return _take(jnp.stack(slots), (f - jnp.arange(NF_FAST, dtype=jnp.int32)) % NF_FAST, 0)


def _gather_matrix(m):
    d = lax.axis_index("dp")
    j, c = d // 2, d % 2
    rows, cols = m.shape[0] // (NDP_FAST // 2), m.shape[1] // 2
    piece = lax.dynamic_slice(m, (j * rows, c * cols), (rows, cols))
    z = _z_gather(piece)
    x = lax.all_gather(z, "dp", axis=1, tiled=False)
    x = x.reshape(NF_FAST, NDP_FAST // 2, 2, rows, cols)
    x = jnp.concatenate([x[:, :, 0], x[:, :, 1]], axis=-1)
    return x.reshape(NF_FAST * m.shape[0], m.shape[1])


def fast_gather(mats, gains):
    out = [_gather_matrix(m) for m in mats]
    stacked = jnp.concatenate(gains, axis=0)
    z = _z_gather(stacked)
    full = z.transpose(1, 0, 2).reshape(stacked.shape[0], NF_FAST * stacked.shape[1])
    rows = 0
    for g in gains:
        out.append(full[rows : rows + g.shape[0]])
        rows += g.shape[0]
    return out


def _reduce_matrix(g):
    d = lax.axis_index("dp")
    f = lax.axis_index("fsdp")
    j, c = d // 2, d % 2
    n_chips = NDP_FAST // 2
    rows, cols = g.shape[0] // (NF_FAST * n_chips), g.shape[1] // 2

    def half(which):
        part = lax.dynamic_slice_in_dim(g, which * cols, cols, 1)
        return part.reshape(NF_FAST, n_chips, rows, cols)

    got = lax.ppermute(half(1 - c).astype(jnp.bfloat16), "dp", [(i, i ^ 1) for i in range(NDP_FAST)])
    chip = half(c) + got.astype(jnp.float32)

    def of_chip(k):
        return lax.dynamic_index_in_dim(chip, k, 1, keepdims=False)

    moved = lax.ppermute(
        of_chip(j ^ 3).astype(jnp.bfloat16),
        "dp",
        [(i, i ^ 2) if i % 2 == 0 else (i, i ^ 4) for i in range(NDP_FAST)],
    ).astype(jnp.float32)
    to_x = of_chip(j ^ 1) + jnp.where(c == 1, moved, 0.0)
    to_y = of_chip(j ^ 2) + jnp.where(c == 0, moved, 0.0)
    from_x = lax.ppermute(to_x.astype(jnp.bfloat16), "dp", [(i, i ^ 2) for i in range(NDP_FAST)])
    from_y = lax.ppermute(to_y.astype(jnp.bfloat16), "dp", [(i, i ^ 4) for i in range(NDP_FAST)])
    plane = of_chip(j) + from_x.astype(jnp.float32) + from_y.astype(jnp.float32)
    total = lax.dynamic_index_in_dim(plane, f, 0, keepdims=False)
    for k in range(1, NF_FAST):
        part = lax.dynamic_index_in_dim(plane, (f + k) % NF_FAST, 0, keepdims=False)
        total = total + lax.ppermute(
            part.astype(jnp.bfloat16), "fsdp", [(i, (i + k) % NF_FAST) for i in range(NF_FAST)]
        ).astype(jnp.float32)
    return total


def _finish(totals):
    x = lax.all_gather(jnp.concatenate(totals, axis=1), "dp", axis=0, tiled=False)
    n_chips = NDP_FAST // 2
    rows = totals[0].shape[0]
    x = x.reshape(n_chips, 2, rows, x.shape[-1])
    out = []
    offset = 0
    for t in totals:
        part = x[..., offset : offset + t.shape[1]]
        full = jnp.concatenate([part[:, 0], part[:, 1]], axis=-1)
        out.append(full.reshape(n_chips * rows, 2 * t.shape[1]))
        offset += t.shape[1]
    return out


def _reduce_one(g):
    return _finish([_reduce_matrix(g)])[0]


def fast_reduce(mats, gains):
    stacked = jnp.concatenate(gains, axis=0)
    pad = 2 * LANES - stacked.shape[0]
    first = jnp.concatenate([mats[0], jnp.pad(stacked.T, ((0, 0), (0, pad)))], axis=1)
    shards = _finish([_reduce_matrix(first)] + [_reduce_matrix(m) for m in mats[1:]])
    shard = shards[0]
    width = mats[0].shape[1]
    out = [shard[:, :width]] + shards[1:]
    mine = shard[:, width : width + stacked.shape[0]].T
    rows = 0
    for g in gains:
        out.append(mine[rows : rows + g.shape[0]])
        rows += g.shape[0]
    return out


def map_blocks(fn, members):
    if members[0].shape[0] == 1:
        return jax.tree.map(lambda v: v[None], fn(tuple(m[0] for m in members)))
    return lax.map(fn, members)


def on_device(fast, *args):
    return layer(fast, *args)


def layer(
    fast, tokens, image_lengths, w_qkv, w_out, w_up, w_down, ln_gain, ln_bias, qk_gain, cotangent
):
    if fast:
        full_qkv, full_out, full_up, full_down, gain_all, bias_all, qk_all = fast_gather(
            (w_qkv, w_out, w_up, w_down), (ln_gain, ln_bias, qk_gain)
        )
    else:
        full_qkv, full_out, full_up, full_down, gain_all, bias_all, qk_all = (
            lax.all_gather(w_qkv, "fsdp", axis=0, tiled=True),
            lax.all_gather(w_out, "fsdp", axis=0, tiled=True),
            lax.all_gather(w_up, "fsdp", axis=0, tiled=True),
            lax.all_gather(w_down, "fsdp", axis=0, tiled=True),
            lax.all_gather(ln_gain, "fsdp", axis=1, tiled=True),
            lax.all_gather(ln_bias, "fsdp", axis=1, tiled=True),
            lax.all_gather(qk_gain, "fsdp", axis=1, tiled=True),
        )
    length = tokens.shape[0]
    model_width = tokens.shape[1]
    blocks = length // PATCH_BIG
    scaling = HEAD_DIM ** (-0.5)
    position = jnp.arange(length, dtype=jnp.int32)
    limits = jnp.cumsum(image_lengths[0])
    segment = jnp.sum((position[:, None] >= limits[None, :]).astype(jnp.int32), axis=1)
    valid_rows = (position < limits[-1]).astype(jnp.float32)[:, None]
    norm_gains = gain_all.astype(jnp.float32)
    biases = bias_all.astype(jnp.float32)
    qk_gains = qk_all.astype(jnp.float32).reshape(2, HEADS, HEAD_DIM)
    inputs = tokens.astype(jnp.float32)
    normed, first_back = jax.vjp(layer_norm, inputs, norm_gains[0], biases[0])
    normed_low = normed.astype(jnp.bfloat16)
    project = jnp.dot(normed_low, full_qkv, preferred_element_type=jnp.float32)
    queries = project[:, :model_width].reshape(length, HEADS, HEAD_DIM)
    keys_raw = project[:, model_width : 2 * model_width].reshape(length, HEADS, HEAD_DIM)
    values_raw = project[:, 2 * model_width :]
    (q_norm, k_norm), norms_back = jax.vjp(both_norms, queries, keys_raw, qk_gains[0], qk_gains[1])
    q_low = q_norm.astype(jnp.bfloat16).reshape(blocks, PATCH_BIG, HEADS, HEAD_DIM)
    k_low = k_norm.astype(jnp.bfloat16).reshape(blocks, PATCH_BIG, HEADS, HEAD_DIM)
    v_low = values_raw.astype(jnp.bfloat16).reshape(blocks, PATCH_BIG, HEADS, HEAD_DIM)
    s_blocks = segment.reshape(blocks, PATCH_BIG)

    def block_scores(q_block, k_block, s_block):
        scores = (
            jnp.einsum("qhd,khd->hqk", q_block, k_block, preferred_element_type=jnp.float32)
            * scaling
        )
        return jnp.where((s_block[:, None] == s_block[None, :])[None], scores, -1e30)

    def attend(members):
        q_block, k_block, v_block, s_block = members
        scores = block_scores(q_block, k_block, s_block)
        row_top = jnp.max(scores, axis=-1, keepdims=True)
        exp_scores = jnp.exp(scores - row_top)
        row_total = jnp.sum(exp_scores, axis=-1, keepdims=True)
        probability = (exp_scores / row_total).astype(jnp.bfloat16)
        mixed_block = jnp.einsum(
            "hqk,khd->qhd", probability, v_block, preferred_element_type=jnp.float32
        )
        return (mixed_block, row_top + jnp.log(row_total))

    mixed_heads, log_total = lax.map(attend, (q_low, k_low, v_low, s_blocks))
    mixed_low = mixed_heads.reshape(length, model_width).astype(jnp.bfloat16)
    residual = inputs + jnp.dot(mixed_low, full_out, preferred_element_type=jnp.float32)
    second, second_back = jax.vjp(layer_norm, residual, norm_gains[1], biases[1])
    second_low = second.astype(jnp.bfloat16)
    up_pre = jnp.dot(second_low, full_up, preferred_element_type=jnp.float32)
    active, gelu_back = jax.vjp(partial(jax.nn.gelu, approximate=False), up_pre)
    active_low = active.astype(jnp.bfloat16)
    output = residual + jnp.dot(active_low, full_down, preferred_element_type=jnp.float32)
    layer_out = (valid_rows * output).astype(jnp.bfloat16)
    back_qkv, back_out, back_up, back_down = full_qkv, full_out, full_up, full_down
    upstream = cotangent.astype(jnp.float32) * valid_rows
    up_low = upstream.astype(jnp.bfloat16)
    grad_down = jnp.dot(active_low.T, up_low, preferred_element_type=jnp.float32)
    grad_active = jnp.dot(up_low, back_down.T, preferred_element_type=jnp.float32)
    (grad_pre,) = gelu_back(grad_active)
    pre_low = grad_pre.astype(jnp.bfloat16)
    grad_up = jnp.dot(second_low.T, pre_low, preferred_element_type=jnp.float32)
    if fast:
        early = [_reduce_one(grad_up), _reduce_one(grad_down)]
    grad_second = jnp.dot(pre_low, back_up.T, preferred_element_type=jnp.float32)
    grad_resid, gain_two, bias_two = second_back(grad_second)
    grad_resid = grad_resid + upstream
    resid_low = grad_resid.astype(jnp.bfloat16)
    grad_outw = jnp.dot(mixed_low.T, resid_low, preferred_element_type=jnp.float32)
    grad_mixed = jnp.dot(resid_low, back_out.T, preferred_element_type=jnp.float32)
    grad_mixed = grad_mixed.astype(jnp.bfloat16).reshape(blocks, PATCH_BIG, HEADS, HEAD_DIM)

    def attend_back(members):
        q_block, k_block, v_block, s_block, l_block, d_block = members
        scores = block_scores(q_block, k_block, s_block)
        probability = jnp.exp(scores - l_block)
        prob_low = probability.astype(jnp.bfloat16)
        grad_v = jnp.einsum("hqk,qhd->khd", prob_low, d_block, preferred_element_type=jnp.float32)
        grad_p = jnp.einsum("qhd,khd->hqk", d_block, v_block, preferred_element_type=jnp.float32)
        grad_p = lax.optimization_barrier(grad_p.astype(jnp.bfloat16)).astype(jnp.float32)
        grad_s = probability * (grad_p - jnp.sum(probability * grad_p, axis=-1, keepdims=True))
        s_low = grad_s.astype(jnp.bfloat16)
        grad_q = (
            jnp.einsum("hqk,khd->qhd", s_low, k_block, preferred_element_type=jnp.float32) * scaling
        )
        grad_k = (
            jnp.einsum("hqk,qhd->khd", s_low, q_block, preferred_element_type=jnp.float32) * scaling
        )
        return (grad_q, grad_k, grad_v)

    grad_qn, grad_kn, grad_vn = map_blocks(
        attend_back, (q_low, k_low, v_low, s_blocks, log_total, grad_mixed)
    )
    grad_q, grad_k, gain_q, gain_k = norms_back(
        (grad_qn.reshape(length, HEADS, HEAD_DIM), grad_kn.reshape(length, HEADS, HEAD_DIM))
    )
    grad_project = jnp.concatenate(
        [
            grad_q.reshape(length, model_width),
            grad_k.reshape(length, model_width),
            grad_vn.reshape(length, model_width),
        ],
        axis=1,
    ).astype(jnp.bfloat16)
    grad_qkv = jnp.dot(normed_low.T, grad_project, preferred_element_type=jnp.float32)
    grad_normed = jnp.dot(grad_project, back_qkv.T, preferred_element_type=jnp.float32)
    grad_input, gain_one, bias_one = first_back(grad_normed)
    grad_tokens = (grad_input + grad_resid).astype(jnp.bfloat16)
    grad_gain = jnp.stack([gain_one, gain_two])
    grad_bias = jnp.stack([bias_one, bias_two])
    grad_qk = jnp.stack([gain_q.reshape(model_width), gain_k.reshape(model_width)])
    summands = (grad_qkv, grad_outw, grad_up, grad_down, grad_gain, grad_bias, grad_qk)
    if fast:
        late = fast_reduce(summands[:2], summands[4:])
        shares = late[:2] + early + late[2:]
    else:
        pieces = [
            lax.psum_scatter(
                s.astype(jnp.bfloat16), "fsdp", scatter_dimension=0 if k < 4 else 1, tiled=True
            ).astype(jnp.float32)
            for k, s in enumerate(summands)
        ]
        shares = [lax.psum(p.astype(jnp.bfloat16), "dp").astype(jnp.float32) for p in pieces]
    return (
        layer_out,
        grad_tokens,
        shares[0],
        shares[1],
        shares[2],
        shares[3],
        shares[4],
        shares[5],
        shares[6],
    )


def solution(mesh):
    in_specs = (
        P(("dp", "fsdp"), None),
        P(("dp", "fsdp"), None),
        P("fsdp", None),
        P("fsdp", None),
        P("fsdp", None),
        P("fsdp", None),
        P(None, "fsdp"),
        P(None, "fsdp"),
        P(None, "fsdp"),
        P(("dp", "fsdp"), None),
    )
    out_specs = (
        P(("dp", "fsdp"), None),
        P(("dp", "fsdp"), None),
        P("fsdp", None),
        P("fsdp", None),
        P("fsdp", None),
        P("fsdp", None),
        P(None, "fsdp"),
        P(None, "fsdp"),
        P(None, "fsdp"),
    )
    fast = dict(mesh.shape) == {"dp": NDP_FAST, "fsdp": NF_FAST}
    return jax.shard_map(
        partial(on_device, fast), mesh=mesh, in_specs=in_specs, out_specs=out_specs, check_vma=False
    )
```

```python
from functools import partial

import jax
import jax.numpy as jnp
from jax import lax
from jax.sharding import PartitionSpec as P


HEADS = 12
HEAD_DIM = 64
PATCH_BIG = 576


epsilon = 1e-06


def layer_norm(v, gain_row, bias_row):
    centre = v - jnp.mean(v, axis=-1, keepdims=True)
    spread = jnp.mean(centre * centre, axis=-1, keepdims=True)
    return centre * lax.rsqrt(spread + epsilon) * gain_row + bias_row


def head_norm(v, gain_row):
    centre = v - jnp.mean(v, axis=-1, keepdims=True)
    spread = jnp.mean(centre * centre, axis=-1, keepdims=True)
    return centre * lax.rsqrt(spread + epsilon) * gain_row


def both_norms(q_in, k_in, q_gain, k_gain):
    return (head_norm(q_in, q_gain), head_norm(k_in, k_gain))


NF_FAST = 4
NDP_FAST = 8


LANES = 128


def _plane_gather(z):
    d = lax.axis_index("dp")
    c = d % 2
    a = lax.ppermute(z, "dp", [(i, i ^ 2) for i in range(NDP_FAST)])
    b = lax.ppermute(z, "dp", [(i, i ^ 4) for i in range(NDP_FAST)])
    send = jnp.where(c == 0, b, a)
    diag = lax.ppermute(
        send, "dp", [(i, i ^ 2) if i % 2 == 0 else (i, i ^ 4) for i in range(NDP_FAST)]
    )
    mine = jnp.stack([z, a, b, diag])
    sib = lax.ppermute(mine, "dp", [(i, i ^ 1) for i in range(NDP_FAST)])
    return jnp.stack([mine[0], sib[0], mine[1], sib[1], mine[2], sib[2], mine[3], sib[3]])


def _take(x, idx, axis):
    return jnp.take(x, idx, axis=axis, mode="wrap")


def _z_gather(piece):
    f = lax.axis_index("fsdp")
    slots = [piece] + [
        lax.ppermute(piece, "fsdp", [(i, (i + k) % NF_FAST) for i in range(NF_FAST)])
        for k in range(1, NF_FAST)
    ]
    return _take(jnp.stack(slots), (f - jnp.arange(NF_FAST, dtype=jnp.int32)) % NF_FAST, 0)


def _gather_matrix_pp(m):
    d = lax.axis_index("dp")
    j, c = d // 2, d % 2
    n_chips = NDP_FAST // 2
    rows, cols = m.shape[0] // n_chips, m.shape[1] // 2
    z = _z_gather(lax.dynamic_slice(m, (j * rows, c * cols), (rows, cols)))
    x = _take(_plane_gather(z), jnp.arange(NDP_FAST, dtype=jnp.int32) ^ d, 0)
    x = x.reshape(n_chips, 2, NF_FAST, rows, cols)
    x = jnp.concatenate([x[:, 0], x[:, 1]], axis=-1).transpose(1, 0, 2, 3)
    return x.reshape(NF_FAST * m.shape[0], m.shape[1])


def _gather_group(mats, gains):
    d = lax.axis_index("dp")
    j, c = d // 2, d % 2
    n_chips = NDP_FAST // 2
    height = mats[0].shape[0] // n_chips
    blocks, shapes = [], []
    for m in mats:
        rows, cols = m.shape[0] // n_chips, m.shape[1] // 2
        piece = lax.dynamic_slice(m, (j * rows, c * cols), (rows, cols))
        shapes.append((rows, cols))
        blocks.append(piece.reshape(height, rows * cols // height))
    stacked = jnp.concatenate(gains, axis=0)
    flat = stacked.reshape(-1)
    blocks.append(jnp.pad(flat, (0, height * LANES - flat.shape[0])).reshape(height, LANES))
    z = _z_gather(jnp.concatenate(blocks, axis=1))
    out = []
    offset = 0
    for m, (rows, cols) in zip(mats, shapes):
        width = rows * cols // height
        part = z[:, :, offset : offset + width].reshape(NF_FAST, rows, cols)
        x = lax.all_gather(part, "dp", axis=1, tiled=False)
        x = x.reshape(NF_FAST, n_chips, 2, rows, cols)
        x = jnp.concatenate([x[:, :, 0], x[:, :, 1]], axis=-1)
        out.append(x.reshape(NF_FAST * m.shape[0], m.shape[1]))
        offset += width
    g = z[:, :, offset:].reshape(NF_FAST, -1)[:, : flat.shape[0]]
    g = g.reshape(NF_FAST, stacked.shape[0], stacked.shape[1]).transpose(1, 0, 2)
    g = g.reshape(stacked.shape[0], NF_FAST * stacked.shape[1])
    row = 0
    for gain in gains:
        out.append(g[row : row + gain.shape[0]])
        row += gain.shape[0]
    return out


def fast_gather(mats, gains):
    return [_gather_matrix_pp(mats[0])] + _gather_group(mats[1:], gains)


def _reduce_matrix(g):
    d = lax.axis_index("dp")
    f = lax.axis_index("fsdp")
    j, c = d // 2, d % 2
    n_chips = NDP_FAST // 2
    rows, cols = g.shape[0] // (NF_FAST * n_chips), g.shape[1] // 2

    def half(which):
        part = lax.dynamic_slice_in_dim(g, which * cols, cols, 1)
        return part.reshape(NF_FAST, n_chips, rows, cols)

    got = lax.ppermute(half(1 - c).astype(jnp.bfloat16), "dp", [(i, i ^ 1) for i in range(NDP_FAST)])
    chip = half(c) + got.astype(jnp.float32)

    def of_chip(k):
        return lax.dynamic_index_in_dim(chip, k, 1, keepdims=False)

    moved = lax.ppermute(
        of_chip(j ^ 3).astype(jnp.bfloat16),
        "dp",
        [(i, i ^ 2) if i % 2 == 0 else (i, i ^ 4) for i in range(NDP_FAST)],
    ).astype(jnp.float32)
    to_x = of_chip(j ^ 1) + jnp.where(c == 1, moved, 0.0)
    to_y = of_chip(j ^ 2) + jnp.where(c == 0, moved, 0.0)
    from_x = lax.ppermute(to_x.astype(jnp.bfloat16), "dp", [(i, i ^ 2) for i in range(NDP_FAST)])
    from_y = lax.ppermute(to_y.astype(jnp.bfloat16), "dp", [(i, i ^ 4) for i in range(NDP_FAST)])
    plane = of_chip(j) + from_x.astype(jnp.float32) + from_y.astype(jnp.float32)
    total = lax.dynamic_index_in_dim(plane, f, 0, keepdims=False)
    for k in range(1, NF_FAST):
        part = lax.dynamic_index_in_dim(plane, (f + k) % NF_FAST, 0, keepdims=False)
        total = total + lax.ppermute(
            part.astype(jnp.bfloat16), "fsdp", [(i, (i + k) % NF_FAST) for i in range(NF_FAST)]
        ).astype(jnp.float32)
    x = lax.all_gather(total, "dp", axis=0, tiled=False)
    x = x.reshape(n_chips, 2, rows, cols)
    x = jnp.concatenate([x[:, 0], x[:, 1]], axis=-1)
    return x.reshape(n_chips * rows, 2 * cols)


def fast_reduce(mats, gains):
    stacked = jnp.concatenate(gains, axis=0)
    pad = 2 * LANES - stacked.shape[0]
    first = jnp.concatenate([mats[0], jnp.pad(stacked.T, ((0, 0), (0, pad)))], axis=1)
    shard = _reduce_matrix(first)
    width = mats[0].shape[1]
    out = [shard[:, :width]] + [_reduce_matrix(m) for m in mats[1:]]
    mine = shard[:, width : width + stacked.shape[0]].T
    rows = 0
    for g in gains:
        out.append(mine[rows : rows + g.shape[0]])
        rows += g.shape[0]
    return out


def map_blocks(fn, members):
    if members[0].shape[0] == 1:
        return jax.tree.map(lambda v: v[None], fn(tuple(m[0] for m in members)))
    return lax.map(fn, members)


def on_device(fast, *args):
    return layer(fast, *args)


def layer(
    fast, tokens, image_lengths, w_qkv, w_out, w_up, w_down, ln_gain, ln_bias, qk_gain, cotangent
):
    if fast:
        full_qkv, full_out, full_up, full_down, gain_all, bias_all, qk_all = fast_gather(
            (w_qkv, w_out, w_up, w_down), (ln_gain, ln_bias, qk_gain)
        )
    else:
        full_qkv, full_out, full_up, full_down, gain_all, bias_all, qk_all = (
            lax.all_gather(w_qkv, "fsdp", axis=0, tiled=True),
            lax.all_gather(w_out, "fsdp", axis=0, tiled=True),
            lax.all_gather(w_up, "fsdp", axis=0, tiled=True),
            lax.all_gather(w_down, "fsdp", axis=0, tiled=True),
            lax.all_gather(ln_gain, "fsdp", axis=1, tiled=True),
            lax.all_gather(ln_bias, "fsdp", axis=1, tiled=True),
            lax.all_gather(qk_gain, "fsdp", axis=1, tiled=True),
        )
    length = tokens.shape[0]
    model_width = tokens.shape[1]
    blocks = length // PATCH_BIG
    scaling = HEAD_DIM ** (-0.5)
    position = jnp.arange(length, dtype=jnp.int32)
    limits = jnp.cumsum(image_lengths[0])
    segment = jnp.sum((position[:, None] >= limits[None, :]).astype(jnp.int32), axis=1)
    valid_rows = (position < limits[-1]).astype(jnp.float32)[:, None]
    norm_gains = gain_all.astype(jnp.float32)
    biases = bias_all.astype(jnp.float32)
    qk_gains = qk_all.astype(jnp.float32).reshape(2, HEADS, HEAD_DIM)
    inputs = tokens.astype(jnp.float32)
    normed, first_back = jax.vjp(layer_norm, inputs, norm_gains[0], biases[0])
    normed_low = normed.astype(jnp.bfloat16)
    project = jnp.dot(normed_low, full_qkv, preferred_element_type=jnp.float32)
    queries = project[:, :model_width].reshape(length, HEADS, HEAD_DIM)
    keys_raw = project[:, model_width : 2 * model_width].reshape(length, HEADS, HEAD_DIM)
    values_raw = project[:, 2 * model_width :]
    (q_norm, k_norm), norms_back = jax.vjp(both_norms, queries, keys_raw, qk_gains[0], qk_gains[1])
    q_low = q_norm.astype(jnp.bfloat16).reshape(blocks, PATCH_BIG, HEADS, HEAD_DIM)
    k_low = k_norm.astype(jnp.bfloat16).reshape(blocks, PATCH_BIG, HEADS, HEAD_DIM)
    v_low = values_raw.astype(jnp.bfloat16).reshape(blocks, PATCH_BIG, HEADS, HEAD_DIM)
    s_blocks = segment.reshape(blocks, PATCH_BIG)

    def block_scores(q_block, k_block, s_block):
        scores = (
            jnp.einsum("qhd,khd->hqk", q_block, k_block, preferred_element_type=jnp.float32)
            * scaling
        )
        return jnp.where((s_block[:, None] == s_block[None, :])[None], scores, -1e30)

    def attend(members):
        q_block, k_block, v_block, s_block = members
        scores = block_scores(q_block, k_block, s_block)
        row_top = jnp.max(scores, axis=-1, keepdims=True)
        exp_scores = jnp.exp(scores - row_top)
        row_total = jnp.sum(exp_scores, axis=-1, keepdims=True)
        probability = (exp_scores / row_total).astype(jnp.bfloat16)
        mixed_block = jnp.einsum(
            "hqk,khd->qhd", probability, v_block, preferred_element_type=jnp.float32
        )
        return (mixed_block, row_top + jnp.log(row_total))

    mixed_heads, log_total = lax.map(attend, (q_low, k_low, v_low, s_blocks))
    mixed_low = mixed_heads.reshape(length, model_width).astype(jnp.bfloat16)
    residual = inputs + jnp.dot(mixed_low, full_out, preferred_element_type=jnp.float32)
    second, second_back = jax.vjp(layer_norm, residual, norm_gains[1], biases[1])
    second_low = second.astype(jnp.bfloat16)
    up_pre = jnp.dot(second_low, full_up, preferred_element_type=jnp.float32)
    active, gelu_back = jax.vjp(partial(jax.nn.gelu, approximate=False), up_pre)
    active_low = active.astype(jnp.bfloat16)
    output = residual + jnp.dot(active_low, full_down, preferred_element_type=jnp.float32)
    layer_out = (valid_rows * output).astype(jnp.bfloat16)
    back_qkv, back_out, back_up, back_down = full_qkv, full_out, full_up, full_down
    upstream = cotangent.astype(jnp.float32) * valid_rows
    up_low = upstream.astype(jnp.bfloat16)
    grad_down = jnp.dot(active_low.T, up_low, preferred_element_type=jnp.float32)
    grad_active = jnp.dot(up_low, back_down.T, preferred_element_type=jnp.float32)
    (grad_pre,) = gelu_back(grad_active)
    pre_low = grad_pre.astype(jnp.bfloat16)
    grad_up = jnp.dot(second_low.T, pre_low, preferred_element_type=jnp.float32)
    if fast:
        early = [_reduce_matrix(grad_up), _reduce_matrix(grad_down)]
    grad_second = jnp.dot(pre_low, back_up.T, preferred_element_type=jnp.float32)
    grad_resid, gain_two, bias_two = second_back(grad_second)
    grad_resid = grad_resid + upstream
    resid_low = grad_resid.astype(jnp.bfloat16)
    grad_outw = jnp.dot(mixed_low.T, resid_low, preferred_element_type=jnp.float32)
    grad_mixed = jnp.dot(resid_low, back_out.T, preferred_element_type=jnp.float32)
    grad_mixed = grad_mixed.astype(jnp.bfloat16).reshape(blocks, PATCH_BIG, HEADS, HEAD_DIM)

    def attend_back(members):
        q_block, k_block, v_block, s_block, l_block, d_block = members
        scores = block_scores(q_block, k_block, s_block)
        probability = jnp.exp(scores - l_block)
        prob_low = probability.astype(jnp.bfloat16)
        grad_v = jnp.einsum("hqk,qhd->khd", prob_low, d_block, preferred_element_type=jnp.float32)
        grad_p = jnp.einsum("qhd,khd->hqk", d_block, v_block, preferred_element_type=jnp.float32)
        grad_p = lax.optimization_barrier(grad_p.astype(jnp.bfloat16)).astype(jnp.float32)
        grad_s = probability * (grad_p - jnp.sum(probability * grad_p, axis=-1, keepdims=True))
        s_low = grad_s.astype(jnp.bfloat16)
        grad_q = (
            jnp.einsum("hqk,khd->qhd", s_low, k_block, preferred_element_type=jnp.float32) * scaling
        )
        grad_k = (
            jnp.einsum("hqk,qhd->khd", s_low, q_block, preferred_element_type=jnp.float32) * scaling
        )
        return (grad_q, grad_k, grad_v)

    grad_qn, grad_kn, grad_vn = map_blocks(
        attend_back, (q_low, k_low, v_low, s_blocks, log_total, grad_mixed)
    )
    grad_q, grad_k, gain_q, gain_k = norms_back(
        (grad_qn.reshape(length, HEADS, HEAD_DIM), grad_kn.reshape(length, HEADS, HEAD_DIM))
    )
    grad_project = jnp.concatenate(
        [
            grad_q.reshape(length, model_width),
            grad_k.reshape(length, model_width),
            grad_vn.reshape(length, model_width),
        ],
        axis=1,
    ).astype(jnp.bfloat16)
    grad_qkv = jnp.dot(normed_low.T, grad_project, preferred_element_type=jnp.float32)
    grad_normed = jnp.dot(grad_project, back_qkv.T, preferred_element_type=jnp.float32)
    grad_input, gain_one, bias_one = first_back(grad_normed)
    grad_tokens = (grad_input + grad_resid).astype(jnp.bfloat16)
    grad_gain = jnp.stack([gain_one, gain_two])
    grad_bias = jnp.stack([bias_one, bias_two])
    grad_qk = jnp.stack([gain_q.reshape(model_width), gain_k.reshape(model_width)])
    summands = (grad_qkv, grad_outw, grad_up, grad_down, grad_gain, grad_bias, grad_qk)
    if fast:
        late = fast_reduce(summands[:2], summands[4:])
        shares = late[:2] + early + late[2:]
    else:
        pieces = [
            lax.psum_scatter(
                s.astype(jnp.bfloat16), "fsdp", scatter_dimension=0 if k < 4 else 1, tiled=True
            ).astype(jnp.float32)
            for k, s in enumerate(summands)
        ]
        shares = [lax.psum(p.astype(jnp.bfloat16), "dp").astype(jnp.float32) for p in pieces]
    return (
        layer_out,
        grad_tokens,
        shares[0],
        shares[1],
        shares[2],
        shares[3],
        shares[4],
        shares[5],
        shares[6],
    )


def solution(mesh):
    in_specs = (
        P(("dp", "fsdp"), None),
        P(("dp", "fsdp"), None),
        P("fsdp", None),
        P("fsdp", None),
        P("fsdp", None),
        P("fsdp", None),
        P(None, "fsdp"),
        P(None, "fsdp"),
        P(None, "fsdp"),
        P(("dp", "fsdp"), None),
    )
    out_specs = (
        P(("dp", "fsdp"), None),
        P(("dp", "fsdp"), None),
        P("fsdp", None),
        P("fsdp", None),
        P("fsdp", None),
        P("fsdp", None),
        P(None, "fsdp"),
        P(None, "fsdp"),
        P(None, "fsdp"),
    )
    fast = dict(mesh.shape) == {"dp": NDP_FAST, "fsdp": NF_FAST}
    return jax.shard_map(
        partial(on_device, fast), mesh=mesh, in_specs=in_specs, out_specs=out_specs, check_vma=False
    )
```

```python
from functools import partial

import jax
import jax.numpy as jnp
from jax import lax
from jax.sharding import PartitionSpec as P


HEADS = 12
HEAD_DIM = 64
PATCH_BIG = 576


epsilon = 1e-06


def layer_norm(v, gain_row, bias_row):
    centre = v - jnp.mean(v, axis=-1, keepdims=True)
    spread = jnp.mean(centre * centre, axis=-1, keepdims=True)
    return centre * lax.rsqrt(spread + epsilon) * gain_row + bias_row


def head_norm(v, gain_row):
    centre = v - jnp.mean(v, axis=-1, keepdims=True)
    spread = jnp.mean(centre * centre, axis=-1, keepdims=True)
    return centre * lax.rsqrt(spread + epsilon) * gain_row


def both_norms(q_in, k_in, q_gain, k_gain):
    return (head_norm(q_in, q_gain), head_norm(k_in, k_gain))


NF_FAST = 4
NDP_FAST = 8


LANES = 128


def _plane_gather(z):
    d = lax.axis_index("dp")
    c = d % 2
    a = lax.ppermute(z, "dp", [(i, i ^ 2) for i in range(NDP_FAST)])
    b = lax.ppermute(z, "dp", [(i, i ^ 4) for i in range(NDP_FAST)])
    send = jnp.where(c == 0, b, a)
    diag = lax.ppermute(
        send, "dp", [(i, i ^ 2) if i % 2 == 0 else (i, i ^ 4) for i in range(NDP_FAST)]
    )
    mine = jnp.stack([z, a, b, diag])
    sib = lax.ppermute(mine, "dp", [(i, i ^ 1) for i in range(NDP_FAST)])
    return jnp.stack([mine[0], sib[0], mine[1], sib[1], mine[2], sib[2], mine[3], sib[3]])


def _take(x, idx, axis):
    return jnp.take(x, idx, axis=axis, mode="wrap")


def _z_gather(piece):
    f = lax.axis_index("fsdp")
    slots = [piece] + [
        lax.ppermute(piece, "fsdp", [(i, (i + k) % NF_FAST) for i in range(NF_FAST)])
        for k in range(1, NF_FAST)
    ]
    return _take(jnp.stack(slots), (f - jnp.arange(NF_FAST, dtype=jnp.int32)) % NF_FAST, 0)


def _gather_matrix(m):
    d = lax.axis_index("dp")
    j, c = d // 2, d % 2
    rows, cols = m.shape[0] // (NDP_FAST // 2), m.shape[1] // 2
    piece = lax.dynamic_slice(m, (j * rows, c * cols), (rows, cols))
    z = _z_gather(piece)
    x = lax.all_gather(z, "dp", axis=1, tiled=False)
    x = x.reshape(NF_FAST, NDP_FAST // 2, 2, rows, cols)
    x = jnp.concatenate([x[:, :, 0], x[:, :, 1]], axis=-1)
    return x.reshape(NF_FAST * m.shape[0], m.shape[1])


def _gather_matrix_pp(m):
    d = lax.axis_index("dp")
    j, c = d // 2, d % 2
    n_chips = NDP_FAST // 2
    rows, cols = m.shape[0] // n_chips, m.shape[1] // 2
    z = _z_gather(lax.dynamic_slice(m, (j * rows, c * cols), (rows, cols)))
    x = _take(_plane_gather(z), jnp.arange(NDP_FAST, dtype=jnp.int32) ^ d, 0)
    x = x.reshape(n_chips, 2, NF_FAST, rows, cols)
    x = jnp.concatenate([x[:, 0], x[:, 1]], axis=-1).transpose(1, 0, 2, 3)
    return x.reshape(NF_FAST * m.shape[0], m.shape[1])


def fast_gather(mats, gains):
    out = [_gather_matrix_pp(mats[0])] + [_gather_matrix(m) for m in mats[1:]]
    stacked = jnp.concatenate(gains, axis=0)
    z = _z_gather(stacked)
    full = z.transpose(1, 0, 2).reshape(stacked.shape[0], NF_FAST * stacked.shape[1])
    rows = 0
    for g in gains:
        out.append(full[rows : rows + g.shape[0]])
        rows += g.shape[0]
    return out


def _reduce_matrix(g):
    d = lax.axis_index("dp")
    f = lax.axis_index("fsdp")
    j, c = d // 2, d % 2
    n_chips = NDP_FAST // 2
    rows, cols = g.shape[0] // (NF_FAST * n_chips), g.shape[1] // 2

    def half(which):
        part = lax.dynamic_slice_in_dim(g, which * cols, cols, 1)
        return part.reshape(NF_FAST, n_chips, rows, cols)

    got = lax.ppermute(half(1 - c).astype(jnp.bfloat16), "dp", [(i, i ^ 1) for i in range(NDP_FAST)])
    chip = half(c) + got.astype(jnp.float32)

    def of_chip(k):
        return lax.dynamic_index_in_dim(chip, k, 1, keepdims=False)

    moved = lax.ppermute(
        of_chip(j ^ 3).astype(jnp.bfloat16),
        "dp",
        [(i, i ^ 2) if i % 2 == 0 else (i, i ^ 4) for i in range(NDP_FAST)],
    ).astype(jnp.float32)
    to_x = of_chip(j ^ 1) + jnp.where(c == 1, moved, 0.0)
    to_y = of_chip(j ^ 2) + jnp.where(c == 0, moved, 0.0)
    from_x = lax.ppermute(to_x.astype(jnp.bfloat16), "dp", [(i, i ^ 2) for i in range(NDP_FAST)])
    from_y = lax.ppermute(to_y.astype(jnp.bfloat16), "dp", [(i, i ^ 4) for i in range(NDP_FAST)])
    plane = of_chip(j) + from_x.astype(jnp.float32) + from_y.astype(jnp.float32)
    total = lax.dynamic_index_in_dim(plane, f, 0, keepdims=False)
    for k in range(1, NF_FAST):
        part = lax.dynamic_index_in_dim(plane, (f + k) % NF_FAST, 0, keepdims=False)
        total = total + lax.ppermute(
            part.astype(jnp.bfloat16), "fsdp", [(i, (i + k) % NF_FAST) for i in range(NF_FAST)]
        ).astype(jnp.float32)
    x = lax.all_gather(total.astype(jnp.bfloat16), "dp", axis=0, tiled=False).astype(jnp.float32)
    x = x.reshape(n_chips, 2, rows, cols)
    x = jnp.concatenate([x[:, 0], x[:, 1]], axis=-1)
    return x.reshape(n_chips * rows, 2 * cols)


def fast_reduce(mats, gains):
    stacked = jnp.concatenate(gains, axis=0)
    pad = 2 * LANES - stacked.shape[0]
    first = jnp.concatenate([mats[0], jnp.pad(stacked.T, ((0, 0), (0, pad)))], axis=1)
    shard = _reduce_matrix(first)
    width = mats[0].shape[1]
    out = [shard[:, :width]] + [_reduce_matrix(m) for m in mats[1:]]
    mine = shard[:, width : width + stacked.shape[0]].T
    rows = 0
    for g in gains:
        out.append(mine[rows : rows + g.shape[0]])
        rows += g.shape[0]
    return out


def map_blocks(fn, members):
    if members[0].shape[0] == 1:
        return jax.tree.map(lambda v: v[None], fn(tuple(m[0] for m in members)))
    return lax.map(fn, members)


def on_device(fast, *args):
    return layer(fast, *args)


def layer(
    fast, tokens, image_lengths, w_qkv, w_out, w_up, w_down, ln_gain, ln_bias, qk_gain, cotangent
):
    if fast:
        full_qkv, full_out, full_up, full_down, gain_all, bias_all, qk_all = fast_gather(
            (w_qkv, w_out, w_up, w_down), (ln_gain, ln_bias, qk_gain)
        )
    else:
        full_qkv, full_out, full_up, full_down, gain_all, bias_all, qk_all = (
            lax.all_gather(w_qkv, "fsdp", axis=0, tiled=True),
            lax.all_gather(w_out, "fsdp", axis=0, tiled=True),
            lax.all_gather(w_up, "fsdp", axis=0, tiled=True),
            lax.all_gather(w_down, "fsdp", axis=0, tiled=True),
            lax.all_gather(ln_gain, "fsdp", axis=1, tiled=True),
            lax.all_gather(ln_bias, "fsdp", axis=1, tiled=True),
            lax.all_gather(qk_gain, "fsdp", axis=1, tiled=True),
        )
    length = tokens.shape[0]
    model_width = tokens.shape[1]
    blocks = length // PATCH_BIG
    scaling = HEAD_DIM ** (-0.5)
    position = jnp.arange(length, dtype=jnp.int32)
    limits = jnp.cumsum(image_lengths[0])
    segment = jnp.sum((position[:, None] >= limits[None, :]).astype(jnp.int32), axis=1)
    valid_rows = (position < limits[-1]).astype(jnp.float32)[:, None]
    norm_gains = gain_all.astype(jnp.float32)
    biases = bias_all.astype(jnp.float32)
    qk_gains = qk_all.astype(jnp.float32).reshape(2, HEADS, HEAD_DIM)
    inputs = tokens.astype(jnp.float32)
    normed, first_back = jax.vjp(layer_norm, inputs, norm_gains[0], biases[0])
    normed_low = normed.astype(jnp.bfloat16)
    project = jnp.dot(normed_low, full_qkv, preferred_element_type=jnp.float32)
    queries = project[:, :model_width].reshape(length, HEADS, HEAD_DIM)
    keys_raw = project[:, model_width : 2 * model_width].reshape(length, HEADS, HEAD_DIM)
    values_raw = project[:, 2 * model_width :]
    (q_norm, k_norm), norms_back = jax.vjp(both_norms, queries, keys_raw, qk_gains[0], qk_gains[1])
    q_low = q_norm.astype(jnp.bfloat16).reshape(blocks, PATCH_BIG, HEADS, HEAD_DIM)
    k_low = k_norm.astype(jnp.bfloat16).reshape(blocks, PATCH_BIG, HEADS, HEAD_DIM)
    v_low = values_raw.astype(jnp.bfloat16).reshape(blocks, PATCH_BIG, HEADS, HEAD_DIM)
    s_blocks = segment.reshape(blocks, PATCH_BIG)

    def block_scores(q_block, k_block, s_block):
        scores = (
            jnp.einsum("qhd,khd->hqk", q_block, k_block, preferred_element_type=jnp.float32)
            * scaling
        )
        return jnp.where((s_block[:, None] == s_block[None, :])[None], scores, -1e30)

    def attend(members):
        q_block, k_block, v_block, s_block = members
        scores = block_scores(q_block, k_block, s_block)
        row_top = jnp.max(scores, axis=-1, keepdims=True)
        exp_scores = jnp.exp(scores - row_top)
        row_total = jnp.sum(exp_scores, axis=-1, keepdims=True)
        probability = (exp_scores / row_total).astype(jnp.bfloat16)
        mixed_block = jnp.einsum(
            "hqk,khd->qhd", probability, v_block, preferred_element_type=jnp.float32
        )
        return (mixed_block, row_top + jnp.log(row_total))

    mixed_heads, log_total = lax.map(attend, (q_low, k_low, v_low, s_blocks))
    mixed_low = mixed_heads.reshape(length, model_width).astype(jnp.bfloat16)
    residual = inputs + jnp.dot(mixed_low, full_out, preferred_element_type=jnp.float32)
    second, second_back = jax.vjp(layer_norm, residual, norm_gains[1], biases[1])
    second_low = second.astype(jnp.bfloat16)
    up_pre = jnp.dot(second_low, full_up, preferred_element_type=jnp.float32)
    active, gelu_back = jax.vjp(partial(jax.nn.gelu, approximate=False), up_pre)
    active_low = active.astype(jnp.bfloat16)
    output = residual + jnp.dot(active_low, full_down, preferred_element_type=jnp.float32)
    layer_out = (valid_rows * output).astype(jnp.bfloat16)
    back_qkv, back_out, back_up, back_down = full_qkv, full_out, full_up, full_down
    upstream = cotangent.astype(jnp.float32) * valid_rows
    up_low = upstream.astype(jnp.bfloat16)
    grad_down = jnp.dot(active_low.T, up_low, preferred_element_type=jnp.float32)
    grad_active = jnp.dot(up_low, back_down.T, preferred_element_type=jnp.float32)
    (grad_pre,) = gelu_back(grad_active)
    pre_low = grad_pre.astype(jnp.bfloat16)
    grad_up = jnp.dot(second_low.T, pre_low, preferred_element_type=jnp.float32)
    if fast:
        early = [_reduce_matrix(grad_up), _reduce_matrix(grad_down)]
    grad_second = jnp.dot(pre_low, back_up.T, preferred_element_type=jnp.float32)
    grad_resid, gain_two, bias_two = second_back(grad_second)
    grad_resid = grad_resid + upstream
    resid_low = grad_resid.astype(jnp.bfloat16)
    grad_outw = jnp.dot(mixed_low.T, resid_low, preferred_element_type=jnp.float32)
    grad_mixed = jnp.dot(resid_low, back_out.T, preferred_element_type=jnp.float32)
    grad_mixed = grad_mixed.astype(jnp.bfloat16).reshape(blocks, PATCH_BIG, HEADS, HEAD_DIM)

    def attend_back(members):
        q_block, k_block, v_block, s_block, l_block, d_block = members
        scores = block_scores(q_block, k_block, s_block)
        probability = jnp.exp(scores - l_block)
        prob_low = probability.astype(jnp.bfloat16)
        grad_v = jnp.einsum("hqk,qhd->khd", prob_low, d_block, preferred_element_type=jnp.float32)
        grad_p = jnp.einsum("qhd,khd->hqk", d_block, v_block, preferred_element_type=jnp.float32)
        grad_p = lax.optimization_barrier(grad_p.astype(jnp.bfloat16)).astype(jnp.float32)
        grad_s = probability * (grad_p - jnp.sum(probability * grad_p, axis=-1, keepdims=True))
        s_low = grad_s.astype(jnp.bfloat16)
        grad_q = (
            jnp.einsum("hqk,khd->qhd", s_low, k_block, preferred_element_type=jnp.float32) * scaling
        )
        grad_k = (
            jnp.einsum("hqk,qhd->khd", s_low, q_block, preferred_element_type=jnp.float32) * scaling
        )
        return (grad_q, grad_k, grad_v)

    grad_qn, grad_kn, grad_vn = map_blocks(
        attend_back, (q_low, k_low, v_low, s_blocks, log_total, grad_mixed)
    )
    grad_q, grad_k, gain_q, gain_k = norms_back(
        (grad_qn.reshape(length, HEADS, HEAD_DIM), grad_kn.reshape(length, HEADS, HEAD_DIM))
    )
    grad_project = jnp.concatenate(
        [
            grad_q.reshape(length, model_width),
            grad_k.reshape(length, model_width),
            grad_vn.reshape(length, model_width),
        ],
        axis=1,
    ).astype(jnp.bfloat16)
    grad_qkv = jnp.dot(normed_low.T, grad_project, preferred_element_type=jnp.float32)
    grad_normed = jnp.dot(grad_project, back_qkv.T, preferred_element_type=jnp.float32)
    grad_input, gain_one, bias_one = first_back(grad_normed)
    grad_tokens = (grad_input + grad_resid).astype(jnp.bfloat16)
    grad_gain = jnp.stack([gain_one, gain_two])
    grad_bias = jnp.stack([bias_one, bias_two])
    grad_qk = jnp.stack([gain_q.reshape(model_width), gain_k.reshape(model_width)])
    summands = (grad_qkv, grad_outw, grad_up, grad_down, grad_gain, grad_bias, grad_qk)
    if fast:
        late = fast_reduce(summands[:2], summands[4:])
        shares = late[:2] + early + late[2:]
    else:
        pieces = [
            lax.psum_scatter(
                s.astype(jnp.bfloat16), "fsdp", scatter_dimension=0 if k < 4 else 1, tiled=True
            ).astype(jnp.float32)
            for k, s in enumerate(summands)
        ]
        shares = [lax.psum(p.astype(jnp.bfloat16), "dp").astype(jnp.float32) for p in pieces]
    return (
        layer_out,
        grad_tokens,
        shares[0],
        shares[1],
        shares[2],
        shares[3],
        shares[4],
        shares[5],
        shares[6],
    )


def solution(mesh):
    in_specs = (
        P(("dp", "fsdp"), None),
        P(("dp", "fsdp"), None),
        P("fsdp", None),
        P("fsdp", None),
        P("fsdp", None),
        P("fsdp", None),
        P(None, "fsdp"),
        P(None, "fsdp"),
        P(None, "fsdp"),
        P(("dp", "fsdp"), None),
    )
    out_specs = (
        P(("dp", "fsdp"), None),
        P(("dp", "fsdp"), None),
        P("fsdp", None),
        P("fsdp", None),
        P("fsdp", None),
        P("fsdp", None),
        P(None, "fsdp"),
        P(None, "fsdp"),
        P(None, "fsdp"),
    )
    fast = dict(mesh.shape) == {"dp": NDP_FAST, "fsdp": NF_FAST}
    return jax.shard_map(
        partial(on_device, fast), mesh=mesh, in_specs=in_specs, out_specs=out_specs, check_vma=False
    )
```

```python
from functools import partial

import jax
import jax.numpy as jnp
from jax import lax
from jax.sharding import PartitionSpec as P


HEADS = 12
HEAD_DIM = 64
PATCH_BIG = 576


epsilon = 1e-06


def layer_norm(v, gain_row, bias_row):
    centre = v - jnp.mean(v, axis=-1, keepdims=True)
    spread = jnp.mean(centre * centre, axis=-1, keepdims=True)
    return centre * lax.rsqrt(spread + epsilon) * gain_row + bias_row


def head_norm(v, gain_row):
    centre = v - jnp.mean(v, axis=-1, keepdims=True)
    spread = jnp.mean(centre * centre, axis=-1, keepdims=True)
    return centre * lax.rsqrt(spread + epsilon) * gain_row


def both_norms(q_in, k_in, q_gain, k_gain):
    return (head_norm(q_in, q_gain), head_norm(k_in, k_gain))


NF_FAST = 4
NDP_FAST = 8


LANES = 128


def _plane_gather(z):
    d = lax.axis_index("dp")
    c = d % 2
    a = lax.ppermute(z, "dp", [(i, i ^ 2) for i in range(NDP_FAST)])
    b = lax.ppermute(z, "dp", [(i, i ^ 4) for i in range(NDP_FAST)])
    send = jnp.where(c == 0, b, a)
    diag = lax.ppermute(
        send, "dp", [(i, i ^ 2) if i % 2 == 0 else (i, i ^ 4) for i in range(NDP_FAST)]
    )
    mine = jnp.stack([z, a, b, diag])
    sib = lax.ppermute(mine, "dp", [(i, i ^ 1) for i in range(NDP_FAST)])
    return jnp.stack([mine[0], sib[0], mine[1], sib[1], mine[2], sib[2], mine[3], sib[3]])


def _take(x, idx, axis):
    return jnp.take(x, idx, axis=axis, mode="wrap")


def _z_gather(piece):
    f = lax.axis_index("fsdp")
    slots = [piece] + [
        lax.ppermute(piece, "fsdp", [(i, (i + k) % NF_FAST) for i in range(NF_FAST)])
        for k in range(1, NF_FAST)
    ]
    return _take(jnp.stack(slots), (f - jnp.arange(NF_FAST, dtype=jnp.int32)) % NF_FAST, 0)


def _gather_matrix(m):
    d = lax.axis_index("dp")
    j, c = d // 2, d % 2
    rows, cols = m.shape[0] // (NDP_FAST // 2), m.shape[1] // 2
    piece = lax.dynamic_slice(m, (j * rows, c * cols), (rows, cols))
    z = _z_gather(piece)
    x = lax.all_gather(z, "dp", axis=1, tiled=False)
    x = x.reshape(NF_FAST, NDP_FAST // 2, 2, rows, cols)
    x = jnp.concatenate([x[:, :, 0], x[:, :, 1]], axis=-1)
    return x.reshape(NF_FAST * m.shape[0], m.shape[1])


def _gather_matrix_pp(m):
    d = lax.axis_index("dp")
    j, c = d // 2, d % 2
    n_chips = NDP_FAST // 2
    rows, cols = m.shape[0] // n_chips, m.shape[1] // 2
    z = _z_gather(lax.dynamic_slice(m, (j * rows, c * cols), (rows, cols)))
    x = _take(_plane_gather(z), jnp.arange(NDP_FAST, dtype=jnp.int32) ^ d, 0)
    x = x.reshape(n_chips, 2, NF_FAST, rows, cols)
    x = jnp.concatenate([x[:, 0], x[:, 1]], axis=-1).transpose(1, 0, 2, 3)
    return x.reshape(NF_FAST * m.shape[0], m.shape[1])


def fast_gather(mats, gains):
    out = [_gather_matrix_pp(mats[0])] + [_gather_matrix(m) for m in mats[1:]]
    stacked = jnp.concatenate(gains, axis=0)
    z = _z_gather(stacked)
    full = z.transpose(1, 0, 2).reshape(stacked.shape[0], NF_FAST * stacked.shape[1])
    rows = 0
    for g in gains:
        out.append(full[rows : rows + g.shape[0]])
        rows += g.shape[0]
    return out


def _reduce_matrix(g, hold=None):
    d = lax.axis_index("dp")
    f = lax.axis_index("fsdp")
    j, c = d // 2, d % 2
    n_chips = NDP_FAST // 2
    rows, cols = g.shape[0] // (NF_FAST * n_chips), g.shape[1] // 2

    def half(which):
        part = lax.dynamic_slice_in_dim(g, which * cols, cols, 1)
        return part.reshape(NF_FAST, n_chips, rows, cols)

    got = lax.ppermute(half(1 - c).astype(jnp.bfloat16), "dp", [(i, i ^ 1) for i in range(NDP_FAST)])
    chip = half(c) + got.astype(jnp.float32)

    def of_chip(k):
        return lax.dynamic_index_in_dim(chip, k, 1, keepdims=False)

    moved = lax.ppermute(
        of_chip(j ^ 3).astype(jnp.bfloat16),
        "dp",
        [(i, i ^ 2) if i % 2 == 0 else (i, i ^ 4) for i in range(NDP_FAST)],
    ).astype(jnp.float32)
    to_x = of_chip(j ^ 1) + jnp.where(c == 1, moved, 0.0)
    to_y = of_chip(j ^ 2) + jnp.where(c == 0, moved, 0.0)
    from_x = lax.ppermute(to_x.astype(jnp.bfloat16), "dp", [(i, i ^ 2) for i in range(NDP_FAST)])
    from_y = lax.ppermute(to_y.astype(jnp.bfloat16), "dp", [(i, i ^ 4) for i in range(NDP_FAST)])
    plane = of_chip(j) + from_x.astype(jnp.float32) + from_y.astype(jnp.float32)
    total = lax.dynamic_index_in_dim(plane, f, 0, keepdims=False)
    for k in range(1, NF_FAST):
        part = lax.dynamic_index_in_dim(plane, (f + k) % NF_FAST, 0, keepdims=False)
        total = total + lax.ppermute(
            part.astype(jnp.bfloat16), "fsdp", [(i, (i + k) % NF_FAST) for i in range(NF_FAST)]
        ).astype(jnp.float32)
    if hold is not None:
        total, hold = lax.optimization_barrier((total, hold))
    x = lax.all_gather(total, "dp", axis=0, tiled=False)
    x = x.reshape(n_chips, 2, rows, cols)
    x = jnp.concatenate([x[:, 0], x[:, 1]], axis=-1)
    shard = x.reshape(n_chips * rows, 2 * cols)
    return shard if hold is None else (shard, hold)


def fast_reduce(mats, gains, hold):
    stacked = jnp.concatenate(gains, axis=0)
    pad = 2 * LANES - stacked.shape[0]
    first = jnp.concatenate([mats[0], jnp.pad(stacked.T, ((0, 0), (0, pad)))], axis=1)
    shard, hold = _reduce_matrix(first, hold)
    width = mats[0].shape[1]
    out = [shard[:, :width]] + [_reduce_matrix(m) for m in mats[1:]]
    mine = shard[:, width : width + stacked.shape[0]].T
    rows = 0
    for g in gains:
        out.append(mine[rows : rows + g.shape[0]])
        rows += g.shape[0]
    return out, hold


def map_blocks(fn, members):
    if members[0].shape[0] == 1:
        return jax.tree.map(lambda v: v[None], fn(tuple(m[0] for m in members)))
    return lax.map(fn, members)


def on_device(fast, *args):
    return layer(fast, *args)


def layer(
    fast, tokens, image_lengths, w_qkv, w_out, w_up, w_down, ln_gain, ln_bias, qk_gain, cotangent
):
    if fast:
        full_qkv, full_out, full_up, full_down, gain_all, bias_all, qk_all = fast_gather(
            (w_qkv, w_out, w_up, w_down), (ln_gain, ln_bias, qk_gain)
        )
    else:
        full_qkv, full_out, full_up, full_down, gain_all, bias_all, qk_all = (
            lax.all_gather(w_qkv, "fsdp", axis=0, tiled=True),
            lax.all_gather(w_out, "fsdp", axis=0, tiled=True),
            lax.all_gather(w_up, "fsdp", axis=0, tiled=True),
            lax.all_gather(w_down, "fsdp", axis=0, tiled=True),
            lax.all_gather(ln_gain, "fsdp", axis=1, tiled=True),
            lax.all_gather(ln_bias, "fsdp", axis=1, tiled=True),
            lax.all_gather(qk_gain, "fsdp", axis=1, tiled=True),
        )
    length = tokens.shape[0]
    model_width = tokens.shape[1]
    blocks = length // PATCH_BIG
    scaling = HEAD_DIM ** (-0.5)
    position = jnp.arange(length, dtype=jnp.int32)
    limits = jnp.cumsum(image_lengths[0])
    segment = jnp.sum((position[:, None] >= limits[None, :]).astype(jnp.int32), axis=1)
    valid_rows = (position < limits[-1]).astype(jnp.float32)[:, None]
    norm_gains = gain_all.astype(jnp.float32)
    biases = bias_all.astype(jnp.float32)
    qk_gains = qk_all.astype(jnp.float32).reshape(2, HEADS, HEAD_DIM)
    inputs = tokens.astype(jnp.float32)
    normed, first_back = jax.vjp(layer_norm, inputs, norm_gains[0], biases[0])
    normed_low = normed.astype(jnp.bfloat16)
    project = jnp.dot(normed_low, full_qkv, preferred_element_type=jnp.float32)
    queries = project[:, :model_width].reshape(length, HEADS, HEAD_DIM)
    keys_raw = project[:, model_width : 2 * model_width].reshape(length, HEADS, HEAD_DIM)
    values_raw = project[:, 2 * model_width :]
    (q_norm, k_norm), norms_back = jax.vjp(both_norms, queries, keys_raw, qk_gains[0], qk_gains[1])
    q_low = q_norm.astype(jnp.bfloat16).reshape(blocks, PATCH_BIG, HEADS, HEAD_DIM)
    k_low = k_norm.astype(jnp.bfloat16).reshape(blocks, PATCH_BIG, HEADS, HEAD_DIM)
    v_low = values_raw.astype(jnp.bfloat16).reshape(blocks, PATCH_BIG, HEADS, HEAD_DIM)
    s_blocks = segment.reshape(blocks, PATCH_BIG)

    def block_scores(q_block, k_block, s_block):
        scores = (
            jnp.einsum("qhd,khd->hqk", q_block, k_block, preferred_element_type=jnp.float32)
            * scaling
        )
        return jnp.where((s_block[:, None] == s_block[None, :])[None], scores, -1e30)

    def attend(members):
        q_block, k_block, v_block, s_block = members
        scores = block_scores(q_block, k_block, s_block)
        row_top = jnp.max(scores, axis=-1, keepdims=True)
        exp_scores = jnp.exp(scores - row_top)
        row_total = jnp.sum(exp_scores, axis=-1, keepdims=True)
        probability = (exp_scores / row_total).astype(jnp.bfloat16)
        mixed_block = jnp.einsum(
            "hqk,khd->qhd", probability, v_block, preferred_element_type=jnp.float32
        )
        return (mixed_block, row_top + jnp.log(row_total))

    mixed_heads, log_total = lax.map(attend, (q_low, k_low, v_low, s_blocks))
    mixed_low = mixed_heads.reshape(length, model_width).astype(jnp.bfloat16)
    residual = inputs + jnp.dot(mixed_low, full_out, preferred_element_type=jnp.float32)
    second, second_back = jax.vjp(layer_norm, residual, norm_gains[1], biases[1])
    second_low = second.astype(jnp.bfloat16)
    up_pre = jnp.dot(second_low, full_up, preferred_element_type=jnp.float32)
    active, gelu_back = jax.vjp(partial(jax.nn.gelu, approximate=False), up_pre)
    active_low = active.astype(jnp.bfloat16)
    output = residual + jnp.dot(active_low, full_down, preferred_element_type=jnp.float32)
    layer_out = (valid_rows * output).astype(jnp.bfloat16)
    back_qkv, back_out, back_up, back_down = full_qkv, full_out, full_up, full_down
    upstream = cotangent.astype(jnp.float32) * valid_rows
    up_low = upstream.astype(jnp.bfloat16)
    grad_down = jnp.dot(active_low.T, up_low, preferred_element_type=jnp.float32)
    grad_active = jnp.dot(up_low, back_down.T, preferred_element_type=jnp.float32)
    (grad_pre,) = gelu_back(grad_active)
    pre_low = grad_pre.astype(jnp.bfloat16)
    grad_up = jnp.dot(second_low.T, pre_low, preferred_element_type=jnp.float32)
    if fast:
        early = [_reduce_matrix(grad_up), _reduce_matrix(grad_down)]
    grad_second = jnp.dot(pre_low, back_up.T, preferred_element_type=jnp.float32)
    grad_resid, gain_two, bias_two = second_back(grad_second)
    grad_resid = grad_resid + upstream
    resid_low = grad_resid.astype(jnp.bfloat16)
    grad_outw = jnp.dot(mixed_low.T, resid_low, preferred_element_type=jnp.float32)
    grad_mixed = jnp.dot(resid_low, back_out.T, preferred_element_type=jnp.float32)
    grad_mixed = grad_mixed.astype(jnp.bfloat16).reshape(blocks, PATCH_BIG, HEADS, HEAD_DIM)

    def attend_back(members):
        q_block, k_block, v_block, s_block, l_block, d_block = members
        scores = block_scores(q_block, k_block, s_block)
        probability = jnp.exp(scores - l_block)
        prob_low = probability.astype(jnp.bfloat16)
        grad_v = jnp.einsum("hqk,qhd->khd", prob_low, d_block, preferred_element_type=jnp.float32)
        grad_p = jnp.einsum("qhd,khd->hqk", d_block, v_block, preferred_element_type=jnp.float32)
        grad_p = lax.optimization_barrier(grad_p.astype(jnp.bfloat16)).astype(jnp.float32)
        grad_s = probability * (grad_p - jnp.sum(probability * grad_p, axis=-1, keepdims=True))
        s_low = grad_s.astype(jnp.bfloat16)
        grad_q = (
            jnp.einsum("hqk,khd->qhd", s_low, k_block, preferred_element_type=jnp.float32) * scaling
        )
        grad_k = (
            jnp.einsum("hqk,qhd->khd", s_low, q_block, preferred_element_type=jnp.float32) * scaling
        )
        return (grad_q, grad_k, grad_v)

    grad_qn, grad_kn, grad_vn = map_blocks(
        attend_back, (q_low, k_low, v_low, s_blocks, log_total, grad_mixed)
    )
    grad_q, grad_k, gain_q, gain_k = norms_back(
        (grad_qn.reshape(length, HEADS, HEAD_DIM), grad_kn.reshape(length, HEADS, HEAD_DIM))
    )
    grad_project = jnp.concatenate(
        [
            grad_q.reshape(length, model_width),
            grad_k.reshape(length, model_width),
            grad_vn.reshape(length, model_width),
        ],
        axis=1,
    ).astype(jnp.bfloat16)
    grad_qkv = jnp.dot(normed_low.T, grad_project, preferred_element_type=jnp.float32)
    grad_normed = jnp.dot(grad_project, back_qkv.T, preferred_element_type=jnp.float32)
    grad_input, gain_one, bias_one = first_back(grad_normed)
    grad_tokens = (grad_input + grad_resid).astype(jnp.bfloat16)
    grad_gain = jnp.stack([gain_one, gain_two])
    grad_bias = jnp.stack([bias_one, bias_two])
    grad_qk = jnp.stack([gain_q.reshape(model_width), gain_k.reshape(model_width)])
    summands = (grad_qkv, grad_outw, grad_up, grad_down, grad_gain, grad_bias, grad_qk)
    if fast:
        late, early = fast_reduce(summands[:2], summands[4:], early)
        shares = late[:2] + list(early) + late[2:]
    else:
        pieces = [
            lax.psum_scatter(
                s.astype(jnp.bfloat16), "fsdp", scatter_dimension=0 if k < 4 else 1, tiled=True
            ).astype(jnp.float32)
            for k, s in enumerate(summands)
        ]
        shares = [lax.psum(p.astype(jnp.bfloat16), "dp").astype(jnp.float32) for p in pieces]
    return (
        layer_out,
        grad_tokens,
        shares[0],
        shares[1],
        shares[2],
        shares[3],
        shares[4],
        shares[5],
        shares[6],
    )


def solution(mesh):
    in_specs = (
        P(("dp", "fsdp"), None),
        P(("dp", "fsdp"), None),
        P("fsdp", None),
        P("fsdp", None),
        P("fsdp", None),
        P("fsdp", None),
        P(None, "fsdp"),
        P(None, "fsdp"),
        P(None, "fsdp"),
        P(("dp", "fsdp"), None),
    )
    out_specs = (
        P(("dp", "fsdp"), None),
        P(("dp", "fsdp"), None),
        P("fsdp", None),
        P("fsdp", None),
        P("fsdp", None),
        P("fsdp", None),
        P(None, "fsdp"),
        P(None, "fsdp"),
        P(None, "fsdp"),
    )
    fast = dict(mesh.shape) == {"dp": NDP_FAST, "fsdp": NF_FAST}
    return jax.shard_map(
        partial(on_device, fast), mesh=mesh, in_specs=in_specs, out_specs=out_specs, check_vma=False
    )
```

```python
from functools import partial

import jax
import jax.numpy as jnp
from jax import lax
from jax.sharding import PartitionSpec as P


HEADS = 12
HEAD_DIM = 64
PATCH_BIG = 576


epsilon = 1e-06


def layer_norm(v, gain_row, bias_row):
    centre = v - jnp.mean(v, axis=-1, keepdims=True)
    spread = jnp.mean(centre * centre, axis=-1, keepdims=True)
    return centre * lax.rsqrt(spread + epsilon) * gain_row + bias_row


def head_norm(v, gain_row):
    centre = v - jnp.mean(v, axis=-1, keepdims=True)
    spread = jnp.mean(centre * centre, axis=-1, keepdims=True)
    return centre * lax.rsqrt(spread + epsilon) * gain_row


def both_norms(q_in, k_in, q_gain, k_gain):
    return (head_norm(q_in, q_gain), head_norm(k_in, k_gain))


NF_FAST = 4
NDP_FAST = 8


LANES = 128


def _plane_gather(z):
    d = lax.axis_index("dp")
    c = d % 2
    a = lax.ppermute(z, "dp", [(i, i ^ 2) for i in range(NDP_FAST)])
    b = lax.ppermute(z, "dp", [(i, i ^ 4) for i in range(NDP_FAST)])
    send = jnp.where(c == 0, b, a)
    diag = lax.ppermute(
        send, "dp", [(i, i ^ 2) if i % 2 == 0 else (i, i ^ 4) for i in range(NDP_FAST)]
    )
    mine = jnp.stack([z, a, b, diag])
    sib = lax.ppermute(mine, "dp", [(i, i ^ 1) for i in range(NDP_FAST)])
    return jnp.stack([mine[0], sib[0], mine[1], sib[1], mine[2], sib[2], mine[3], sib[3]])


def _take(x, idx, axis):
    return jnp.take(x, idx, axis=axis, mode="wrap")


def _z_gather(piece):
    f = lax.axis_index("fsdp")
    slots = [piece] + [
        lax.ppermute(piece, "fsdp", [(i, (i + k) % NF_FAST) for i in range(NF_FAST)])
        for k in range(1, NF_FAST)
    ]
    return _take(jnp.stack(slots), (f - jnp.arange(NF_FAST, dtype=jnp.int32)) % NF_FAST, 0)


def _gather_matrix(m):
    d = lax.axis_index("dp")
    j, c = d // 2, d % 2
    rows, cols = m.shape[0] // (NDP_FAST // 2), m.shape[1] // 2
    piece = lax.dynamic_slice(m, (j * rows, c * cols), (rows, cols))
    z = _z_gather(piece)
    x = lax.all_gather(z, "dp", axis=1, tiled=False)
    x = x.reshape(NF_FAST, NDP_FAST // 2, 2, rows, cols)
    x = jnp.concatenate([x[:, :, 0], x[:, :, 1]], axis=-1)
    return x.reshape(NF_FAST * m.shape[0], m.shape[1])


def _gather_matrix_pp(m):
    d = lax.axis_index("dp")
    j, c = d // 2, d % 2
    n_chips = NDP_FAST // 2
    rows, cols = m.shape[0] // n_chips, m.shape[1] // 2
    z = _z_gather(lax.dynamic_slice(m, (j * rows, c * cols), (rows, cols)))
    x = _take(_plane_gather(z), jnp.arange(NDP_FAST, dtype=jnp.int32) ^ d, 0)
    x = x.reshape(n_chips, 2, NF_FAST, rows, cols)
    x = jnp.concatenate([x[:, 0], x[:, 1]], axis=-1).transpose(1, 0, 2, 3)
    return x.reshape(NF_FAST * m.shape[0], m.shape[1])


def fast_gather(mats, gains):
    out = [_gather_matrix_pp(mats[0])]
    out += [_gather_matrix(m) for m in mats[1:]]
    stacked = jnp.concatenate(gains, axis=0)
    z = _z_gather(stacked)
    full = z.transpose(1, 0, 2).reshape(stacked.shape[0], NF_FAST * stacked.shape[1])
    rows = 0
    for g in gains:
        out.append(full[rows : rows + g.shape[0]])
        rows += g.shape[0]
    return out


def _reduce_matrix(g):
    d = lax.axis_index("dp")
    f = lax.axis_index("fsdp")
    j, c = d // 2, d % 2
    n_chips = NDP_FAST // 2
    rows, cols = g.shape[0] // (NF_FAST * n_chips), g.shape[1] // 2

    def half(which):
        part = lax.dynamic_slice_in_dim(g, which * cols, cols, 1)
        return part.reshape(NF_FAST, n_chips, rows, cols)

    got = lax.ppermute(half(1 - c).astype(jnp.bfloat16), "dp", [(i, i ^ 1) for i in range(NDP_FAST)])
    chip = half(c) + got.astype(jnp.float32)

    def of_chip(k):
        return lax.dynamic_index_in_dim(chip, k, 1, keepdims=False)

    moved = lax.ppermute(
        of_chip(j ^ 3).astype(jnp.bfloat16),
        "dp",
        [(i, i ^ 2) if i % 2 == 0 else (i, i ^ 4) for i in range(NDP_FAST)],
    ).astype(jnp.float32)
    to_x = of_chip(j ^ 1) + jnp.where(c == 1, moved, 0.0)
    to_y = of_chip(j ^ 2) + jnp.where(c == 0, moved, 0.0)
    from_x = lax.ppermute(to_x.astype(jnp.bfloat16), "dp", [(i, i ^ 2) for i in range(NDP_FAST)])
    from_y = lax.ppermute(to_y.astype(jnp.bfloat16), "dp", [(i, i ^ 4) for i in range(NDP_FAST)])
    plane = of_chip(j) + from_x.astype(jnp.float32) + from_y.astype(jnp.float32)
    total = lax.dynamic_index_in_dim(plane, f, 0, keepdims=False)
    for k in range(1, NF_FAST):
        part = lax.dynamic_index_in_dim(plane, (f + k) % NF_FAST, 0, keepdims=False)
        total = total + lax.ppermute(
            part.astype(jnp.bfloat16), "fsdp", [(i, (i + k) % NF_FAST) for i in range(NF_FAST)]
        ).astype(jnp.float32)
    x = lax.all_gather(total, "dp", axis=0, tiled=False)
    x = x.reshape(n_chips, 2, rows, cols)
    x = jnp.concatenate([x[:, 0], x[:, 1]], axis=-1)
    return x.reshape(n_chips * rows, 2 * cols)


def fast_reduce(mats, gains):
    stacked = jnp.concatenate(gains, axis=0)
    pad = 2 * LANES - stacked.shape[0]
    first = jnp.concatenate([mats[0], jnp.pad(stacked.T, ((0, 0), (0, pad)))], axis=1)
    shard = _reduce_matrix(first)
    width = mats[0].shape[1]
    out = [shard[:, :width]] + [_reduce_matrix(m) for m in mats[1:]]
    mine = shard[:, width : width + stacked.shape[0]].T
    rows = 0
    for g in gains:
        out.append(mine[rows : rows + g.shape[0]])
        rows += g.shape[0]
    return out


def map_blocks(fn, members):
    if members[0].shape[0] == 1:
        return jax.tree.map(lambda v: v[None], fn(tuple(m[0] for m in members)))
    return lax.map(fn, members)


def on_device(fast, *args):
    return layer(fast, *args)


def layer(
    fast, tokens, image_lengths, w_qkv, w_out, w_up, w_down, ln_gain, ln_bias, qk_gain, cotangent
):
    if fast:
        full_qkv, full_out, full_up, full_down, gain_all, bias_all, qk_all = fast_gather(
            (w_qkv, w_out, w_up, w_down), (ln_gain, ln_bias, qk_gain)
        )
    else:
        full_qkv, full_out, full_up, full_down, gain_all, bias_all, qk_all = (
            lax.all_gather(w_qkv, "fsdp", axis=0, tiled=True),
            lax.all_gather(w_out, "fsdp", axis=0, tiled=True),
            lax.all_gather(w_up, "fsdp", axis=0, tiled=True),
            lax.all_gather(w_down, "fsdp", axis=0, tiled=True),
            lax.all_gather(ln_gain, "fsdp", axis=1, tiled=True),
            lax.all_gather(ln_bias, "fsdp", axis=1, tiled=True),
            lax.all_gather(qk_gain, "fsdp", axis=1, tiled=True),
        )
    length = tokens.shape[0]
    model_width = tokens.shape[1]
    blocks = length // PATCH_BIG
    scaling = HEAD_DIM ** (-0.5)
    position = jnp.arange(length, dtype=jnp.int32)
    limits = jnp.cumsum(image_lengths[0])
    segment = jnp.sum((position[:, None] >= limits[None, :]).astype(jnp.int32), axis=1)
    valid_rows = (position < limits[-1]).astype(jnp.float32)[:, None]
    norm_gains = gain_all.astype(jnp.float32)
    biases = bias_all.astype(jnp.float32)
    qk_gains = qk_all.astype(jnp.float32).reshape(2, HEADS, HEAD_DIM)
    inputs = tokens.astype(jnp.float32)
    normed, first_back = jax.vjp(layer_norm, inputs, norm_gains[0], biases[0])
    normed_low = normed.astype(jnp.bfloat16)
    project = jnp.dot(normed_low, full_qkv, preferred_element_type=jnp.float32)
    queries = project[:, :model_width].reshape(length, HEADS, HEAD_DIM)
    keys_raw = project[:, model_width : 2 * model_width].reshape(length, HEADS, HEAD_DIM)
    values_raw = project[:, 2 * model_width :]
    (q_norm, k_norm), norms_back = jax.vjp(both_norms, queries, keys_raw, qk_gains[0], qk_gains[1])
    q_low = q_norm.astype(jnp.bfloat16).reshape(blocks, PATCH_BIG, HEADS, HEAD_DIM)
    k_low = k_norm.astype(jnp.bfloat16).reshape(blocks, PATCH_BIG, HEADS, HEAD_DIM)
    v_low = values_raw.astype(jnp.bfloat16).reshape(blocks, PATCH_BIG, HEADS, HEAD_DIM)
    s_blocks = segment.reshape(blocks, PATCH_BIG)

    def block_scores(q_block, k_block, s_block):
        scores = (
            jnp.einsum("qhd,khd->hqk", q_block, k_block, preferred_element_type=jnp.float32)
            * scaling
        )
        return jnp.where((s_block[:, None] == s_block[None, :])[None], scores, -1e30)

    def attend(members):
        q_block, k_block, v_block, s_block = members
        scores = block_scores(q_block, k_block, s_block)
        row_top = jnp.max(scores, axis=-1, keepdims=True)
        exp_scores = jnp.exp(scores - row_top)
        row_total = jnp.sum(exp_scores, axis=-1, keepdims=True)
        probability = (exp_scores / row_total).astype(jnp.bfloat16)
        mixed_block = jnp.einsum(
            "hqk,khd->qhd", probability, v_block, preferred_element_type=jnp.float32
        )
        return (mixed_block, row_top + jnp.log(row_total))

    mixed_heads, log_total = lax.map(attend, (q_low, k_low, v_low, s_blocks))
    mixed_low = mixed_heads.reshape(length, model_width).astype(jnp.bfloat16)
    residual = inputs + jnp.dot(mixed_low, full_out, preferred_element_type=jnp.float32)
    second, second_back = jax.vjp(layer_norm, residual, norm_gains[1], biases[1])
    second_low = second.astype(jnp.bfloat16)
    up_pre = jnp.dot(second_low, full_up, preferred_element_type=jnp.float32)
    active, gelu_back = jax.vjp(partial(jax.nn.gelu, approximate=False), up_pre)
    active_low = active.astype(jnp.bfloat16)
    output = residual + jnp.dot(active_low, full_down, preferred_element_type=jnp.float32)
    layer_out = (valid_rows * output).astype(jnp.bfloat16)
    back_qkv, back_out, back_up, back_down = full_qkv, full_out, full_up, full_down
    upstream = cotangent.astype(jnp.float32) * valid_rows
    up_low = upstream.astype(jnp.bfloat16)
    grad_down = jnp.dot(active_low.T, up_low, preferred_element_type=jnp.float32)
    grad_active = jnp.dot(up_low, back_down.T, preferred_element_type=jnp.float32)
    (grad_pre,) = gelu_back(grad_active)
    pre_low = grad_pre.astype(jnp.bfloat16)
    grad_up = jnp.dot(second_low.T, pre_low, preferred_element_type=jnp.float32)
    if fast:
        early = [_reduce_matrix(grad_up), _reduce_matrix(grad_down)]
    grad_second = jnp.dot(pre_low, back_up.T, preferred_element_type=jnp.float32)
    grad_resid, gain_two, bias_two = second_back(grad_second)
    grad_resid = grad_resid + upstream
    resid_low = grad_resid.astype(jnp.bfloat16)
    grad_outw = jnp.dot(mixed_low.T, resid_low, preferred_element_type=jnp.float32)
    grad_mixed = jnp.dot(resid_low, back_out.T, preferred_element_type=jnp.float32)
    grad_mixed = grad_mixed.astype(jnp.bfloat16).reshape(blocks, PATCH_BIG, HEADS, HEAD_DIM)

    def attend_back(members):
        q_block, k_block, v_block, s_block, l_block, d_block = members
        scores = block_scores(q_block, k_block, s_block)
        probability = jnp.exp(scores - l_block)
        prob_low = probability.astype(jnp.bfloat16)
        grad_v = jnp.einsum("hqk,qhd->khd", prob_low, d_block, preferred_element_type=jnp.float32)
        grad_p = jnp.einsum("qhd,khd->hqk", d_block, v_block, preferred_element_type=jnp.float32)
        grad_p = lax.optimization_barrier(grad_p.astype(jnp.bfloat16)).astype(jnp.float32)
        grad_s = probability * (grad_p - jnp.sum(probability * grad_p, axis=-1, keepdims=True))
        s_low = grad_s.astype(jnp.bfloat16)
        grad_q = (
            jnp.einsum("hqk,khd->qhd", s_low, k_block, preferred_element_type=jnp.float32) * scaling
        )
        grad_k = (
            jnp.einsum("hqk,qhd->khd", s_low, q_block, preferred_element_type=jnp.float32) * scaling
        )
        return (grad_q, grad_k, grad_v)

    grad_qn, grad_kn, grad_vn = map_blocks(
        attend_back, (q_low, k_low, v_low, s_blocks, log_total, grad_mixed)
    )
    grad_q, grad_k, gain_q, gain_k = norms_back(
        (grad_qn.reshape(length, HEADS, HEAD_DIM), grad_kn.reshape(length, HEADS, HEAD_DIM))
    )
    grad_project = jnp.concatenate(
        [
            grad_q.reshape(length, model_width),
            grad_k.reshape(length, model_width),
            grad_vn.reshape(length, model_width),
        ],
        axis=1,
    ).astype(jnp.bfloat16)
    grad_qkv = jnp.dot(normed_low.T, grad_project, preferred_element_type=jnp.float32)
    grad_normed = jnp.dot(grad_project, back_qkv.T, preferred_element_type=jnp.float32)
    grad_input, gain_one, bias_one = first_back(grad_normed)
    grad_tokens = (grad_input + grad_resid).astype(jnp.bfloat16)
    grad_gain = jnp.stack([gain_one, gain_two])
    grad_bias = jnp.stack([bias_one, bias_two])
    grad_qk = jnp.stack([gain_q.reshape(model_width), gain_k.reshape(model_width)])
    summands = (grad_qkv, grad_outw, grad_up, grad_down, grad_gain, grad_bias, grad_qk)
    if fast:
        late = fast_reduce(summands[:2], summands[4:])
        shares = late[:2] + early + late[2:]
    else:
        pieces = [
            lax.psum_scatter(
                s.astype(jnp.bfloat16), "fsdp", scatter_dimension=0 if k < 4 else 1, tiled=True
            ).astype(jnp.float32)
            for k, s in enumerate(summands)
        ]
        shares = [lax.psum(p.astype(jnp.bfloat16), "dp").astype(jnp.float32) for p in pieces]
    return (
        layer_out,
        grad_tokens,
        shares[0],
        shares[1],
        shares[2],
        shares[3],
        shares[4],
        shares[5],
        shares[6],
    )


def solution(mesh):
    in_specs = (
        P(("dp", "fsdp"), None),
        P(("dp", "fsdp"), None),
        P("fsdp", None),
        P("fsdp", None),
        P("fsdp", None),
        P("fsdp", None),
        P(None, "fsdp"),
        P(None, "fsdp"),
        P(None, "fsdp"),
        P(("dp", "fsdp"), None),
    )
    out_specs = (
        P(("dp", "fsdp"), None),
        P(("dp", "fsdp"), None),
        P("fsdp", None),
        P("fsdp", None),
        P("fsdp", None),
        P("fsdp", None),
        P(None, "fsdp"),
        P(None, "fsdp"),
        P(None, "fsdp"),
    )
    fast = dict(mesh.shape) == {"dp": NDP_FAST, "fsdp": NF_FAST}
    return jax.shard_map(
        partial(on_device, fast), mesh=mesh, in_specs=in_specs, out_specs=out_specs, check_vma=False
    )
```

```python
from functools import partial

import jax
import jax.numpy as jnp
from jax import lax
from jax.sharding import PartitionSpec as P


HEADS = 12
HEAD_DIM = 64
PATCH_BIG = 576


epsilon = 1e-06


def layer_norm(v, gain_row, bias_row):
    centre = v - jnp.mean(v, axis=-1, keepdims=True)
    spread = jnp.mean(centre * centre, axis=-1, keepdims=True)
    return centre * lax.rsqrt(spread + epsilon) * gain_row + bias_row


def head_norm(v, gain_row):
    centre = v - jnp.mean(v, axis=-1, keepdims=True)
    spread = jnp.mean(centre * centre, axis=-1, keepdims=True)
    return centre * lax.rsqrt(spread + epsilon) * gain_row


def both_norms(q_in, k_in, q_gain, k_gain):
    return (head_norm(q_in, q_gain), head_norm(k_in, k_gain))


NF_FAST = 4
NDP_FAST = 8


LANES = 128


def _plane_gather(z):
    d = lax.axis_index("dp")
    c = d % 2
    a = lax.ppermute(z, "dp", [(i, i ^ 2) for i in range(NDP_FAST)])
    b = lax.ppermute(z, "dp", [(i, i ^ 4) for i in range(NDP_FAST)])
    send = jnp.where(c == 0, b, a)
    diag = lax.ppermute(
        send, "dp", [(i, i ^ 2) if i % 2 == 0 else (i, i ^ 4) for i in range(NDP_FAST)]
    )
    mine = jnp.stack([z, a, b, diag])
    sib = lax.ppermute(mine, "dp", [(i, i ^ 1) for i in range(NDP_FAST)])
    return jnp.stack([mine[0], sib[0], mine[1], sib[1], mine[2], sib[2], mine[3], sib[3]])


def _take(x, idx, axis):
    return jnp.take(x, idx, axis=axis, mode="wrap")


def _z_gather(piece):
    f = lax.axis_index("fsdp")
    slots = [piece] + [
        lax.ppermute(piece, "fsdp", [(i, (i + k) % NF_FAST) for i in range(NF_FAST)])
        for k in range(1, NF_FAST)
    ]
    return _take(jnp.stack(slots), (f - jnp.arange(NF_FAST, dtype=jnp.int32)) % NF_FAST, 0)


def _gather_matrix(m):
    d = lax.axis_index("dp")
    j, c = d // 2, d % 2
    rows, cols = m.shape[0] // (NDP_FAST // 2), m.shape[1] // 2
    piece = lax.dynamic_slice(m, (j * rows, c * cols), (rows, cols))
    z = _z_gather(piece)
    x = lax.all_gather(z, "dp", axis=1, tiled=False)
    x = x.reshape(NF_FAST, NDP_FAST // 2, 2, rows, cols)
    x = jnp.concatenate([x[:, :, 0], x[:, :, 1]], axis=-1)
    return x.reshape(NF_FAST * m.shape[0], m.shape[1])


def _gather_matrix_pp(m):
    d = lax.axis_index("dp")
    j, c = d // 2, d % 2
    n_chips = NDP_FAST // 2
    rows, cols = m.shape[0] // n_chips, m.shape[1] // 2
    z = _z_gather(lax.dynamic_slice(m, (j * rows, c * cols), (rows, cols)))
    x = _take(_plane_gather(z), jnp.arange(NDP_FAST, dtype=jnp.int32) ^ d, 0)
    x = x.reshape(n_chips, 2, NF_FAST, rows, cols)
    x = jnp.concatenate([x[:, 0], x[:, 1]], axis=-1).transpose(1, 0, 2, 3)
    return x.reshape(NF_FAST * m.shape[0], m.shape[1])


def fast_gather(mats, gains):
    out = [_gather_matrix_pp(mats[0])] + [_gather_matrix(m) for m in mats[1:]]
    stacked = jnp.concatenate(gains, axis=0)
    z = _z_gather(stacked)
    full = z.transpose(1, 0, 2).reshape(stacked.shape[0], NF_FAST * stacked.shape[1])
    rows = 0
    for g in gains:
        out.append(full[rows : rows + g.shape[0]])
        rows += g.shape[0]
    return out


def _reduce_matrix(g):
    d = lax.axis_index("dp")
    f = lax.axis_index("fsdp")
    j, c = d // 2, d % 2
    n_chips = NDP_FAST // 2
    rows, cols = g.shape[0] // (NF_FAST * n_chips), g.shape[1] // 2

    def half(which):
        part = lax.dynamic_slice_in_dim(g, which * cols, cols, 1)
        return part.reshape(NF_FAST, n_chips, rows, cols)

    got = lax.ppermute(half(1 - c).astype(jnp.bfloat16), "dp", [(i, i ^ 1) for i in range(NDP_FAST)])
    chip = half(c) + got.astype(jnp.float32)

    def of_chip(k):
        return lax.dynamic_index_in_dim(chip, k, 1, keepdims=False)

    moved = lax.ppermute(
        of_chip(j ^ 3).astype(jnp.bfloat16),
        "dp",
        [(i, i ^ 2) if i % 2 == 0 else (i, i ^ 4) for i in range(NDP_FAST)],
    ).astype(jnp.float32)
    to_x = of_chip(j ^ 1) + jnp.where(c == 1, moved, 0.0)
    to_y = of_chip(j ^ 2) + jnp.where(c == 0, moved, 0.0)
    from_x = lax.ppermute(to_x.astype(jnp.bfloat16), "dp", [(i, i ^ 2) for i in range(NDP_FAST)])
    from_y = lax.ppermute(to_y.astype(jnp.bfloat16), "dp", [(i, i ^ 4) for i in range(NDP_FAST)])
    plane = of_chip(j) + from_x.astype(jnp.float32) + from_y.astype(jnp.float32)
    total = lax.dynamic_index_in_dim(plane, f, 0, keepdims=False)
    for k in range(1, NF_FAST):
        part = lax.dynamic_index_in_dim(plane, (f + k) % NF_FAST, 0, keepdims=False)
        total = total + lax.ppermute(
            part.astype(jnp.bfloat16), "fsdp", [(i, (i + k) % NF_FAST) for i in range(NF_FAST)]
        ).astype(jnp.float32)
    x = lax.all_gather(total, "dp", axis=0, tiled=False)
    x = x.reshape(n_chips, 2, rows, cols)
    x = jnp.concatenate([x[:, 0], x[:, 1]], axis=-1)
    return x.reshape(n_chips * rows, 2 * cols)


def fast_reduce(mats, gains):
    stacked = jnp.concatenate(gains, axis=0)
    pad = 2 * LANES - stacked.shape[0]
    last = jnp.concatenate([mats[-1], jnp.pad(stacked.T, ((0, 0), (0, pad)))], axis=1)
    out = [_reduce_matrix(m) for m in mats[:-1]]
    shard = _reduce_matrix(last)
    width = mats[-1].shape[1]
    out.append(shard[:, :width])
    mine = shard[:, width : width + stacked.shape[0]].T
    rows = 0
    for g in gains:
        out.append(mine[rows : rows + g.shape[0]])
        rows += g.shape[0]
    return out


def map_blocks(fn, members):
    if members[0].shape[0] == 1:
        return jax.tree.map(lambda v: v[None], fn(tuple(m[0] for m in members)))
    return lax.map(fn, members)


def on_device(fast, *args):
    return layer(fast, *args)


def layer(
    fast, tokens, image_lengths, w_qkv, w_out, w_up, w_down, ln_gain, ln_bias, qk_gain, cotangent
):
    if fast:
        full_qkv, full_out, full_up, full_down, gain_all, bias_all, qk_all = fast_gather(
            (w_qkv, w_out, w_up, w_down), (ln_gain, ln_bias, qk_gain)
        )
    else:
        full_qkv, full_out, full_up, full_down, gain_all, bias_all, qk_all = (
            lax.all_gather(w_qkv, "fsdp", axis=0, tiled=True),
            lax.all_gather(w_out, "fsdp", axis=0, tiled=True),
            lax.all_gather(w_up, "fsdp", axis=0, tiled=True),
            lax.all_gather(w_down, "fsdp", axis=0, tiled=True),
            lax.all_gather(ln_gain, "fsdp", axis=1, tiled=True),
            lax.all_gather(ln_bias, "fsdp", axis=1, tiled=True),
            lax.all_gather(qk_gain, "fsdp", axis=1, tiled=True),
        )
    length = tokens.shape[0]
    model_width = tokens.shape[1]
    blocks = length // PATCH_BIG
    scaling = HEAD_DIM ** (-0.5)
    position = jnp.arange(length, dtype=jnp.int32)
    limits = jnp.cumsum(image_lengths[0])
    segment = jnp.sum((position[:, None] >= limits[None, :]).astype(jnp.int32), axis=1)
    valid_rows = (position < limits[-1]).astype(jnp.float32)[:, None]
    norm_gains = gain_all.astype(jnp.float32)
    biases = bias_all.astype(jnp.float32)
    qk_gains = qk_all.astype(jnp.float32).reshape(2, HEADS, HEAD_DIM)
    inputs = tokens.astype(jnp.float32)
    normed, first_back = jax.vjp(layer_norm, inputs, norm_gains[0], biases[0])
    normed_low = normed.astype(jnp.bfloat16)
    project = jnp.dot(normed_low, full_qkv, preferred_element_type=jnp.float32)
    queries = project[:, :model_width].reshape(length, HEADS, HEAD_DIM)
    keys_raw = project[:, model_width : 2 * model_width].reshape(length, HEADS, HEAD_DIM)
    values_raw = project[:, 2 * model_width :]
    (q_norm, k_norm), norms_back = jax.vjp(both_norms, queries, keys_raw, qk_gains[0], qk_gains[1])
    q_low = q_norm.astype(jnp.bfloat16).reshape(blocks, PATCH_BIG, HEADS, HEAD_DIM)
    k_low = k_norm.astype(jnp.bfloat16).reshape(blocks, PATCH_BIG, HEADS, HEAD_DIM)
    v_low = values_raw.astype(jnp.bfloat16).reshape(blocks, PATCH_BIG, HEADS, HEAD_DIM)
    s_blocks = segment.reshape(blocks, PATCH_BIG)

    def block_scores(q_block, k_block, s_block):
        scores = (
            jnp.einsum("qhd,khd->hqk", q_block, k_block, preferred_element_type=jnp.float32)
            * scaling
        )
        return jnp.where((s_block[:, None] == s_block[None, :])[None], scores, -1e30)

    def attend(members):
        q_block, k_block, v_block, s_block = members
        scores = block_scores(q_block, k_block, s_block)
        row_top = jnp.max(scores, axis=-1, keepdims=True)
        exp_scores = jnp.exp(scores - row_top)
        row_total = jnp.sum(exp_scores, axis=-1, keepdims=True)
        probability = (exp_scores / row_total).astype(jnp.bfloat16)
        mixed_block = jnp.einsum(
            "hqk,khd->qhd", probability, v_block, preferred_element_type=jnp.float32
        )
        return (mixed_block, row_top + jnp.log(row_total))

    mixed_heads, log_total = lax.map(attend, (q_low, k_low, v_low, s_blocks))
    mixed_low = mixed_heads.reshape(length, model_width).astype(jnp.bfloat16)
    residual = inputs + jnp.dot(mixed_low, full_out, preferred_element_type=jnp.float32)
    second, second_back = jax.vjp(layer_norm, residual, norm_gains[1], biases[1])
    second_low = second.astype(jnp.bfloat16)
    up_pre = jnp.dot(second_low, full_up, preferred_element_type=jnp.float32)
    active, gelu_back = jax.vjp(partial(jax.nn.gelu, approximate=False), up_pre)
    active_low = active.astype(jnp.bfloat16)
    output = residual + jnp.dot(active_low, full_down, preferred_element_type=jnp.float32)
    layer_out = (valid_rows * output).astype(jnp.bfloat16)
    back_qkv, back_out, back_up, back_down = full_qkv, full_out, full_up, full_down
    upstream = cotangent.astype(jnp.float32) * valid_rows
    up_low = upstream.astype(jnp.bfloat16)
    grad_down = jnp.dot(active_low.T, up_low, preferred_element_type=jnp.float32)
    grad_active = jnp.dot(up_low, back_down.T, preferred_element_type=jnp.float32)
    (grad_pre,) = gelu_back(grad_active)
    pre_low = grad_pre.astype(jnp.bfloat16)
    grad_up = jnp.dot(second_low.T, pre_low, preferred_element_type=jnp.float32)
    if fast:
        early = [_reduce_matrix(grad_up), _reduce_matrix(grad_down)]
    grad_second = jnp.dot(pre_low, back_up.T, preferred_element_type=jnp.float32)
    grad_resid, gain_two, bias_two = second_back(grad_second)
    grad_resid = grad_resid + upstream
    resid_low = grad_resid.astype(jnp.bfloat16)
    grad_outw = jnp.dot(mixed_low.T, resid_low, preferred_element_type=jnp.float32)
    grad_mixed = jnp.dot(resid_low, back_out.T, preferred_element_type=jnp.float32)
    grad_mixed = grad_mixed.astype(jnp.bfloat16).reshape(blocks, PATCH_BIG, HEADS, HEAD_DIM)

    def attend_back(members):
        q_block, k_block, v_block, s_block, l_block, d_block = members
        scores = block_scores(q_block, k_block, s_block)
        probability = jnp.exp(scores - l_block)
        prob_low = probability.astype(jnp.bfloat16)
        grad_v = jnp.einsum("hqk,qhd->khd", prob_low, d_block, preferred_element_type=jnp.float32)
        grad_p = jnp.einsum("qhd,khd->hqk", d_block, v_block, preferred_element_type=jnp.float32)
        grad_p = lax.optimization_barrier(grad_p.astype(jnp.bfloat16)).astype(jnp.float32)
        grad_s = probability * (grad_p - jnp.sum(probability * grad_p, axis=-1, keepdims=True))
        s_low = grad_s.astype(jnp.bfloat16)
        grad_q = (
            jnp.einsum("hqk,khd->qhd", s_low, k_block, preferred_element_type=jnp.float32) * scaling
        )
        grad_k = (
            jnp.einsum("hqk,qhd->khd", s_low, q_block, preferred_element_type=jnp.float32) * scaling
        )
        return (grad_q, grad_k, grad_v)

    grad_qn, grad_kn, grad_vn = map_blocks(
        attend_back, (q_low, k_low, v_low, s_blocks, log_total, grad_mixed)
    )
    grad_q, grad_k, gain_q, gain_k = norms_back(
        (grad_qn.reshape(length, HEADS, HEAD_DIM), grad_kn.reshape(length, HEADS, HEAD_DIM))
    )
    grad_project = jnp.concatenate(
        [
            grad_q.reshape(length, model_width),
            grad_k.reshape(length, model_width),
            grad_vn.reshape(length, model_width),
        ],
        axis=1,
    ).astype(jnp.bfloat16)
    grad_qkv = jnp.dot(normed_low.T, grad_project, preferred_element_type=jnp.float32)
    grad_normed = jnp.dot(grad_project, back_qkv.T, preferred_element_type=jnp.float32)
    grad_input, gain_one, bias_one = first_back(grad_normed)
    grad_tokens = (grad_input + grad_resid).astype(jnp.bfloat16)
    grad_gain = jnp.stack([gain_one, gain_two])
    grad_bias = jnp.stack([bias_one, bias_two])
    grad_qk = jnp.stack([gain_q.reshape(model_width), gain_k.reshape(model_width)])
    summands = (grad_qkv, grad_outw, grad_up, grad_down, grad_gain, grad_bias, grad_qk)
    if fast:
        late = fast_reduce(summands[:2], summands[4:])
        shares = late[:2] + early + late[2:]
    else:
        pieces = [
            lax.psum_scatter(
                s.astype(jnp.bfloat16), "fsdp", scatter_dimension=0 if k < 4 else 1, tiled=True
            ).astype(jnp.float32)
            for k, s in enumerate(summands)
        ]
        shares = [lax.psum(p.astype(jnp.bfloat16), "dp").astype(jnp.float32) for p in pieces]
    return (
        layer_out,
        grad_tokens,
        shares[0],
        shares[1],
        shares[2],
        shares[3],
        shares[4],
        shares[5],
        shares[6],
    )


def solution(mesh):
    in_specs = (
        P(("dp", "fsdp"), None),
        P(("dp", "fsdp"), None),
        P("fsdp", None),
        P("fsdp", None),
        P("fsdp", None),
        P("fsdp", None),
        P(None, "fsdp"),
        P(None, "fsdp"),
        P(None, "fsdp"),
        P(("dp", "fsdp"), None),
    )
    out_specs = (
        P(("dp", "fsdp"), None),
        P(("dp", "fsdp"), None),
        P("fsdp", None),
        P("fsdp", None),
        P("fsdp", None),
        P("fsdp", None),
        P(None, "fsdp"),
        P(None, "fsdp"),
        P(None, "fsdp"),
    )
    fast = dict(mesh.shape) == {"dp": NDP_FAST, "fsdp": NF_FAST}
    return jax.shard_map(
        partial(on_device, fast), mesh=mesh, in_specs=in_specs, out_specs=out_specs, check_vma=False
    )
```
